32 devices in a mesh: cand: 4 (over y, x), hist: 8 (over z, core).
Axes of the slice: x: 2, y: 2, z: 4, core: 2. Of those that a mesh axis runs over, the one named last changes fastest.
Arguments:
- cand_x: bfloat16 [2, 1024, 1024], P(None, ('cand', 'hist')), may hold values from -6 to 6
- qu_weight: bfloat16 [1024, 2048], replicated, may hold values from -0.1875 to 0.1875
- out_weight: bfloat16 [1024, 1024], replicated, may hold values from -0.1875 to 0.1875
- k_cache: bfloat16 [131072, 1024], P('hist', 'cand'), may hold values from -1.5 to 1.5
- v_cache: bfloat16 [131072, 1024], P('hist', 'cand'), may hold values from -6 to 6
- hist_len: int32 [16], replicated, may hold values from 1 to 32768, as said below
- cand_count: int32 [2, 16], replicated, may hold values from 1 to 128, 1024 in all within a row
- tile_user: int32 [1024], P('hist'), may hold values from 0 to 16, as said below
- tile_rank: int32 [1024], P('hist'), may hold values from 0 to 255, as said below
Outputs:
- ranked: bfloat16 [2, 1024, 1024], P(None, ('cand', 'hist'))
The draws below stay inside these ranges and needn't reach their ends.
Inputs may be any that keep to these rules, and one draw needn't show every extreme that they name: A user's history fills exactly ceil(hist_len / 128) tile slots; one user's history is 32768 rows long. `tile_user`: slot owner, 16 for an empty slot; within each hist index's 128 slots the occupied ones come first; every user owns at least one slot. `tile_rank`: each tile position 0 to ceil(hist_len[u] / 128) - 1 of every user u stands in exactly one slot; empty slots hold 0. `cand_count`: row m gives the candidates of each user in micro-batch m, numbered user by user; they sum to 1024 and one user has exactly 128.
All inputs are finite; a program needn't handle non-finite values.
Results may differ from the reference program's by a relative error of at most 0.0051.
Values may be sent and summed in bfloat16 or wider, within the bound.
No kernel may reach another device: no remote copies, remote signals or barrier semaphores. Data moves between devices by JAX's collectives and lax.ppermute only.
A program may use at most 128 MiB of HBM per device.

```python
import math
import jax
import jax.numpy as jnp
import numpy as np
from jax import lax

D = 1024
HEADS = 8
HEAD_DIM = 128
TILE = 128
USERS = 16
MICRO = 2
TILES_DEV = 128
CANDS = 1024
TILES = 1024
HIST_ROWS = 131072
MAXC = 128


def tile_layout(key):
    base_key = jax.random.fold_in(key, 7)
    pick_key, count_key, tail_key, weight_key, score_key = jax.random.split(base_key, 5)
    shards = TILES // TILES_DEV
    user_ids = jnp.arange(USERS, dtype=jnp.int32)
    longest = jax.random.randint(pick_key, (), 0, USERS)
    others = jax.random.randint(count_key, (USERS,), 1, TILES // 2 // (USERS - 1) + 1)
    tile_counts = jnp.where(user_ids == longest, TILES // 4, others).astype(jnp.int32)
    tail_rows = jax.random.randint(tail_key, (USERS,), 1, TILE + 1)
    lengths = jnp.where(user_ids == longest, tile_counts * TILE, (tile_counts - 1) * TILE + tail_rows)
    end_tiles = jnp.cumsum(tile_counts).astype(jnp.int32)
    starts = end_tiles - tile_counts
    occupied = end_tiles[USERS - 1]
    slot_ids = jnp.arange(TILES, dtype=jnp.int32)
    factors = 1 + jax.random.randint(weight_key, (shards,), 0, 4)
    scores = jax.random.randint(score_key, (TILES,), 0, 4096) * factors[slot_ids // TILES_DEV] * TILES + slot_ids
    slot_order = jnp.argsort(scores)
    assigned = jnp.argsort(slot_order).astype(jnp.int32)
    blocks = assigned.reshape(shards, TILES_DEV)
    sorted_ids = jnp.sort(blocks, axis=1).reshape(TILES)
    filled = sorted_ids < occupied
    owners = jnp.sum((sorted_ids[:, None] >= end_tiles[None, :]).astype(jnp.int32), axis=1)
    clipped = jnp.minimum(owners, USERS - 1)
    first_tile = jnp.sum(jnp.where(clipped[:, None] == user_ids[None, :], starts[None, :], 0), axis=1)
    user_col = jnp.where(filled, owners, USERS)
    rank_col = jnp.where(filled, sorted_ids - first_tile, 0)
    return (lengths.astype(jnp.int32), user_col.astype(jnp.int32), rank_col.astype(jnp.int32))


def draw_hist_len(key, part):
    return tile_layout(key)[0]


def draw_tile_user(key, part):
    return tile_layout(key)[1]


def draw_tile_rank(key, part):
    return tile_layout(key)[2]


def levels(own_key, extent, pieces, low, top_value):
    def one(dim, shards_of):
        draws = jax.random.uniform(jax.random.fold_in(jax.random.fold_in(own_key, 6), dim), (shards_of,), jnp.float32, low / len(pieces), top_value / len(pieces))
        return jnp.repeat(jnp.exp(draws), extent[dim] // shards_of).reshape((-1,) + (1,) * (len(extent) - dim - 1))

    factor_of = one(*pieces[0])
    for cut in pieces[1:]:
        factor_of = factor_of * one(*cut)
    return factor_of


def profile(count, total, reach, lean):
    portions = [(1 << 20) // math.isqrt(rank ** lean) + 1 for rank in range(2, count + 1)]
    spare, given = total - reach - (count - 1), [1] * (count - 1)
    while spare > 0:
        candidates = [i for i in range(count - 1) if given[i] < reach]
        whole, remaining = sum([portions[i] for i in candidates]), spare
        for i in candidates:
            extra = min(reach - given[i], max(1, remaining * portions[i] // whole), spare)
            given[i] = given[i] + extra
            spare = spare - extra
    return np.array([reach] + given)


def ragged_sizes(key, number_of, total, bound, lean):
    if number_of == 2:
        one = jax.random.randint(key, (), max(1, total - bound), min(bound, total - 1) + 1)
        return jnp.stack([one, total - one])
    sizes = jnp.asarray(profile(number_of, total, bound, lean), jnp.int32)
    twos = (number_of - 1) // 2
    donor, sink = sizes[1:1 + 2 * twos:2], sizes[2:2 + 2 * twos:2]
    room = jnp.minimum(donor - 1, bound - sink)
    passed = jax.random.randint(jax.random.fold_in(key, 1), (twos,), 0, 1 << 20) % (room + 1)
    sizes = sizes.at[1:1 + 2 * twos:2].set(donor - passed).at[2:2 + 2 * twos:2].set(sink + passed)
    return sizes[jax.random.permutation(jax.random.fold_in(key, 2), number_of)]


def bell_draw(own_key, extent, width, reach, pieces=(), kind=jnp.bfloat16):
    values = jax.random.normal(own_key, extent, jnp.float32) * width
    if len(pieces) > 0:
        values = levels(own_key, extent, pieces, -0.22, 0.18) * values
    return jnp.clip(values, min=-reach, max=reach).astype(kind)


def setup_inputs(seed: int = 0) -> dict:
    seeds = jax.random.split(jax.random.key(seed), 10)
    cand_x = bell_draw(seeds[0], (MICRO, CANDS, D), 1.0, 6.0, ((1, 32),))
    qu_weight = bell_draw(seeds[1], (D, 2 * D), D ** -0.5, 0.1875)
    out_weight = bell_draw(seeds[2], (D, D), D ** -0.5, 0.1875)
    k_cache = bell_draw(seeds[3], (HIST_ROWS, D), 0.25, 1.5, ((0, 8), (1, 4)))
    v_cache = bell_draw(seeds[4], (HIST_ROWS, D), 1.0, 6.0, ((0, 8), (1, 4)))
    hist_len = draw_hist_len(jax.random.fold_in(seeds[9], 71), 0)
    cand_count = jax.vmap(lambda own: ragged_sizes(own, USERS, CANDS, MAXC, 2))(jax.random.split(seeds[6], MICRO)).reshape((MICRO, USERS)).astype(jnp.int32)
    tile_user = draw_tile_user(jax.random.fold_in(seeds[9], 71), 0)
    tile_rank = draw_tile_rank(jax.random.fold_in(seeds[9], 71), 0)
    return dict(cand_x=cand_x, qu_weight=qu_weight, out_weight=out_weight, k_cache=k_cache, v_cache=v_cache, hist_len=hist_len, cand_count=cand_count, tile_user=tile_user, tile_rank=tile_rank)


EPSILON = 1e-06

def attend_batch(queries, counts, k_cache, v_cache, hist_len, tile_user, tile_rank):
    cand_start = (jnp.cumsum(counts) - counts).astype(jnp.int32)
    key_tiles = k_cache.reshape(TILES, TILE, HEADS, HEAD_DIM)
    value_tiles = v_cache.reshape(TILES, TILE, HEADS, HEAD_DIM)
    row_ids = jnp.arange(MAXC, dtype=jnp.int32)
    tile_rows = jnp.arange(TILE, dtype=jnp.int32)

    def visit_tile(partial_value, inputs):
        key_block, value_block, tile_owner, position = inputs

        def compute(running):
            clipped = jnp.minimum(tile_owner, USERS - 1)
            length = hist_len[clipped]
            first_cand = cand_start[clipped]
            cand_total = counts[clipped]
            offset = jnp.minimum(first_cand, CANDS - MAXC).astype(jnp.int32)
            window = lax.dynamic_slice_in_dim(queries, offset, MAXC, 0).astype(jnp.float32)
            window = window.reshape(MAXC, HEADS, HEAD_DIM)
            scores = jnp.einsum('whd,khd->hwk', window, key_block.astype(jnp.float32), precision=lax.Precision.HIGHEST)
            cand_ids = offset + row_ids
            cand_ok = (cand_ids >= first_cand) & (cand_ids < first_cand + cand_total)
            key_ok = position * TILE + tile_rows < length
            keep_mask = cand_ok[None, :, None] & key_ok[None, None, :]
            weights = jnp.where(keep_mask, jax.nn.silu(scores), 0.0).astype(jnp.bfloat16)
            weights = lax.optimization_barrier(weights).astype(jnp.float32)
            contrib = jnp.einsum('hwk,khd->whd', weights, value_block.astype(jnp.float32), precision=lax.Precision.HIGHEST).reshape(MAXC, D)
            current = lax.dynamic_slice_in_dim(running, offset, MAXC, 0)
            return lax.dynamic_update_slice_in_dim(running, current + contrib, offset, 0)

        def unchanged(running):
            return running
        return (lax.cond(tile_owner < USERS, compute, unchanged, partial_value), None)
    initial = jnp.zeros((CANDS, D), jnp.float32)
    result, _ = lax.scan(visit_tile, initial, (key_tiles, value_tiles, tile_user, tile_rank))
    return result

def reference(cand_x, qu_weight, out_weight, k_cache, v_cache, hist_len, cand_count, tile_user, tile_rank):
    outputs = []
    for micro_index in range(MICRO):
        cand_rows = cand_x[micro_index]
        projected = jax.nn.silu(jnp.dot(cand_rows, qu_weight, preferred_element_type=jnp.float32))
        queries = projected[:, :D].astype(jnp.bfloat16)
        gate_vals = projected[:, D:].astype(jnp.bfloat16)
        attended = attend_batch(queries, cand_count[micro_index], k_cache, v_cache, hist_len, tile_user, tile_rank)
        average = lax.optimization_barrier(jnp.mean(attended, axis=-1, keepdims=True))
        centered = attended - average
        spread_sq = lax.optimization_barrier(jnp.mean(centered * centered, axis=-1, keepdims=True))
        normed = centered * lax.rsqrt(spread_sq + EPSILON)
        mixed_rows = (normed * gate_vals.astype(jnp.float32)).astype(jnp.bfloat16)
        ranked = jnp.dot(mixed_rows, out_weight, preferred_element_type=jnp.float32) + cand_rows.astype(jnp.float32)
        outputs.append(ranked.astype(jnp.bfloat16))
    return jnp.stack(outputs)
```

```python
import functools

import jax
import jax.numpy as jnp
from jax import lax
from jax.experimental import pallas as pl
from jax.experimental.pallas import tpu as pltpu
from jax.sharding import PartitionSpec as P

HEAD_DIM = 128
TILE = 128
USERS = 16
MICRO = 2
BLOCK_TILES = 8
FIELDS = 2 + 4 * MICRO


EPSILON = 1e-06


def attend_kernel(info_ref, last_ref, q_ref, k_ref, v_ref, out_ref, *, window, heads_here):
    block = pl.program_id(0)

    @pl.when(block == 0)
    def _():
        out_ref[...] = jnp.zeros_like(out_ref)

    row_ids = lax.broadcasted_iota(jnp.int32, (window, 1), 0)
    key_ids = lax.broadcasted_iota(jnp.int32, (TILE, 1), 0)

    def one_tile(j, carry):
        base = (block * BLOCK_TILES + j) * FIELDS

        @pl.when(info_ref[base] > 0)
        def _():
            klen = info_ref[base + 1]
            rows = pl.ds(pl.multiple_of(j * TILE, TILE), TILE)
            keys = jnp.where(key_ids < klen, k_ref[rows, :], 0)
            values = v_ref[rows, :]
            for m in range(MICRO):
                base_row = pl.multiple_of(info_ref[base + 2 + 4 * m], 8)
                shift = info_ref[base + 3 + 4 * m]
                lo = info_ref[base + 4 + 4 * m]
                hi = info_ref[base + 5 + 4 * m]
                span = pl.ds(base_row, window + 8)
                padded_q = q_ref[m, span, :]
                window_q = pltpu.roll(padded_q, (window + 8 - shift) % (window + 8), 0)[:window]
                keep = (row_ids >= lo) & (row_ids < hi)
                window_q = jnp.where(keep, window_q, 0.0).astype(jnp.bfloat16)
                parts = []
                for h in range(heads_here):
                    cols = slice(h * HEAD_DIM, (h + 1) * HEAD_DIM)
                    scores = lax.dot_general(
                        window_q[:, cols],
                        keys[:, cols],
                        (((1,), (1,)), ((), ())),
                        preferred_element_type=jnp.float32,
                    )
                    weights = (scores / (1.0 + jnp.exp(-scores))).astype(jnp.bfloat16)
                    parts.append(
                        jnp.dot(weights, values[:, cols], preferred_element_type=jnp.float32)
                    )
                contrib = parts[0] if heads_here == 1 else jnp.concatenate(parts, axis=1)
                contrib = jnp.concatenate([contrib, jnp.zeros((8, contrib.shape[1]), contrib.dtype)])
                out_ref[m, span, :] += pltpu.roll(contrib, shift, 0)

        return carry

    lax.fori_loop(0, BLOCK_TILES, one_tile, 0)


def body(
    cand_x, qu_weight, out_weight, k_cache, v_cache, hist_len, cand_count, tile_user, tile_rank
):
    n_cand = lax.axis_size("cand")
    n_hist = lax.axis_size("hist")
    micro, local_rows, model_width = cand_x.shape
    head_cols = k_cache.shape[1]
    heads_here = head_cols // HEAD_DIM
    tiles_here = k_cache.shape[0] // TILE

    cand_rows = cand_x.reshape(micro * local_rows, model_width)
    projected = jax.nn.silu(jnp.dot(cand_rows, qu_weight, preferred_element_type=jnp.float32))
    queries = projected[:, :model_width].astype(jnp.bfloat16).reshape(micro, local_rows, model_width)
    gate_vals = projected[:, model_width:].astype(jnp.bfloat16)
    gathered = lax.all_gather(queries, "hist", axis=1, tiled=True)
    queries_all = lax.all_to_all(gathered, "cand", split_axis=2, concat_axis=1, tiled=True)
    all_cands = queries_all.shape[1]
    window = 2 * all_cands // USERS

    starts = jnp.cumsum(cand_count, axis=1) - cand_count
    offsets = jnp.minimum(starts, all_cands - window)
    base_rows = jnp.minimum(offsets // 8 * 8, all_cands - window - 8)
    shifts = offsets - base_rows
    lows = starts - offsets
    highs = lows + cand_count
    occupied = tile_user < USERS
    owner = jnp.minimum(tile_user, USERS - 1)
    key_len = hist_len[owner] - tile_rank * TILE
    fields = [occupied.astype(jnp.int32), key_len]
    for m in range(micro):
        fields += [base_rows[m][owner], shifts[m][owner], lows[m][owner], highs[m][owner]]
    info = jnp.stack(fields, axis=1).astype(jnp.int32).reshape(-1)
    block_ids = jnp.arange(tiles_here, dtype=jnp.int32) // BLOCK_TILES
    last_block = jnp.max(jnp.where(occupied, block_ids, 0)).reshape(1).astype(jnp.int32)

    rows_per_block = BLOCK_TILES * TILE
    n_blocks = tiles_here // BLOCK_TILES
    whole = pl.BlockSpec((micro, all_cands, head_cols), lambda b, info, last: (0, 0, 0))
    tiles = pl.BlockSpec(
        (rows_per_block, head_cols), lambda b, info, last: (jnp.minimum(b, last[0]), 0)
    )
    partial_value = pl.pallas_call(
        functools.partial(attend_kernel, window=window, heads_here=heads_here),
        grid_spec=pltpu.PrefetchScalarGridSpec(
            num_scalar_prefetch=2,
            grid=(n_blocks,),
            in_specs=[whole, tiles, tiles],
            out_specs=whole,
        ),
        out_shape=jax.ShapeDtypeStruct((micro, all_cands, head_cols), jnp.float32),
        compiler_params=pltpu.CompilerParams(dimension_semantics=("arbitrary",)),
    )(info, last_block, queries_all.astype(jnp.float32), k_cache, v_cache)

    blocks = partial_value.reshape(micro, n_cand, n_hist, local_rows, head_cols)
    reduced = lax.psum_scatter(blocks, "hist", scatter_dimension=2, tiled=True)
    reduced = reduced.reshape(micro, n_cand, local_rows, head_cols)
    attended = lax.all_to_all(reduced, "cand", split_axis=1, concat_axis=3, tiled=True)
    attended = attended.reshape(micro * local_rows, model_width)
    average = jnp.mean(attended, axis=-1, keepdims=True)
    centered = attended - average
    spread_sq = jnp.mean(centered * centered, axis=-1, keepdims=True)
    normed = centered * lax.rsqrt(spread_sq + EPSILON)
    mixed_rows = (normed * gate_vals.astype(jnp.float32)).astype(jnp.bfloat16)
    ranked = jnp.dot(
        mixed_rows, out_weight, preferred_element_type=jnp.float32
    ) + cand_rows.astype(jnp.float32)
    return ranked.astype(jnp.bfloat16).reshape(micro, local_rows, model_width)


def solution(mesh):
    return jax.shard_map(
        body,
        mesh=mesh,
        in_specs=(
            P(None, ("cand", "hist"), None),
            P(),
            P(),
            P("hist", "cand"),
            P("hist", "cand"),
            P(),
            P(),
            P("hist"),
            P("hist"),
        ),
        out_specs=P(None, ("cand", "hist"), None),
        check_vma=False,
    )
```

```python
import functools

import jax
import jax.numpy as jnp
from jax import lax
from jax.experimental import pallas as pl
from jax.experimental.pallas import tpu as pltpu
from jax.sharding import PartitionSpec as P

HEAD_DIM = 128
TILE = 128
USERS = 16
MICRO = 2
BLOCK_TILES = 8


EPSILON = 1e-06


def silu_f32(x):
    return x / (1.0 + jnp.exp(-x))


def attend_kernel(
    owner_ref, rank_ref, len_ref, user_ref, last_ref, row_ref,
    q_ref, k_ref, v_ref, out_ref, user_q, user_acc, *, window, heads_here, micro,
):
    block = pl.program_id(0)
    row_ids = lax.broadcasted_iota(jnp.int32, (window, 1), 0)
    pad = jnp.zeros((8, out_ref.shape[2]), jnp.float32)

    @pl.when(block == 0)
    def _():
        user_acc[...] = jnp.zeros_like(user_acc)
        for m in range(micro):
            def fill(user, carry):
                entry = (m * USERS + user) * 4
                span = pl.ds(pl.multiple_of(user_ref[entry], 8), window + 8)
                shift = user_ref[entry + 1]
                rows = pltpu.roll(q_ref[m, span, :], (window + 8 - shift) % (window + 8), 0)
                keep = (row_ids >= user_ref[entry + 2]) & (row_ids < user_ref[entry + 3])
                user_q[pl.ds(pl.multiple_of(user * (micro * window) + m * window, window), window), :] = jnp.where(
                    keep, rows[:window], 0.0
                )
                return carry

            lax.fori_loop(0, USERS, fill, 0)

    key_ids = lax.broadcasted_iota(jnp.int32, (TILE, 1), 0)

    def one_tile(j, carry):
        slot = block * BLOCK_TILES + j
        user = owner_ref[slot]

        @pl.when(user < USERS)
        def _():
            klen = len_ref[user] - rank_ref[slot] * TILE
            rows = pl.ds(pl.multiple_of(j * TILE, TILE), TILE)
            keys = jnp.where(key_ids < klen, k_ref[rows, :], 0)
            values = v_ref[rows, :]
            user_rows = pl.ds(pl.multiple_of(row_ref[slot], micro * window), micro * window)
            queries = user_q[user_rows, :].astype(jnp.bfloat16)
            parts = []
            for h in range(heads_here):
                cols = slice(h * HEAD_DIM, (h + 1) * HEAD_DIM)
                scores = lax.dot_general(
                    queries[:, cols],
                    keys[:, cols],
                    (((1,), (1,)), ((), ())),
                    preferred_element_type=jnp.float32,
                )
                weights = silu_f32(scores).astype(jnp.bfloat16)
                parts.append(jnp.dot(weights, values[:, cols], preferred_element_type=jnp.float32))
            user_acc[user_rows, :] += parts[0] if heads_here == 1 else jnp.concatenate(parts, axis=1)

        return carry

    lax.fori_loop(0, BLOCK_TILES, one_tile, 0)

    @pl.when(block == pl.num_programs(0) - 1)
    def _():
        out_ref[...] = jnp.zeros_like(out_ref)
        for m in range(micro):
            def place(user, carry):
                entry = (m * USERS + user) * 4
                span = pl.ds(pl.multiple_of(user_ref[entry], 8), window + 8)
                first = pl.multiple_of(user * (micro * window) + m * window, window)
                sums = jnp.concatenate([user_acc[pl.ds(first, window), :], pad])
                out_ref[m, span, :] += pltpu.roll(sums, user_ref[entry + 1], 0)
                return carry

            lax.fori_loop(0, USERS, place, 0)


def body(
    cand_x, qu_weight, out_weight, k_cache, v_cache, hist_len, cand_count, tile_user, tile_rank
):
    n_cand = lax.axis_size("cand")
    n_hist = lax.axis_size("hist")
    micro, local_rows, model_width = cand_x.shape
    head_cols = k_cache.shape[1]
    heads_here = head_cols // HEAD_DIM
    tiles_here = k_cache.shape[0] // TILE

    cand_rows = cand_x.reshape(micro * local_rows, model_width)
    projected = jax.nn.silu(jnp.dot(cand_rows, qu_weight, preferred_element_type=jnp.float32))
    queries = projected[:, :model_width].astype(jnp.bfloat16).reshape(micro, local_rows, model_width)
    gate_vals = projected[:, model_width:].astype(jnp.bfloat16)
    gathered = lax.all_gather(queries, "hist", axis=1, tiled=True)
    queries_all = lax.all_to_all(gathered, "cand", split_axis=2, concat_axis=1, tiled=True)
    all_cands = queries_all.shape[1]
    window = 2 * all_cands // USERS

    starts = jnp.cumsum(cand_count, axis=1) - cand_count
    offsets = jnp.minimum(starts, all_cands - window)
    base_rows = jnp.minimum(offsets // 8 * 8, all_cands - window - 8)
    shifts = offsets - base_rows
    lows = starts - offsets
    highs = lows + cand_count
    user_info = jnp.stack([base_rows, shifts, lows, highs], axis=2).astype(jnp.int32).reshape(-1)
    block_ids = jnp.arange(tiles_here, dtype=jnp.int32) // BLOCK_TILES
    last_block = jnp.max(jnp.where(tile_user < USERS, block_ids, 0)).reshape(1).astype(jnp.int32)

    first_rows = (jnp.minimum(tile_user, USERS - 1) * (micro * window)).astype(jnp.int32)
    rows_per_block = BLOCK_TILES * TILE
    n_blocks = tiles_here // BLOCK_TILES
    whole = pl.BlockSpec((micro, all_cands, head_cols), lambda b, *_: (0, 0, 0))
    tiles = pl.BlockSpec(
        (rows_per_block, head_cols), lambda b, *_: (jnp.minimum(b, _[4][0]), 0)
    )
    per_user = pl.BlockSpec((USERS * micro * window, head_cols), lambda b, *_: (0, 0))
    partial_value, _, _ = pl.pallas_call(
        functools.partial(attend_kernel, window=window, heads_here=heads_here, micro=micro),
        grid_spec=pltpu.PrefetchScalarGridSpec(
            num_scalar_prefetch=6,
            grid=(n_blocks,),
            in_specs=[whole, tiles, tiles],
            out_specs=[whole, per_user, per_user],
        ),
        out_shape=[
            jax.ShapeDtypeStruct((micro, all_cands, head_cols), jnp.float32),
            jax.ShapeDtypeStruct((USERS * micro * window, head_cols), jnp.float32),
            jax.ShapeDtypeStruct((USERS * micro * window, head_cols), jnp.float32),
        ],
        compiler_params=pltpu.CompilerParams(dimension_semantics=("arbitrary",)),
    )(tile_user, tile_rank, hist_len, user_info, last_block, first_rows, queries_all.astype(jnp.float32), k_cache, v_cache)

    blocks = partial_value.reshape(micro, n_cand, n_hist, local_rows, head_cols)
    blocks = jnp.transpose(blocks, (2, 0, 1, 3, 4))
    received = lax.all_to_all(blocks, "hist", split_axis=0, concat_axis=0, tiled=True)
    reduced = received.sum(axis=0)
    attended = lax.all_to_all(reduced, "cand", split_axis=1, concat_axis=3, tiled=True)
    attended = attended.reshape(micro * local_rows, model_width)
    average = jnp.mean(attended, axis=-1, keepdims=True)
    centered = attended - average
    spread_sq = jnp.mean(centered * centered, axis=-1, keepdims=True)
    normed = centered * lax.rsqrt(spread_sq + EPSILON)
    mixed_rows = (normed * gate_vals.astype(jnp.float32)).astype(jnp.bfloat16)
    ranked = jnp.dot(
        mixed_rows, out_weight, preferred_element_type=jnp.float32
    ) + cand_rows.astype(jnp.float32)
    return ranked.astype(jnp.bfloat16).reshape(micro, local_rows, model_width)


def solution(mesh):
    return jax.shard_map(
        body,
        mesh=mesh,
        in_specs=(
            P(None, ("cand", "hist"), None),
            P(),
            P(),
            P("hist", "cand"),
            P("hist", "cand"),
            P(),
            P(),
            P("hist"),
            P("hist"),
        ),
        out_specs=P(None, ("cand", "hist"), None),
        check_vma=False,
    )
```

```python
import functools

import jax
import jax.numpy as jnp
from jax import lax
from jax.experimental import pallas as pl
from jax.experimental.pallas import tpu as pltpu
from jax.sharding import PartitionSpec as P

HEAD_DIM = 128
TILE = 128
USERS = 16
MICRO = 2
BLOCK_TILES = 8


EPSILON = 1e-06


def silu_f32(x):
    return x / (1.0 + jnp.exp(-x))


def attend_kernel(
    owner_ref, rank_ref, len_ref, user_ref, last_ref, row_ref,
    q_ref, k_ref, v_ref, out_ref, user_q, user_acc, *, window, heads_here, micro,
):
    block = pl.program_id(0)
    row_ids = lax.broadcasted_iota(jnp.int32, (window, 1), 0)
    pad = jnp.zeros((8, out_ref.shape[2]), jnp.float32)

    @pl.when(block == 0)
    def _():
        user_acc[...] = jnp.zeros_like(user_acc)
        for m in range(micro):
            def fill(user, carry):
                entry = (m * USERS + user) * 4
                span = pl.ds(pl.multiple_of(user_ref[entry], 8), window + 8)
                shift = user_ref[entry + 1]
                rows = pltpu.roll(q_ref[m, span, :], (window + 8 - shift) % (window + 8), 0)
                keep = (row_ids >= user_ref[entry + 2]) & (row_ids < user_ref[entry + 3])
                user_q[pl.ds(pl.multiple_of(user * (micro * window) + m * window, window), window), :] = jnp.where(
                    keep, rows[:window], 0.0
                )
                return carry

            lax.fori_loop(0, USERS, fill, 0)

    key_ids = lax.broadcasted_iota(jnp.int32, (TILE, 1), 0)

    def one_tile(j, carry):
        slot = block * BLOCK_TILES + j
        user = owner_ref[slot]

        @pl.when(user < USERS)
        def _():
            klen = len_ref[user] - rank_ref[slot] * TILE
            rows = pl.ds(pl.multiple_of(j * TILE, TILE), TILE)
            keys = jnp.where(key_ids < klen, k_ref[rows, :], 0)
            values = v_ref[rows, :]
            user_rows = pl.ds(pl.multiple_of(row_ref[slot], micro * window), micro * window)
            queries = user_q[user_rows, :].astype(jnp.bfloat16)
            parts = []
            for h in range(heads_here):
                cols = slice(h * HEAD_DIM, (h + 1) * HEAD_DIM)
                scores = lax.dot_general(
                    queries[:, cols],
                    keys[:, cols],
                    (((1,), (1,)), ((), ())),
                    preferred_element_type=jnp.float32,
                )
                weights = silu_f32(scores).astype(jnp.bfloat16)
                parts.append(jnp.dot(weights, values[:, cols], preferred_element_type=jnp.float32))
            user_acc[user_rows, :] += parts[0] if heads_here == 1 else jnp.concatenate(parts, axis=1)

        return carry

    lax.fori_loop(0, BLOCK_TILES, one_tile, 0)

    @pl.when(block == pl.num_programs(0) - 1)
    def _():
        out_ref[...] = jnp.zeros_like(out_ref)
        for m in range(micro):
            def place(user, carry):
                entry = (m * USERS + user) * 4
                span = pl.ds(pl.multiple_of(user_ref[entry], 8), window + 8)
                first = pl.multiple_of(user * (micro * window) + m * window, window)
                sums = jnp.concatenate([user_acc[pl.ds(first, window), :], pad])
                out_ref[m, span, :] += pltpu.roll(sums, user_ref[entry + 1], 0)
                return carry

            lax.fori_loop(0, USERS, place, 0)


def reduce_over_hist(partial):
    micro, n_cand, n_hist, rows, cols = partial.shape
    chips = n_hist // 2
    me = lax.axis_index("hist")
    chip, core = me // 2, me % 2
    halves = partial.reshape(micro, n_cand, chips, 2, rows, cols)
    mine = lax.dynamic_index_in_dim(halves, core, axis=3, keepdims=False)
    theirs = lax.dynamic_index_in_dim(halves, 1 - core, axis=3, keepdims=False)
    swapped = lax.ppermute(
        theirs.astype(jnp.bfloat16), "hist", perm=[(i, i ^ 1) for i in range(n_hist)]
    )
    chip_sums = mine + swapped.astype(jnp.float32)

    def block_of(index):
        index = jnp.clip(index, 0, chips - 1)
        return lax.dynamic_index_in_dim(chip_sums, index, axis=2, keepdims=False)

    rightward = jnp.zeros_like(block_of(0))
    leftward = jnp.zeros_like(rightward)
    for step in range(1, chips):
        send_right = (block_of(chip + chips - step) + rightward).astype(jnp.bfloat16)
        send_left = (block_of(chip - chips + step) + leftward).astype(jnp.bfloat16)
        to_right = [(2 * c + k, 2 * (c + 1) + k) for c in range(step) for k in range(2)]
        to_left = [(2 * c + k, 2 * (c - 1) + k) for c in range(chips - step, chips) for k in range(2)]
        rightward = lax.ppermute(send_right, "hist", perm=to_right).astype(jnp.float32)
        leftward = lax.ppermute(send_left, "hist", perm=to_left).astype(jnp.float32)
    return block_of(chip) + rightward + leftward


def body(
    cand_x, qu_weight, out_weight, k_cache, v_cache, hist_len, cand_count, tile_user, tile_rank
):
    n_cand = lax.axis_size("cand")
    n_hist = lax.axis_size("hist")
    micro, local_rows, model_width = cand_x.shape
    head_cols = k_cache.shape[1]
    heads_here = head_cols // HEAD_DIM
    tiles_here = k_cache.shape[0] // TILE

    cand_rows = cand_x.reshape(micro * local_rows, model_width)
    projected = jax.nn.silu(jnp.dot(cand_rows, qu_weight, preferred_element_type=jnp.float32))
    queries = projected[:, :model_width].astype(jnp.bfloat16).reshape(micro, local_rows, model_width)
    gate_vals = projected[:, model_width:].astype(jnp.bfloat16)
    gathered = lax.all_gather(queries, "hist", axis=1, tiled=True)
    queries_all = lax.all_to_all(gathered, "cand", split_axis=2, concat_axis=1, tiled=True)
    all_cands = queries_all.shape[1]
    window = 2 * all_cands // USERS

    starts = jnp.cumsum(cand_count, axis=1) - cand_count
    offsets = jnp.minimum(starts, all_cands - window)
    base_rows = jnp.minimum(offsets // 8 * 8, all_cands - window - 8)
    shifts = offsets - base_rows
    lows = starts - offsets
    highs = lows + cand_count
    user_info = jnp.stack([base_rows, shifts, lows, highs], axis=2).astype(jnp.int32).reshape(-1)
    block_ids = jnp.arange(tiles_here, dtype=jnp.int32) // BLOCK_TILES
    last_block = jnp.max(jnp.where(tile_user < USERS, block_ids, 0)).reshape(1).astype(jnp.int32)

    first_rows = (jnp.minimum(tile_user, USERS - 1) * (micro * window)).astype(jnp.int32)
    rows_per_block = BLOCK_TILES * TILE
    n_blocks = tiles_here // BLOCK_TILES
    whole = pl.BlockSpec((micro, all_cands, head_cols), lambda b, *_: (0, 0, 0))
    tiles = pl.BlockSpec(
        (rows_per_block, head_cols), lambda b, *_: (jnp.minimum(b, _[4][0]), 0)
    )
    per_user = pl.BlockSpec((USERS * micro * window, head_cols), lambda b, *_: (0, 0))
    partial_value, _, _ = pl.pallas_call(
        functools.partial(attend_kernel, window=window, heads_here=heads_here, micro=micro),
        grid_spec=pltpu.PrefetchScalarGridSpec(
            num_scalar_prefetch=6,
            grid=(n_blocks,),
            in_specs=[whole, tiles, tiles],
            out_specs=[whole, per_user, per_user],
        ),
        out_shape=[
            jax.ShapeDtypeStruct((micro, all_cands, head_cols), jnp.float32),
            jax.ShapeDtypeStruct((USERS * micro * window, head_cols), jnp.float32),
            jax.ShapeDtypeStruct((USERS * micro * window, head_cols), jnp.float32),
        ],
        compiler_params=pltpu.CompilerParams(dimension_semantics=("arbitrary",)),
    )(tile_user, tile_rank, hist_len, user_info, last_block, first_rows, queries_all.astype(jnp.float32), k_cache, v_cache)

    reduced = reduce_over_hist(partial_value.reshape(micro, n_cand, n_hist, local_rows, head_cols))
    attended = lax.all_to_all(reduced, "cand", split_axis=1, concat_axis=3, tiled=True)
    attended = attended.reshape(micro * local_rows, model_width)
    average = jnp.mean(attended, axis=-1, keepdims=True)
    centered = attended - average
    spread_sq = jnp.mean(centered * centered, axis=-1, keepdims=True)
    normed = centered * lax.rsqrt(spread_sq + EPSILON)
    mixed_rows = (normed * gate_vals.astype(jnp.float32)).astype(jnp.bfloat16)
    ranked = jnp.dot(
        mixed_rows, out_weight, preferred_element_type=jnp.float32
    ) + cand_rows.astype(jnp.float32)
    return ranked.astype(jnp.bfloat16).reshape(micro, local_rows, model_width)


def solution(mesh):
    return jax.shard_map(
        body,
        mesh=mesh,
        in_specs=(
            P(None, ("cand", "hist"), None),
            P(),
            P(),
            P("hist", "cand"),
            P("hist", "cand"),
            P(),
            P(),
            P("hist"),
            P("hist"),
        ),
        out_specs=P(None, ("cand", "hist"), None),
        check_vma=False,
    )
```

```python
import functools

import jax
import jax.numpy as jnp
from jax import lax
from jax.experimental import pallas as pl
from jax.experimental.pallas import tpu as pltpu
from jax.sharding import PartitionSpec as P

HEAD_DIM = 128
TILE = 128
USERS = 16
MICRO = 2
BLOCK_TILES = 8


EPSILON = 1e-06


def silu_f32(x):
    return 0.5 * x * (1.0 + jnp.tanh(0.5 * x))


def attend_kernel(
    owner_ref, rank_ref, len_ref, user_ref, last_ref, row_ref,
    q_ref, k_ref, v_ref, out_ref, user_q, user_acc, *, window, heads_here, micro,
):
    block = pl.program_id(0)
    row_ids = lax.broadcasted_iota(jnp.int32, (window, 1), 0)
    pad = jnp.zeros((8, out_ref.shape[2]), jnp.float32)

    @pl.when(block == 0)
    def _():
        user_acc[...] = jnp.zeros_like(user_acc)
        for m in range(micro):
            def fill(user, carry):
                entry = (m * USERS + user) * 4
                span = pl.ds(pl.multiple_of(user_ref[entry], 8), window + 8)
                shift = user_ref[entry + 1]
                rows = pltpu.roll(q_ref[m, span, :], (window + 8 - shift) % (window + 8), 0)
                keep = (row_ids >= user_ref[entry + 2]) & (row_ids < user_ref[entry + 3])
                user_q[pl.ds(pl.multiple_of(user * (micro * window) + m * window, window), window), :] = jnp.where(
                    keep, rows[:window], 0.0
                )
                return carry

            lax.fori_loop(0, USERS, fill, 0)

    key_ids = lax.broadcasted_iota(jnp.int32, (TILE, 1), 0)

    def one_tile(j, carry):
        slot = block * BLOCK_TILES + j
        user = owner_ref[slot]

        @pl.when(user < USERS)
        def _():
            klen = len_ref[user] - rank_ref[slot] * TILE
            rows = pl.ds(pl.multiple_of(j * TILE, TILE), TILE)
            keys = jnp.where(key_ids < klen, k_ref[rows, :], 0)
            values = v_ref[rows, :]
            user_rows = pl.ds(pl.multiple_of(row_ref[slot], micro * window), micro * window)
            queries = user_q[user_rows, :].astype(jnp.bfloat16)
            if heads_here == 2:
                lanes = lax.broadcasted_iota(jnp.int32, (1, 2 * HEAD_DIM), 1)
                first = lanes < HEAD_DIM

                def diagonal(tile):
                    return jnp.concatenate(
                        [jnp.where(first, tile, 0), jnp.where(first, 0, tile)], axis=0
                    )

                scores = lax.dot_general(
                    queries,
                    diagonal(keys),
                    (((1,), (1,)), ((), ())),
                    preferred_element_type=jnp.float32,
                )
                weights = silu_f32(scores).astype(jnp.bfloat16)
                user_acc[user_rows, :] += jnp.dot(
                    weights, diagonal(values), preferred_element_type=jnp.float32
                )
            else:
                parts = []
                for h in range(heads_here):
                    cols = slice(h * HEAD_DIM, (h + 1) * HEAD_DIM)
                    scores = lax.dot_general(
                        queries[:, cols],
                        keys[:, cols],
                        (((1,), (1,)), ((), ())),
                        preferred_element_type=jnp.float32,
                    )
                    weights = silu_f32(scores).astype(jnp.bfloat16)
                    parts.append(
                        jnp.dot(weights, values[:, cols], preferred_element_type=jnp.float32)
                    )
                user_acc[user_rows, :] += jnp.concatenate(parts, axis=1) if heads_here > 1 else parts[0]

        return carry

    lax.fori_loop(0, BLOCK_TILES, one_tile, 0)

    @pl.when(block == pl.num_programs(0) - 1)
    def _():
        out_ref[...] = jnp.zeros_like(out_ref)
        for m in range(micro):
            def place(user, carry):
                entry = (m * USERS + user) * 4
                span = pl.ds(pl.multiple_of(user_ref[entry], 8), window + 8)
                first = pl.multiple_of(user * (micro * window) + m * window, window)
                sums = jnp.concatenate([user_acc[pl.ds(first, window), :], pad])
                out_ref[m, span, :] += pltpu.roll(sums, user_ref[entry + 1], 0)
                return carry

            lax.fori_loop(0, USERS, place, 0)


def reduce_over_hist(partial):
    micro, n_cand, n_hist, rows, cols = partial.shape
    chips = n_hist // 2
    me = lax.axis_index("hist")
    chip, core = me // 2, me % 2
    halves = partial.reshape(micro, n_cand, chips, 2, rows, cols)
    mine = lax.dynamic_index_in_dim(halves, core, axis=3, keepdims=False)
    theirs = lax.dynamic_index_in_dim(halves, 1 - core, axis=3, keepdims=False)
    swapped = lax.ppermute(
        theirs.astype(jnp.bfloat16), "hist", perm=[(i, i ^ 1) for i in range(n_hist)]
    )
    chip_sums = mine + swapped.astype(jnp.float32)

    def block_of(index):
        index = jnp.clip(index, 0, chips - 1)
        return lax.dynamic_index_in_dim(chip_sums, index, axis=2, keepdims=False)

    rightward = jnp.zeros_like(block_of(0))
    leftward = jnp.zeros_like(rightward)
    for step in range(1, chips):
        send_right = (block_of(chip + chips - step) + rightward).astype(jnp.bfloat16)
        send_left = (block_of(chip - chips + step) + leftward).astype(jnp.bfloat16)
        to_right = [(2 * c + k, 2 * (c + 1) + k) for c in range(step) for k in range(2)]
        to_left = [(2 * c + k, 2 * (c - 1) + k) for c in range(chips - step, chips) for k in range(2)]
        rightward = lax.ppermute(send_right, "hist", perm=to_right).astype(jnp.float32)
        leftward = lax.ppermute(send_left, "hist", perm=to_left).astype(jnp.float32)
    return block_of(chip) + rightward + leftward


def body(
    cand_x, qu_weight, out_weight, k_cache, v_cache, hist_len, cand_count, tile_user, tile_rank
):
    n_cand = lax.axis_size("cand")
    n_hist = lax.axis_size("hist")
    micro, local_rows, model_width = cand_x.shape
    head_cols = k_cache.shape[1]
    heads_here = head_cols // HEAD_DIM
    tiles_here = k_cache.shape[0] // TILE

    cand_rows = cand_x.reshape(micro * local_rows, model_width)
    projected = jax.nn.silu(jnp.dot(cand_rows, qu_weight, preferred_element_type=jnp.float32))
    queries = projected[:, :model_width].astype(jnp.bfloat16).reshape(micro, local_rows, model_width)
    gate_vals = projected[:, model_width:].astype(jnp.bfloat16)
    gathered = lax.all_gather(queries, "hist", axis=1, tiled=True)
    queries_all = lax.all_to_all(gathered, "cand", split_axis=2, concat_axis=1, tiled=True)
    all_cands = queries_all.shape[1]
    window = 2 * all_cands // USERS

    starts = jnp.cumsum(cand_count, axis=1) - cand_count
    offsets = jnp.minimum(starts, all_cands - window)
    base_rows = jnp.minimum(offsets // 8 * 8, all_cands - window - 8)
    shifts = offsets - base_rows
    lows = starts - offsets
    highs = lows + cand_count
    user_info = jnp.stack([base_rows, shifts, lows, highs], axis=2).astype(jnp.int32).reshape(-1)
    block_ids = jnp.arange(tiles_here, dtype=jnp.int32) // BLOCK_TILES
    last_block = jnp.max(jnp.where(tile_user < USERS, block_ids, 0)).reshape(1).astype(jnp.int32)

    first_rows = (jnp.minimum(tile_user, USERS - 1) * (micro * window)).astype(jnp.int32)
    rows_per_block = BLOCK_TILES * TILE
    n_blocks = tiles_here // BLOCK_TILES
    whole = pl.BlockSpec((micro, all_cands, head_cols), lambda b, *_: (0, 0, 0))
    tiles = pl.BlockSpec(
        (rows_per_block, head_cols), lambda b, *_: (jnp.minimum(b, _[4][0]), 0)
    )
    per_user = pl.BlockSpec((USERS * micro * window, head_cols), lambda b, *_: (0, 0))
    partial_value, _, _ = pl.pallas_call(
        functools.partial(attend_kernel, window=window, heads_here=heads_here, micro=micro),
        grid_spec=pltpu.PrefetchScalarGridSpec(
            num_scalar_prefetch=6,
            grid=(n_blocks,),
            in_specs=[whole, tiles, tiles],
            out_specs=[whole, per_user, per_user],
        ),
        out_shape=[
            jax.ShapeDtypeStruct((micro, all_cands, head_cols), jnp.float32),
            jax.ShapeDtypeStruct((USERS * micro * window, head_cols), jnp.float32),
            jax.ShapeDtypeStruct((USERS * micro * window, head_cols), jnp.float32),
        ],
        compiler_params=pltpu.CompilerParams(dimension_semantics=("arbitrary",)),
    )(tile_user, tile_rank, hist_len, user_info, last_block, first_rows, queries_all.astype(jnp.float32), k_cache, v_cache)

    reduced = reduce_over_hist(partial_value.reshape(micro, n_cand, n_hist, local_rows, head_cols))
    attended = lax.all_to_all(reduced, "cand", split_axis=1, concat_axis=3, tiled=True)
    attended = attended.reshape(micro * local_rows, model_width)
    average = jnp.mean(attended, axis=-1, keepdims=True)
    centered = attended - average
    spread_sq = jnp.mean(centered * centered, axis=-1, keepdims=True)
    normed = centered * lax.rsqrt(spread_sq + EPSILON)
    mixed_rows = (normed * gate_vals.astype(jnp.float32)).astype(jnp.bfloat16)
    ranked = jnp.dot(
        mixed_rows, out_weight, preferred_element_type=jnp.float32
    ) + cand_rows.astype(jnp.float32)
    return ranked.astype(jnp.bfloat16).reshape(micro, local_rows, model_width)


def solution(mesh):
    return jax.shard_map(
        body,
        mesh=mesh,
        in_specs=(
            P(None, ("cand", "hist"), None),
            P(),
            P(),
            P("hist", "cand"),
            P("hist", "cand"),
            P(),
            P(),
            P("hist"),
            P("hist"),
        ),
        out_specs=P(None, ("cand", "hist"), None),
        check_vma=False,
    )
```

```python
import functools

import jax
import jax.numpy as jnp
from jax import lax
from jax.experimental import pallas as pl
from jax.experimental.pallas import tpu as pltpu
from jax.sharding import PartitionSpec as P

HEAD_DIM = 128
TILE = 128
USERS = 16
MICRO = 2
BLOCK_TILES = 8


EPSILON = 1e-06


def silu_f32(x):
    return 0.5 * x * (1.0 + jnp.tanh(0.5 * x))


def attend_kernel(
    owner_ref, rank_ref, len_ref, user_ref, last_ref, row_ref,
    q_ref, k_ref, v_ref, out_ref, user_q, user_acc, *, window, heads_here, micro,
):
    block = pl.program_id(0)
    row_ids = lax.broadcasted_iota(jnp.int32, (window, 1), 0)
    pad = jnp.zeros((8, out_ref.shape[2]), jnp.float32)

    @pl.when(block == 0)
    def _():
        user_acc[...] = jnp.zeros_like(user_acc)
        for m in range(micro):
            def fill(user, carry):
                entry = (m * USERS + user) * 4
                span = pl.ds(pl.multiple_of(user_ref[entry], 8), window + 8)
                shift = user_ref[entry + 1]
                rows = pltpu.roll(q_ref[m, span, :], (window + 8 - shift) % (window + 8), 0)
                keep = (row_ids >= user_ref[entry + 2]) & (row_ids < user_ref[entry + 3])
                user_q[pl.ds(pl.multiple_of(user * (micro * window) + m * window, window), window), :] = jnp.where(
                    keep, rows[:window], 0.0
                )
                return carry

            lax.fori_loop(0, USERS, fill, 0)

    key_ids = lax.broadcasted_iota(jnp.int32, (TILE, 1), 0)

    def one_tile(j):
        if True:
            slot = block * BLOCK_TILES + j
            user = owner_ref[slot]
            klen = jnp.where(
                user < USERS, len_ref[jnp.minimum(user, USERS - 1)] - rank_ref[slot] * TILE, 0
            )
            rows = slice(j * TILE, (j + 1) * TILE)
            keys = jnp.where(key_ids < klen, k_ref[rows, :], 0)
            values = v_ref[rows, :]
            user_rows = pl.ds(pl.multiple_of(row_ref[slot], micro * window), micro * window)
            queries = user_q[user_rows, :].astype(jnp.bfloat16)
            if heads_here == 2:
                lanes = lax.broadcasted_iota(jnp.int32, (1, 2 * HEAD_DIM), 1)
                first = lanes < HEAD_DIM

                def diagonal(tile):
                    return jnp.concatenate(
                        [jnp.where(first, tile, 0), jnp.where(first, 0, tile)], axis=0
                    )

                scores = lax.dot_general(
                    queries,
                    diagonal(keys),
                    (((1,), (1,)), ((), ())),
                    preferred_element_type=jnp.float32,
                )
                weights = silu_f32(scores).astype(jnp.bfloat16)
                user_acc[user_rows, :] += jnp.dot(
                    weights, diagonal(values), preferred_element_type=jnp.float32
                )
            else:
                parts = []
                for h in range(heads_here):
                    cols = slice(h * HEAD_DIM, (h + 1) * HEAD_DIM)
                    scores = lax.dot_general(
                        queries[:, cols],
                        keys[:, cols],
                        (((1,), (1,)), ((), ())),
                        preferred_element_type=jnp.float32,
                    )
                    weights = silu_f32(scores).astype(jnp.bfloat16)
                    parts.append(
                        jnp.dot(weights, values[:, cols], preferred_element_type=jnp.float32)
                    )
                user_acc[user_rows, :] += jnp.concatenate(parts, axis=1) if heads_here > 1 else parts[0]


    @pl.when(block <= last_ref[0])
    def _():
        for j in range(BLOCK_TILES):
            one_tile(j)

    @pl.when(block == pl.num_programs(0) - 1)
    def _():
        out_ref[...] = jnp.zeros_like(out_ref)
        for m in range(micro):
            def place(user, carry):
                entry = (m * USERS + user) * 4
                span = pl.ds(pl.multiple_of(user_ref[entry], 8), window + 8)
                first = pl.multiple_of(user * (micro * window) + m * window, window)
                sums = jnp.concatenate([user_acc[pl.ds(first, window), :], pad])
                out_ref[m, span, :] += pltpu.roll(sums, user_ref[entry + 1], 0)
                return carry

            lax.fori_loop(0, USERS, place, 0)


def reduce_over_hist(partial):
    micro, n_cand, n_hist, rows, cols = partial.shape
    chips = n_hist // 2
    me = lax.axis_index("hist")
    chip, core = me // 2, me % 2
    halves = partial.reshape(micro, n_cand, chips, 2, rows, cols)
    mine = lax.dynamic_index_in_dim(halves, core, axis=3, keepdims=False)
    theirs = lax.dynamic_index_in_dim(halves, 1 - core, axis=3, keepdims=False)
    swapped = lax.ppermute(
        theirs.astype(jnp.bfloat16), "hist", perm=[(i, i ^ 1) for i in range(n_hist)]
    )
    chip_sums = mine + swapped.astype(jnp.float32)

    def block_of(index):
        index = jnp.clip(index, 0, chips - 1)
        return lax.dynamic_index_in_dim(chip_sums, index, axis=2, keepdims=False)

    rightward = jnp.zeros_like(block_of(0))
    leftward = jnp.zeros_like(rightward)
    for step in range(1, chips):
        send_right = (block_of(chip + chips - step) + rightward).astype(jnp.bfloat16)
        send_left = (block_of(chip - chips + step) + leftward).astype(jnp.bfloat16)
        to_right = [(2 * c + k, 2 * (c + 1) + k) for c in range(step) for k in range(2)]
        to_left = [(2 * c + k, 2 * (c - 1) + k) for c in range(chips - step, chips) for k in range(2)]
        rightward = lax.ppermute(send_right, "hist", perm=to_right).astype(jnp.float32)
        leftward = lax.ppermute(send_left, "hist", perm=to_left).astype(jnp.float32)
    return block_of(chip) + rightward + leftward


def body(
    cand_x, qu_weight, out_weight, k_cache, v_cache, hist_len, cand_count, tile_user, tile_rank
):
    n_cand = lax.axis_size("cand")
    n_hist = lax.axis_size("hist")
    micro, local_rows, model_width = cand_x.shape
    head_cols = k_cache.shape[1]
    heads_here = head_cols // HEAD_DIM
    tiles_here = k_cache.shape[0] // TILE

    cand_rows = cand_x.reshape(micro * local_rows, model_width)
    projected = jax.nn.silu(jnp.dot(cand_rows, qu_weight, preferred_element_type=jnp.float32))
    queries = projected[:, :model_width].astype(jnp.bfloat16).reshape(micro, local_rows, model_width)
    gate_vals = projected[:, model_width:].astype(jnp.bfloat16)
    gathered = lax.all_gather(queries, "hist", axis=1, tiled=True)
    queries_all = lax.all_to_all(gathered, "cand", split_axis=2, concat_axis=1, tiled=True)
    all_cands = queries_all.shape[1]
    window = 2 * all_cands // USERS

    starts = jnp.cumsum(cand_count, axis=1) - cand_count
    offsets = jnp.minimum(starts, all_cands - window)
    base_rows = jnp.minimum(offsets // 8 * 8, all_cands - window - 8)
    shifts = offsets - base_rows
    lows = starts - offsets
    highs = lows + cand_count
    user_info = jnp.stack([base_rows, shifts, lows, highs], axis=2).astype(jnp.int32).reshape(-1)
    block_ids = jnp.arange(tiles_here, dtype=jnp.int32) // BLOCK_TILES
    last_block = jnp.max(jnp.where(tile_user < USERS, block_ids, 0)).reshape(1).astype(jnp.int32)

    first_rows = (jnp.minimum(tile_user, USERS - 1) * (micro * window)).astype(jnp.int32)
    rows_per_block = BLOCK_TILES * TILE
    n_blocks = tiles_here // BLOCK_TILES
    whole = pl.BlockSpec((micro, all_cands, head_cols), lambda b, *_: (0, 0, 0))
    tiles = pl.BlockSpec(
        (rows_per_block, head_cols), lambda b, *_: (jnp.minimum(b, _[4][0]), 0)
    )
    per_user = pl.BlockSpec((USERS * micro * window, head_cols), lambda b, *_: (0, 0))
    partial_value, _, _ = pl.pallas_call(
        functools.partial(attend_kernel, window=window, heads_here=heads_here, micro=micro),
        grid_spec=pltpu.PrefetchScalarGridSpec(
            num_scalar_prefetch=6,
            grid=(n_blocks,),
            in_specs=[whole, tiles, tiles],
            out_specs=[whole, per_user, per_user],
        ),
        out_shape=[
            jax.ShapeDtypeStruct((micro, all_cands, head_cols), jnp.float32),
            jax.ShapeDtypeStruct((USERS * micro * window, head_cols), jnp.float32),
            jax.ShapeDtypeStruct((USERS * micro * window, head_cols), jnp.float32),
        ],
        compiler_params=pltpu.CompilerParams(dimension_semantics=("arbitrary",)),
    )(tile_user, tile_rank, hist_len, user_info, last_block, first_rows, queries_all.astype(jnp.float32), k_cache, v_cache)

    reduced = reduce_over_hist(partial_value.reshape(micro, n_cand, n_hist, local_rows, head_cols))
    attended = lax.all_to_all(reduced, "cand", split_axis=1, concat_axis=3, tiled=True)
    attended = attended.reshape(micro * local_rows, model_width)
    average = jnp.mean(attended, axis=-1, keepdims=True)
    centered = attended - average
    spread_sq = jnp.mean(centered * centered, axis=-1, keepdims=True)
    normed = centered * lax.rsqrt(spread_sq + EPSILON)
    mixed_rows = (normed * gate_vals.astype(jnp.float32)).astype(jnp.bfloat16)
    ranked = jnp.dot(
        mixed_rows, out_weight, preferred_element_type=jnp.float32
    ) + cand_rows.astype(jnp.float32)
    return ranked.astype(jnp.bfloat16).reshape(micro, local_rows, model_width)


def solution(mesh):
    return jax.shard_map(
        body,
        mesh=mesh,
        in_specs=(
            P(None, ("cand", "hist"), None),
            P(),
            P(),
            P("hist", "cand"),
            P("hist", "cand"),
            P(),
            P(),
            P("hist"),
            P("hist"),
        ),
        out_specs=P(None, ("cand", "hist"), None),
        check_vma=False,
    )
```

```python
import functools

import jax
import jax.numpy as jnp
from jax import lax
from jax.experimental import pallas as pl
from jax.experimental.pallas import tpu as pltpu
from jax.sharding import PartitionSpec as P

HEAD_DIM = 128
TILE = 128
USERS = 16
MICRO = 2
BLOCK_TILES = 8


EPSILON = 1e-06


def silu_f32(x):
    return 0.5 * x * (1.0 + jnp.tanh(0.5 * x))


def attend_kernel(
    owner_ref, rank_ref, len_ref, user_ref, last_ref, row_ref,
    q_ref, k_ref, v_ref, out_ref, user_q, user_acc, *, window, heads_here, micro,
):
    block = pl.program_id(0)
    row_ids = lax.broadcasted_iota(jnp.int32, (window, 1), 0)
    pad = jnp.zeros((8, out_ref.shape[2]), jnp.float32)

    @pl.when(block == 0)
    def _():
        user_acc[...] = jnp.zeros_like(user_acc)
        for m in range(micro):
            def fill(user, carry):
                entry = (m * USERS + user) * 4
                span = pl.ds(pl.multiple_of(user_ref[entry], 8), window + 8)
                shift = user_ref[entry + 1]
                rows = pltpu.roll(q_ref[m, span, :], (window + 8 - shift) % (window + 8), 0)
                keep = (row_ids >= user_ref[entry + 2]) & (row_ids < user_ref[entry + 3])
                user_q[pl.ds(pl.multiple_of(user * (micro * window) + m * window, window), window), :] = jnp.where(
                    keep, rows[:window], 0.0
                )
                return carry

            lax.fori_loop(0, USERS, fill, 0)

    key_ids = lax.broadcasted_iota(jnp.int32, (TILE, 1), 0)

    def one_tile(j):
        if True:
            slot = block * BLOCK_TILES + j
            user = owner_ref[slot]
            klen = jnp.where(
                user < USERS, len_ref[jnp.minimum(user, USERS - 1)] - rank_ref[slot] * TILE, 0
            )
            rows = slice(j * TILE, (j + 1) * TILE)
            keys = jnp.where(key_ids < klen, k_ref[rows, :], 0)
            values = v_ref[rows, :]
            user_rows = pl.ds(pl.multiple_of(row_ref[slot], micro * window), micro * window)
            queries = user_q[user_rows, :].astype(jnp.bfloat16)
            if heads_here == 2:
                lanes = lax.broadcasted_iota(jnp.int32, (1, 2 * HEAD_DIM), 1)
                first = lanes < HEAD_DIM

                def diagonal(tile):
                    return jnp.concatenate(
                        [jnp.where(first, tile, 0), jnp.where(first, 0, tile)], axis=0
                    )

                scores = lax.dot_general(
                    queries,
                    diagonal(keys),
                    (((1,), (1,)), ((), ())),
                    preferred_element_type=jnp.float32,
                )
                weights = silu_f32(scores).astype(jnp.bfloat16)
                user_acc[user_rows, :] += jnp.dot(
                    weights, diagonal(values), preferred_element_type=jnp.float32
                )
            else:
                parts = []
                for h in range(heads_here):
                    cols = slice(h * HEAD_DIM, (h + 1) * HEAD_DIM)
                    scores = lax.dot_general(
                        queries[:, cols],
                        keys[:, cols],
                        (((1,), (1,)), ((), ())),
                        preferred_element_type=jnp.float32,
                    )
                    weights = silu_f32(scores).astype(jnp.bfloat16)
                    parts.append(
                        jnp.dot(weights, values[:, cols], preferred_element_type=jnp.float32)
                    )
                user_acc[user_rows, :] += jnp.concatenate(parts, axis=1) if heads_here > 1 else parts[0]


    @pl.when(block <= last_ref[0])
    def _():
        for j in range(BLOCK_TILES):
            one_tile(j)

    @pl.when(block == pl.num_programs(0) - 1)
    def _():
        out_ref[...] = jnp.zeros_like(out_ref)
        for m in range(micro):
            def place(user, carry):
                entry = (m * USERS + user) * 4
                span = pl.ds(pl.multiple_of(user_ref[entry], 8), window + 8)
                first = pl.multiple_of(user * (micro * window) + m * window, window)
                sums = jnp.concatenate([user_acc[pl.ds(first, window), :], pad])
                out_ref[m, span, :] += pltpu.roll(sums, user_ref[entry + 1], 0)
                return carry

            lax.fori_loop(0, USERS, place, 0)


def reduce_over_hist(partial):
    micro, n_cand, n_hist, rows, cols = partial.shape
    chips = n_hist // 2
    me = lax.axis_index("hist")
    chip, core = me // 2, me % 2
    halves = partial.reshape(micro, n_cand, chips, 2, rows, cols)
    mine = lax.dynamic_index_in_dim(halves, core, axis=3, keepdims=False)
    theirs = lax.dynamic_index_in_dim(halves, 1 - core, axis=3, keepdims=False)
    swapped = lax.ppermute(
        theirs.astype(jnp.bfloat16), "hist", perm=[(i, i ^ 1) for i in range(n_hist)]
    )
    chip_sums = mine + swapped.astype(jnp.float32)

    def block_of(index):
        index = jnp.clip(index, 0, chips - 1)
        return lax.dynamic_index_in_dim(chip_sums, index, axis=2, keepdims=False)

    rightward = jnp.zeros_like(block_of(0))
    leftward = jnp.zeros_like(rightward)
    for step in range(1, chips):
        send_right = (block_of(chip + chips - step) + rightward).astype(jnp.bfloat16)
        send_left = (block_of(chip - chips + step) + leftward).astype(jnp.bfloat16)
        to_right = [(2 * c + k, 2 * (c + 1) + k) for c in range(step) for k in range(2)]
        to_left = [(2 * c + k, 2 * (c - 1) + k) for c in range(chips - step, chips) for k in range(2)]
        rightward = lax.ppermute(send_right, "hist", perm=to_right).astype(jnp.float32)
        leftward = lax.ppermute(send_left, "hist", perm=to_left).astype(jnp.float32)
    return block_of(chip) + rightward + leftward


def gather_queries(queries, n_cand, n_hist):
    micro, rows, width = queries.shape
    group = width // n_cand
    me_cand = lax.axis_index("cand")
    chunks = queries.reshape(micro, rows, n_cand, group)
    received = []
    for shift in range(n_cand):
        target = (me_cand + shift) % n_cand
        piece = lax.dynamic_index_in_dim(chunks, target, axis=2, keepdims=False)
        if shift:
            piece = lax.ppermute(
                piece, "cand", perm=[(i, (i + shift) % n_cand) for i in range(n_cand)]
            )
        received.append(piece)
    by_offset = jnp.stack(received)
    sources = jnp.stack(
        [
            lax.dynamic_index_in_dim(by_offset, (me_cand - c) % n_cand, axis=0, keepdims=False)
            for c in range(n_cand)
        ]
    )
    chips = n_hist // 2
    me = lax.axis_index("hist")
    chip, core = me // 2, me % 2
    rightward, leftward = [], []
    send_right = send_left = sources
    for step in range(1, chips):
        to_right = [(2 * c + k, 2 * (c + 1) + k) for c in range(step - 1, chips - 1) for k in range(2)]
        to_left = [(2 * c + k, 2 * (c - 1) + k) for c in range(1, chips - step + 1) for k in range(2)]
        send_right = lax.ppermute(send_right, "hist", perm=to_right)
        send_left = lax.ppermute(send_left, "hist", perm=to_left)
        rightward.append(send_right)
        leftward.append(send_left)
    by_distance = jnp.stack(leftward[::-1] + [sources] + rightward)
    mine = jnp.stack(
        [
            lax.dynamic_index_in_dim(by_distance, chips - 1 + chip - c, axis=0, keepdims=False)
            for c in range(chips)
        ]
    )
    theirs = lax.ppermute(mine, "hist", perm=[(i, i ^ 1) for i in range(n_hist)])
    both = jnp.where(core == 0, jnp.stack([mine, theirs], axis=1), jnp.stack([theirs, mine], axis=1))
    both = both.reshape(n_hist, n_cand, micro, rows, group)
    return jnp.transpose(both, (2, 1, 0, 3, 4)).reshape(micro, n_cand * n_hist * rows, group)


def body(
    cand_x, qu_weight, out_weight, k_cache, v_cache, hist_len, cand_count, tile_user, tile_rank
):
    n_cand = lax.axis_size("cand")
    n_hist = lax.axis_size("hist")
    micro, local_rows, model_width = cand_x.shape
    head_cols = k_cache.shape[1]
    heads_here = head_cols // HEAD_DIM
    tiles_here = k_cache.shape[0] // TILE

    cand_rows = cand_x.reshape(micro * local_rows, model_width)
    projected = jax.nn.silu(jnp.dot(cand_rows, qu_weight, preferred_element_type=jnp.float32))
    queries = projected[:, :model_width].astype(jnp.bfloat16).reshape(micro, local_rows, model_width)
    gate_vals = projected[:, model_width:].astype(jnp.bfloat16)
    queries_all = gather_queries(queries, n_cand, n_hist)
    all_cands = queries_all.shape[1]
    window = 2 * all_cands // USERS

    starts = jnp.cumsum(cand_count, axis=1) - cand_count
    offsets = jnp.minimum(starts, all_cands - window)
    base_rows = jnp.minimum(offsets // 8 * 8, all_cands - window - 8)
    shifts = offsets - base_rows
    lows = starts - offsets
    highs = lows + cand_count
    user_info = jnp.stack([base_rows, shifts, lows, highs], axis=2).astype(jnp.int32).reshape(-1)
    block_ids = jnp.arange(tiles_here, dtype=jnp.int32) // BLOCK_TILES
    last_block = jnp.max(jnp.where(tile_user < USERS, block_ids, 0)).reshape(1).astype(jnp.int32)

    first_rows = (jnp.minimum(tile_user, USERS - 1) * (micro * window)).astype(jnp.int32)
    rows_per_block = BLOCK_TILES * TILE
    n_blocks = tiles_here // BLOCK_TILES
    whole = pl.BlockSpec((micro, all_cands, head_cols), lambda b, *_: (0, 0, 0))
    tiles = pl.BlockSpec(
        (rows_per_block, head_cols), lambda b, *_: (jnp.minimum(b, _[4][0]), 0)
    )
    per_user = pl.BlockSpec((USERS * micro * window, head_cols), lambda b, *_: (0, 0))
    partial_value, _, _ = pl.pallas_call(
        functools.partial(attend_kernel, window=window, heads_here=heads_here, micro=micro),
        grid_spec=pltpu.PrefetchScalarGridSpec(
            num_scalar_prefetch=6,
            grid=(n_blocks,),
            in_specs=[whole, tiles, tiles],
            out_specs=[whole, per_user, per_user],
        ),
        out_shape=[
            jax.ShapeDtypeStruct((micro, all_cands, head_cols), jnp.float32),
            jax.ShapeDtypeStruct((USERS * micro * window, head_cols), jnp.float32),
            jax.ShapeDtypeStruct((USERS * micro * window, head_cols), jnp.float32),
        ],
        compiler_params=pltpu.CompilerParams(dimension_semantics=("arbitrary",)),
    )(tile_user, tile_rank, hist_len, user_info, last_block, first_rows, queries_all.astype(jnp.float32), k_cache, v_cache)

    reduced = reduce_over_hist(partial_value.reshape(micro, n_cand, n_hist, local_rows, head_cols))
    attended = lax.all_to_all(reduced, "cand", split_axis=1, concat_axis=3, tiled=True)
    attended = attended.reshape(micro * local_rows, model_width)
    average = jnp.mean(attended, axis=-1, keepdims=True)
    centered = attended - average
    spread_sq = jnp.mean(centered * centered, axis=-1, keepdims=True)
    normed = centered * lax.rsqrt(spread_sq + EPSILON)
    mixed_rows = (normed * gate_vals.astype(jnp.float32)).astype(jnp.bfloat16)
    ranked = jnp.dot(
        mixed_rows, out_weight, preferred_element_type=jnp.float32
    ) + cand_rows.astype(jnp.float32)
    return ranked.astype(jnp.bfloat16).reshape(micro, local_rows, model_width)


def solution(mesh):
    return jax.shard_map(
        body,
        mesh=mesh,
        in_specs=(
            P(None, ("cand", "hist"), None),
            P(),
            P(),
            P("hist", "cand"),
            P("hist", "cand"),
            P(),
            P(),
            P("hist"),
            P("hist"),
        ),
        out_specs=P(None, ("cand", "hist"), None),
        check_vma=False,
    )
```

```python
import functools

import jax
import jax.numpy as jnp
from jax import lax
from jax.experimental import pallas as pl
from jax.experimental.pallas import tpu as pltpu
from jax.sharding import PartitionSpec as P

HEAD_DIM = 128
TILE = 128
USERS = 16
MICRO = 2
BLOCK_TILES = 8


EPSILON = 1e-06


def silu_f32(x):
    return 0.5 * x * (1.0 + jnp.tanh(0.5 * x))


def attend_kernel(
    owner_ref, rank_ref, len_ref, user_ref, last_ref, row_ref,
    q_ref, k_ref, v_ref, out_ref, user_q, user_acc, *, window, heads_here, micro,
):
    block = pl.program_id(0)
    row_ids = lax.broadcasted_iota(jnp.int32, (window, 1), 0)
    pad = jnp.zeros((8, out_ref.shape[2]), jnp.float32)

    @pl.when(block == 0)
    def _():
        user_acc[...] = jnp.zeros_like(user_acc)
        for m in range(micro):
            def fill(user, carry):
                entry = (m * USERS + user) * 4
                span = pl.ds(pl.multiple_of(user_ref[entry], 8), window + 8)
                shift = user_ref[entry + 1]
                rows = pltpu.roll(q_ref[m, span, :], (window + 8 - shift) % (window + 8), 0)
                keep = (row_ids >= user_ref[entry + 2]) & (row_ids < user_ref[entry + 3])
                user_q[pl.ds(pl.multiple_of(user * (micro * window) + m * window, window), window), :] = jnp.where(
                    keep, rows[:window], 0.0
                )
                return carry

            lax.fori_loop(0, USERS, fill, 0)

    key_ids = lax.broadcasted_iota(jnp.int32, (TILE, 1), 0)

    def one_tile(j):
        if True:
            slot = block * BLOCK_TILES + j
            user = owner_ref[slot]
            klen = jnp.where(
                user < USERS, len_ref[jnp.minimum(user, USERS - 1)] - rank_ref[slot] * TILE, 0
            )
            rows = slice(j * TILE, (j + 1) * TILE)
            keys = jnp.where(key_ids < klen, k_ref[rows, :], 0)
            values = v_ref[rows, :]
            user_rows = pl.ds(pl.multiple_of(row_ref[slot], micro * window), micro * window)
            queries = user_q[user_rows, :].astype(jnp.bfloat16)
            if heads_here == 2:
                lanes = lax.broadcasted_iota(jnp.int32, (1, 2 * HEAD_DIM), 1)
                first = lanes < HEAD_DIM

                def diagonal(tile):
                    return jnp.concatenate(
                        [jnp.where(first, tile, 0), jnp.where(first, 0, tile)], axis=0
                    )

                scores = lax.dot_general(
                    queries,
                    diagonal(keys),
                    (((1,), (1,)), ((), ())),
                    preferred_element_type=jnp.float32,
                )
                weights = silu_f32(scores).astype(jnp.bfloat16)
                user_acc[user_rows, :] += jnp.dot(
                    weights, diagonal(values), preferred_element_type=jnp.float32
                )
            else:
                parts = []
                for h in range(heads_here):
                    cols = slice(h * HEAD_DIM, (h + 1) * HEAD_DIM)
                    scores = lax.dot_general(
                        queries[:, cols],
                        keys[:, cols],
                        (((1,), (1,)), ((), ())),
                        preferred_element_type=jnp.float32,
                    )
                    weights = silu_f32(scores).astype(jnp.bfloat16)
                    parts.append(
                        jnp.dot(weights, values[:, cols], preferred_element_type=jnp.float32)
                    )
                user_acc[user_rows, :] += jnp.concatenate(parts, axis=1) if heads_here > 1 else parts[0]


    @pl.when(block <= last_ref[0])
    def _():
        for j in range(BLOCK_TILES):
            one_tile(j)

    @pl.when(block == pl.num_programs(0) - 1)
    def _():
        out_ref[...] = jnp.zeros_like(out_ref)
        for m in range(micro):
            def place(user, carry):
                entry = (m * USERS + user) * 4
                span = pl.ds(pl.multiple_of(user_ref[entry], 8), window + 8)
                first = pl.multiple_of(user * (micro * window) + m * window, window)
                sums = jnp.concatenate([user_acc[pl.ds(first, window), :], pad])
                out_ref[m, span, :] += pltpu.roll(sums, user_ref[entry + 1], 0)
                return carry

            lax.fori_loop(0, USERS, place, 0)


def reduce_over_hist(partial):
    micro, n_cand, n_hist, rows, cols = partial.shape
    chips = n_hist // 2
    me = lax.axis_index("hist")
    chip, core = me // 2, me % 2
    halves = partial.reshape(micro, n_cand, chips, 2, rows, cols)
    mine = lax.dynamic_index_in_dim(halves, core, axis=3, keepdims=False)
    theirs = lax.dynamic_index_in_dim(halves, 1 - core, axis=3, keepdims=False)
    swapped = lax.ppermute(
        theirs.astype(jnp.bfloat16), "hist", perm=[(i, i ^ 1) for i in range(n_hist)]
    )
    chip_sums = mine + swapped.astype(jnp.float32)

    def block_of(index):
        index = jnp.clip(index, 0, chips - 1)
        return lax.dynamic_index_in_dim(chip_sums, index, axis=2, keepdims=False)

    rightward = jnp.zeros_like(block_of(0))
    leftward = jnp.zeros_like(rightward)
    for step in range(1, chips):
        send_right = (block_of(chip + chips - step) + rightward).astype(jnp.bfloat16)
        send_left = (block_of(chip - chips + step) + leftward).astype(jnp.bfloat16)
        to_right = [(2 * c + k, 2 * (c + 1) + k) for c in range(step) for k in range(2)]
        to_left = [(2 * c + k, 2 * (c - 1) + k) for c in range(chips - step, chips) for k in range(2)]
        rightward = lax.ppermute(send_right, "hist", perm=to_right).astype(jnp.float32)
        leftward = lax.ppermute(send_left, "hist", perm=to_left).astype(jnp.float32)
    return block_of(chip) + rightward + leftward


def gather_queries(queries, n_cand, n_hist):
    micro, rows, width = queries.shape
    group = width // n_cand
    me_cand = lax.axis_index("cand")
    chunks = queries.reshape(micro, rows, n_cand, group)
    received = []
    for shift in range(n_cand):
        target = (me_cand + shift) % n_cand
        piece = lax.dynamic_index_in_dim(chunks, target, axis=2, keepdims=False)
        if shift:
            piece = lax.ppermute(
                piece, "cand", perm=[(i, (i + shift) % n_cand) for i in range(n_cand)]
            )
        received.append(piece)
    by_offset = jnp.stack(received)
    sources = jnp.stack(
        [
            lax.dynamic_index_in_dim(by_offset, (me_cand - c) % n_cand, axis=0, keepdims=False)
            for c in range(n_cand)
        ]
    )
    chips = n_hist // 2
    me = lax.axis_index("hist")
    chip, core = me // 2, me % 2
    rightward, leftward = [], []
    send_right = send_left = sources
    for step in range(1, chips):
        to_right = [(2 * c + k, 2 * (c + 1) + k) for c in range(step - 1, chips - 1) for k in range(2)]
        to_left = [(2 * c + k, 2 * (c - 1) + k) for c in range(1, chips - step + 1) for k in range(2)]
        send_right = lax.ppermute(send_right, "hist", perm=to_right)
        send_left = lax.ppermute(send_left, "hist", perm=to_left)
        rightward.append(send_right)
        leftward.append(send_left)
    by_distance = jnp.stack(leftward[::-1] + [sources] + rightward)
    mine = jnp.stack(
        [
            lax.dynamic_index_in_dim(by_distance, chips - 1 + chip - c, axis=0, keepdims=False)
            for c in range(chips)
        ]
    )
    theirs = lax.ppermute(mine, "hist", perm=[(i, i ^ 1) for i in range(n_hist)])
    both = jnp.where(core == 0, jnp.stack([mine, theirs], axis=1), jnp.stack([theirs, mine], axis=1))
    both = both.reshape(n_hist, n_cand, micro, rows, group)
    return jnp.transpose(both, (2, 1, 0, 3, 4)).reshape(micro, n_cand * n_hist * rows, group)


def spread_over_cand(reduced):
    micro, n_cand, rows, group = reduced.shape
    me = lax.axis_index("cand")
    received = []
    for shift in range(n_cand):
        piece = lax.dynamic_index_in_dim(reduced, (me + shift) % n_cand, axis=1, keepdims=False)
        if shift:
            piece = lax.ppermute(
                piece, "cand", perm=[(i, (i + shift) % n_cand) for i in range(n_cand)]
            )
        received.append(piece)
    by_offset = jnp.stack(received)
    return jnp.concatenate(
        [
            lax.dynamic_index_in_dim(by_offset, (me - c) % n_cand, axis=0, keepdims=False)
            for c in range(n_cand)
        ],
        axis=-1,
    )


def body(
    cand_x, qu_weight, out_weight, k_cache, v_cache, hist_len, cand_count, tile_user, tile_rank
):
    n_cand = lax.axis_size("cand")
    n_hist = lax.axis_size("hist")
    micro, local_rows, model_width = cand_x.shape
    head_cols = k_cache.shape[1]
    heads_here = head_cols // HEAD_DIM
    tiles_here = k_cache.shape[0] // TILE

    cand_rows = cand_x.reshape(micro * local_rows, model_width)
    projected = jax.nn.silu(jnp.dot(cand_rows, qu_weight, preferred_element_type=jnp.float32))
    queries = projected[:, :model_width].astype(jnp.bfloat16).reshape(micro, local_rows, model_width)
    gate_vals = projected[:, model_width:].astype(jnp.bfloat16)
    queries_all = gather_queries(queries, n_cand, n_hist)
    all_cands = queries_all.shape[1]
    window = 2 * all_cands // USERS

    starts = jnp.cumsum(cand_count, axis=1) - cand_count
    offsets = jnp.minimum(starts, all_cands - window)
    base_rows = jnp.minimum(offsets // 8 * 8, all_cands - window - 8)
    shifts = offsets - base_rows
    lows = starts - offsets
    highs = lows + cand_count
    user_info = jnp.stack([base_rows, shifts, lows, highs], axis=2).astype(jnp.int32).reshape(-1)
    block_ids = jnp.arange(tiles_here, dtype=jnp.int32) // BLOCK_TILES
    last_block = jnp.max(jnp.where(tile_user < USERS, block_ids, 0)).reshape(1).astype(jnp.int32)

    first_rows = (jnp.minimum(tile_user, USERS - 1) * (micro * window)).astype(jnp.int32)
    rows_per_block = BLOCK_TILES * TILE
    n_blocks = tiles_here // BLOCK_TILES
    whole = pl.BlockSpec((micro, all_cands, head_cols), lambda b, *_: (0, 0, 0))
    tiles = pl.BlockSpec(
        (rows_per_block, head_cols), lambda b, *_: (jnp.minimum(b, _[4][0]), 0)
    )
    per_user = pl.BlockSpec((USERS * micro * window, head_cols), lambda b, *_: (0, 0))
    partial_value, _, _ = pl.pallas_call(
        functools.partial(attend_kernel, window=window, heads_here=heads_here, micro=micro),
        grid_spec=pltpu.PrefetchScalarGridSpec(
            num_scalar_prefetch=6,
            grid=(n_blocks,),
            in_specs=[whole, tiles, tiles],
            out_specs=[whole, per_user, per_user],
        ),
        out_shape=[
            jax.ShapeDtypeStruct((micro, all_cands, head_cols), jnp.float32),
            jax.ShapeDtypeStruct((USERS * micro * window, head_cols), jnp.float32),
            jax.ShapeDtypeStruct((USERS * micro * window, head_cols), jnp.float32),
        ],
        compiler_params=pltpu.CompilerParams(dimension_semantics=("arbitrary",)),
    )(tile_user, tile_rank, hist_len, user_info, last_block, first_rows, queries_all.astype(jnp.float32), k_cache, v_cache)

    reduced = reduce_over_hist(partial_value.reshape(micro, n_cand, n_hist, local_rows, head_cols))
    attended = spread_over_cand(reduced)
    attended = attended.reshape(micro * local_rows, model_width)
    average = jnp.mean(attended, axis=-1, keepdims=True)
    centered = attended - average
    spread_sq = jnp.mean(centered * centered, axis=-1, keepdims=True)
    normed = centered * lax.rsqrt(spread_sq + EPSILON)
    mixed_rows = (normed * gate_vals.astype(jnp.float32)).astype(jnp.bfloat16)
    ranked = jnp.dot(
        mixed_rows, out_weight, preferred_element_type=jnp.float32
    ) + cand_rows.astype(jnp.float32)
    return ranked.astype(jnp.bfloat16).reshape(micro, local_rows, model_width)


def solution(mesh):
    return jax.shard_map(
        body,
        mesh=mesh,
        in_specs=(
            P(None, ("cand", "hist"), None),
            P(),
            P(),
            P("hist", "cand"),
            P("hist", "cand"),
            P(),
            P(),
            P("hist"),
            P("hist"),
        ),
        out_specs=P(None, ("cand", "hist"), None),
        check_vma=False,
    )
```

```python
import functools

import jax
import jax.numpy as jnp
from jax import lax
from jax.experimental import pallas as pl
from jax.experimental.pallas import tpu as pltpu
from jax.sharding import PartitionSpec as P

HEAD_DIM = 128
TILE = 128
USERS = 16
MICRO = 2
BLOCK_TILES = 8


EPSILON = 1e-06


def silu_f32(x):
    return 0.5 * x * (1.0 + jnp.tanh(0.5 * x))


def attend_kernel(
    owner_ref, rank_ref, len_ref, user_ref, last_ref, row_ref,
    q_ref, k_ref, v_ref, out_ref, user_q, user_acc, *, window, heads_here, micro,
):
    block = pl.program_id(0)
    row_ids = lax.broadcasted_iota(jnp.int32, (window, 1), 0)
    pad = jnp.zeros((8, out_ref.shape[2]), jnp.float32)

    @pl.when(block == 0)
    def _():
        user_acc[...] = jnp.zeros_like(user_acc)
        for m in range(micro):
            def fill(user, carry):
                entry = (m * USERS + user) * 4
                span = pl.ds(pl.multiple_of(user_ref[entry], 8), window + 8)
                shift = user_ref[entry + 1]
                rows = pltpu.roll(q_ref[m, span, :], (window + 8 - shift) % (window + 8), 0)
                keep = (row_ids >= user_ref[entry + 2]) & (row_ids < user_ref[entry + 3])
                user_q[pl.ds(pl.multiple_of(user * (micro * window) + m * window, window), window), :] = jnp.where(
                    keep, rows[:window], 0.0
                )
                return carry

            lax.fori_loop(0, USERS, fill, 0)

    key_ids = lax.broadcasted_iota(jnp.int32, (TILE, 1), 0)

    def one_tile(j):
        if True:
            slot = block * BLOCK_TILES + j
            user = owner_ref[slot]
            klen = jnp.where(
                user < USERS, len_ref[jnp.minimum(user, USERS - 1)] - rank_ref[slot] * TILE, 0
            )
            rows = slice(j * TILE, (j + 1) * TILE)
            keys = jnp.where(key_ids < klen, k_ref[rows, :], 0)
            values = v_ref[rows, :]
            user_rows = pl.ds(pl.multiple_of(row_ref[slot], micro * window), micro * window)
            queries = user_q[user_rows, :].astype(jnp.bfloat16)
            if heads_here == 2:
                lanes = lax.broadcasted_iota(jnp.int32, (1, 2 * HEAD_DIM), 1)
                first = lanes < HEAD_DIM

                def diagonal(tile):
                    return jnp.concatenate(
                        [jnp.where(first, tile, 0), jnp.where(first, 0, tile)], axis=0
                    )

                scores = lax.dot_general(
                    queries,
                    diagonal(keys),
                    (((1,), (1,)), ((), ())),
                    preferred_element_type=jnp.float32,
                )
                weights = silu_f32(scores).astype(jnp.bfloat16)
                user_acc[user_rows, :] += jnp.dot(
                    weights, diagonal(values), preferred_element_type=jnp.float32
                )
            else:
                parts = []
                for h in range(heads_here):
                    cols = slice(h * HEAD_DIM, (h + 1) * HEAD_DIM)
                    scores = lax.dot_general(
                        queries[:, cols],
                        keys[:, cols],
                        (((1,), (1,)), ((), ())),
                        preferred_element_type=jnp.float32,
                    )
                    weights = silu_f32(scores).astype(jnp.bfloat16)
                    parts.append(
                        jnp.dot(weights, values[:, cols], preferred_element_type=jnp.float32)
                    )
                user_acc[user_rows, :] += jnp.concatenate(parts, axis=1) if heads_here > 1 else parts[0]


    @pl.when(block <= last_ref[0])
    def _():
        for j in range(BLOCK_TILES):
            one_tile(j)

    @pl.when(block == pl.num_programs(0) - 1)
    def _():
        out_ref[...] = jnp.zeros_like(out_ref)
        for m in range(micro):
            def place(user, carry):
                entry = (m * USERS + user) * 4
                span = pl.ds(pl.multiple_of(user_ref[entry], 8), window + 8)
                first = pl.multiple_of(user * (micro * window) + m * window, window)
                sums = jnp.concatenate([user_acc[pl.ds(first, window), :], pad])
                out_ref[m, span, :] += pltpu.roll(sums, user_ref[entry + 1], 0)
                return carry

            lax.fori_loop(0, USERS, place, 0)


def reduce_over_hist(partial):
    micro, n_cand, n_hist, rows, cols = partial.shape
    chips = n_hist // 2
    me = lax.axis_index("hist")
    chip, core = me // 2, me % 2
    halves = partial.reshape(micro, n_cand, chips, 2, rows, cols)
    mine = lax.dynamic_index_in_dim(halves, core, axis=3, keepdims=False)
    theirs = lax.dynamic_index_in_dim(halves, 1 - core, axis=3, keepdims=False)
    swapped = lax.ppermute(
        theirs.astype(jnp.bfloat16), "hist", perm=[(i, i ^ 1) for i in range(n_hist)]
    )
    chip_sums = mine + swapped.astype(jnp.float32)

    def block_of(index):
        index = jnp.clip(index, 0, chips - 1)
        return lax.dynamic_index_in_dim(chip_sums, index, axis=2, keepdims=False)

    total = block_of(chip)
    for shift in range(1, chips):
        send = block_of((chip + shift) % chips).astype(jnp.bfloat16)
        perm = [(2 * c + k, 2 * ((c + shift) % chips) + k) for c in range(chips) for k in range(2)]
        total = total + lax.ppermute(send, "hist", perm=perm).astype(jnp.float32)
    return total


def gather_queries(queries, n_cand, n_hist):
    micro, rows, width = queries.shape
    group = width // n_cand
    me_cand = lax.axis_index("cand")
    chunks = queries.reshape(micro, rows, n_cand, group)
    received = []
    for shift in range(n_cand):
        target = (me_cand + shift) % n_cand
        piece = lax.dynamic_index_in_dim(chunks, target, axis=2, keepdims=False)
        if shift:
            piece = lax.ppermute(
                piece, "cand", perm=[(i, (i + shift) % n_cand) for i in range(n_cand)]
            )
        received.append(piece)
    by_offset = jnp.stack(received)
    sources = jnp.stack(
        [
            lax.dynamic_index_in_dim(by_offset, (me_cand - c) % n_cand, axis=0, keepdims=False)
            for c in range(n_cand)
        ]
    )
    chips = n_hist // 2
    me = lax.axis_index("hist")
    chip, core = me // 2, me % 2
    by_offset = [sources]
    for shift in range(1, chips):
        perm = [(2 * c + k, 2 * ((c + shift) % chips) + k) for c in range(chips) for k in range(2)]
        by_offset.append(lax.ppermute(sources, "hist", perm=perm))
    by_offset = jnp.stack(by_offset)
    mine = jnp.stack(
        [
            lax.dynamic_index_in_dim(by_offset, (chip - c) % chips, axis=0, keepdims=False)
            for c in range(chips)
        ]
    )
    theirs = lax.ppermute(mine, "hist", perm=[(i, i ^ 1) for i in range(n_hist)])
    both = jnp.where(core == 0, jnp.stack([mine, theirs], axis=1), jnp.stack([theirs, mine], axis=1))
    both = both.reshape(n_hist, n_cand, micro, rows, group)
    return jnp.transpose(both, (2, 1, 0, 3, 4)).reshape(micro, n_cand * n_hist * rows, group)


def spread_over_cand(reduced):
    micro, n_cand, rows, group = reduced.shape
    me = lax.axis_index("cand")
    received = []
    for shift in range(n_cand):
        piece = lax.dynamic_index_in_dim(reduced, (me + shift) % n_cand, axis=1, keepdims=False)
        if shift:
            piece = lax.ppermute(
                piece, "cand", perm=[(i, (i + shift) % n_cand) for i in range(n_cand)]
            )
        received.append(piece)
    by_offset = jnp.stack(received)
    return jnp.concatenate(
        [
            lax.dynamic_index_in_dim(by_offset, (me - c) % n_cand, axis=0, keepdims=False)
            for c in range(n_cand)
        ],
        axis=-1,
    )


def body(
    cand_x, qu_weight, out_weight, k_cache, v_cache, hist_len, cand_count, tile_user, tile_rank
):
    n_cand = lax.axis_size("cand")
    n_hist = lax.axis_size("hist")
    micro, local_rows, model_width = cand_x.shape
    head_cols = k_cache.shape[1]
    heads_here = head_cols // HEAD_DIM
    tiles_here = k_cache.shape[0] // TILE

    cand_rows = cand_x.reshape(micro * local_rows, model_width)
    projected = jax.nn.silu(jnp.dot(cand_rows, qu_weight, preferred_element_type=jnp.float32))
    queries = projected[:, :model_width].astype(jnp.bfloat16).reshape(micro, local_rows, model_width)
    gate_vals = projected[:, model_width:].astype(jnp.bfloat16)
    queries_all = gather_queries(queries, n_cand, n_hist)
    all_cands = queries_all.shape[1]
    window = 2 * all_cands // USERS

    starts = jnp.cumsum(cand_count, axis=1) - cand_count
    offsets = jnp.minimum(starts, all_cands - window)
    base_rows = jnp.minimum(offsets // 8 * 8, all_cands - window - 8)
    shifts = offsets - base_rows
    lows = starts - offsets
    highs = lows + cand_count
    user_info = jnp.stack([base_rows, shifts, lows, highs], axis=2).astype(jnp.int32).reshape(-1)
    block_ids = jnp.arange(tiles_here, dtype=jnp.int32) // BLOCK_TILES
    last_block = jnp.max(jnp.where(tile_user < USERS, block_ids, 0)).reshape(1).astype(jnp.int32)

    first_rows = (jnp.minimum(tile_user, USERS - 1) * (micro * window)).astype(jnp.int32)
    rows_per_block = BLOCK_TILES * TILE
    n_blocks = tiles_here // BLOCK_TILES
    whole = pl.BlockSpec((micro, all_cands, head_cols), lambda b, *_: (0, 0, 0))
    tiles = pl.BlockSpec(
        (rows_per_block, head_cols), lambda b, *_: (jnp.minimum(b, _[4][0]), 0)
    )
    per_user = pl.BlockSpec((USERS * micro * window, head_cols), lambda b, *_: (0, 0))
    partial_value, _, _ = pl.pallas_call(
        functools.partial(attend_kernel, window=window, heads_here=heads_here, micro=micro),
        grid_spec=pltpu.PrefetchScalarGridSpec(
            num_scalar_prefetch=6,
            grid=(n_blocks,),
            in_specs=[whole, tiles, tiles],
            out_specs=[whole, per_user, per_user],
        ),
        out_shape=[
            jax.ShapeDtypeStruct((micro, all_cands, head_cols), jnp.float32),
            jax.ShapeDtypeStruct((USERS * micro * window, head_cols), jnp.float32),
            jax.ShapeDtypeStruct((USERS * micro * window, head_cols), jnp.float32),
        ],
        compiler_params=pltpu.CompilerParams(dimension_semantics=("arbitrary",)),
    )(tile_user, tile_rank, hist_len, user_info, last_block, first_rows, queries_all.astype(jnp.float32), k_cache, v_cache)

    reduced = reduce_over_hist(partial_value.reshape(micro, n_cand, n_hist, local_rows, head_cols))
    attended = spread_over_cand(reduced)
    attended = attended.reshape(micro * local_rows, model_width)
    average = jnp.mean(attended, axis=-1, keepdims=True)
    centered = attended - average
    spread_sq = jnp.mean(centered * centered, axis=-1, keepdims=True)
    normed = centered * lax.rsqrt(spread_sq + EPSILON)
    mixed_rows = (normed * gate_vals.astype(jnp.float32)).astype(jnp.bfloat16)
    ranked = jnp.dot(
        mixed_rows, out_weight, preferred_element_type=jnp.float32
    ) + cand_rows.astype(jnp.float32)
    return ranked.astype(jnp.bfloat16).reshape(micro, local_rows, model_width)


def solution(mesh):
    return jax.shard_map(
        body,
        mesh=mesh,
        in_specs=(
            P(None, ("cand", "hist"), None),
            P(),
            P(),
            P("hist", "cand"),
            P("hist", "cand"),
            P(),
            P(),
            P("hist"),
            P("hist"),
        ),
        out_specs=P(None, ("cand", "hist"), None),
        check_vma=False,
    )
```

```python
import functools

import jax
import jax.numpy as jnp
from jax import lax
from jax.experimental import pallas as pl
from jax.experimental.pallas import tpu as pltpu
from jax.sharding import PartitionSpec as P

HEAD_DIM = 128
TILE = 128
USERS = 16
MICRO = 2
BLOCK_TILES = 8


EPSILON = 1e-06


def silu_f32(x):
    return 0.5 * x * (1.0 + jnp.tanh(0.5 * x))


def attend_kernel(
    owner_ref, rank_ref, len_ref, user_ref, last_ref, row_ref,
    q_ref, k_ref, v_ref, out_ref, user_q, user_acc, *, window, heads_here, micro,
):
    block = pl.program_id(0)
    row_ids = lax.broadcasted_iota(jnp.int32, (window, 1), 0)
    pad = jnp.zeros((8, out_ref.shape[2]), jnp.float32)

    @pl.when(block == 0)
    def _():
        user_acc[...] = jnp.zeros_like(user_acc)
        for m in range(micro):
            def fill(user, carry):
                entry = (m * USERS + user) * 4
                span = pl.ds(pl.multiple_of(user_ref[entry], 8), window + 8)
                shift = user_ref[entry + 1]
                rows = pltpu.roll(q_ref[m, span, :], (window + 8 - shift) % (window + 8), 0)
                keep = (row_ids >= user_ref[entry + 2]) & (row_ids < user_ref[entry + 3])
                user_q[pl.ds(pl.multiple_of(user * (micro * window) + m * window, window), window), :] = jnp.where(
                    keep, rows[:window], 0.0
                )
                return carry

            lax.fori_loop(0, USERS, fill, 0)

    key_ids = lax.broadcasted_iota(jnp.int32, (TILE, 1), 0)

    def one_tile(j):
        if True:
            slot = block * BLOCK_TILES + j
            user = owner_ref[slot]
            klen = jnp.where(
                user < USERS, len_ref[jnp.minimum(user, USERS - 1)] - rank_ref[slot] * TILE, 0
            )
            rows = slice(j * TILE, (j + 1) * TILE)
            keys = jnp.where(key_ids < klen, k_ref[rows, :], 0)
            values = v_ref[rows, :]
            user_rows = pl.ds(pl.multiple_of(row_ref[slot], micro * window), micro * window)
            queries = user_q[user_rows, :].astype(jnp.bfloat16)
            if heads_here == 2:
                lanes = lax.broadcasted_iota(jnp.int32, (1, 2 * HEAD_DIM), 1)
                first = lanes < HEAD_DIM

                def diagonal(tile):
                    return jnp.concatenate(
                        [jnp.where(first, tile, 0), jnp.where(first, 0, tile)], axis=0
                    )

                scores = lax.dot_general(
                    queries,
                    diagonal(keys),
                    (((1,), (1,)), ((), ())),
                    preferred_element_type=jnp.float32,
                )
                weights = silu_f32(scores).astype(jnp.bfloat16)
                user_acc[user_rows, :] += jnp.dot(
                    weights, diagonal(values), preferred_element_type=jnp.float32
                )
            else:
                parts = []
                for h in range(heads_here):
                    cols = slice(h * HEAD_DIM, (h + 1) * HEAD_DIM)
                    scores = lax.dot_general(
                        queries[:, cols],
                        keys[:, cols],
                        (((1,), (1,)), ((), ())),
                        preferred_element_type=jnp.float32,
                    )
                    weights = silu_f32(scores).astype(jnp.bfloat16)
                    parts.append(
                        jnp.dot(weights, values[:, cols], preferred_element_type=jnp.float32)
                    )
                user_acc[user_rows, :] += jnp.concatenate(parts, axis=1) if heads_here > 1 else parts[0]


    @pl.when(block <= last_ref[0])
    def _():
        for j in range(BLOCK_TILES):
            one_tile(j)

    @pl.when(block == pl.num_programs(0) - 1)
    def _():
        out_ref[...] = jnp.zeros_like(out_ref)
        for m in range(micro):
            def place(user, carry):
                entry = (m * USERS + user) * 4
                span = pl.ds(pl.multiple_of(user_ref[entry], 8), window + 8)
                first = pl.multiple_of(user * (micro * window) + m * window, window)
                sums = jnp.concatenate([user_acc[pl.ds(first, window), :], pad])
                out_ref[m, span, :] += pltpu.roll(sums, user_ref[entry + 1], 0)
                return carry

            lax.fori_loop(0, USERS, place, 0)


def reduce_over_hist(partial):
    micro, n_cand, n_hist, rows, cols = partial.shape
    chips = n_hist // 2
    me = lax.axis_index("hist")
    chip, core = me // 2, me % 2
    halves = partial.reshape(micro, n_cand, chips, 2, rows, cols)
    mine = lax.dynamic_index_in_dim(halves, core, axis=3, keepdims=False)
    theirs = lax.dynamic_index_in_dim(halves, 1 - core, axis=3, keepdims=False)
    swapped = lax.ppermute(
        theirs.astype(jnp.bfloat16), "hist", perm=[(i, i ^ 1) for i in range(n_hist)]
    )
    chip_sums = mine + swapped.astype(jnp.float32)

    def block_of(index):
        index = jnp.clip(index, 0, chips - 1)
        return lax.dynamic_index_in_dim(chip_sums, index, axis=2, keepdims=False)

    total = block_of(chip)
    for shift in range(1, chips):
        send = block_of((chip + shift) % chips).astype(jnp.bfloat16)
        perm = [(2 * c + k, 2 * ((c + shift) % chips) + k) for c in range(chips) for k in range(2)]
        total = total + lax.ppermute(send, "hist", perm=perm).astype(jnp.float32)
    return total


def gather_queries(queries, n_cand, n_hist):
    micro, rows, width = queries.shape
    group = width // n_cand
    me_cand = lax.axis_index("cand")
    chunks = queries.reshape(micro, rows, n_cand, group)
    received = []
    for shift in range(n_cand):
        target = (me_cand + shift) % n_cand
        piece = lax.dynamic_index_in_dim(chunks, target, axis=2, keepdims=False)
        if shift:
            piece = lax.ppermute(
                piece, "cand", perm=[(i, (i + shift) % n_cand) for i in range(n_cand)]
            )
        received.append(piece)
    by_offset = jnp.stack(received)
    sources = jnp.stack(
        [
            lax.dynamic_index_in_dim(by_offset, (me_cand - c) % n_cand, axis=0, keepdims=False)
            for c in range(n_cand)
        ]
    )
    chips = n_hist // 2
    me = lax.axis_index("hist")
    chip, core = me // 2, me % 2
    by_offset = [sources]
    for shift in range(1, chips):
        perm = [(2 * c + k, 2 * ((c + shift) % chips) + k) for c in range(chips) for k in range(2)]
        by_offset.append(lax.ppermute(sources, "hist", perm=perm))
    by_offset = jnp.stack(by_offset)
    mine = jnp.stack(
        [
            lax.dynamic_index_in_dim(by_offset, (chip - c) % chips, axis=0, keepdims=False)
            for c in range(chips)
        ]
    )
    theirs = lax.ppermute(mine, "hist", perm=[(i, i ^ 1) for i in range(n_hist)])
    both = jnp.where(core == 0, jnp.stack([mine, theirs], axis=1), jnp.stack([theirs, mine], axis=1))
    both = both.reshape(n_hist, n_cand, micro, rows, group)
    return jnp.transpose(both, (2, 1, 0, 3, 4)).reshape(micro, n_cand * n_hist * rows, group)


def spread_over_cand(reduced):
    micro, n_cand, rows, group = reduced.shape
    me = lax.axis_index("cand")
    received = []
    for shift in range(n_cand):
        piece = lax.dynamic_index_in_dim(reduced, (me + shift) % n_cand, axis=1, keepdims=False)
        if shift:
            piece = lax.ppermute(
                piece, "cand", perm=[(i, (i + shift) % n_cand) for i in range(n_cand)]
            )
        received.append(piece)
    by_offset = jnp.stack(received)
    return jnp.concatenate(
        [
            lax.dynamic_index_in_dim(by_offset, (me - c) % n_cand, axis=0, keepdims=False)
            for c in range(n_cand)
        ],
        axis=-1,
    )


def body(
    cand_x, qu_weight, out_weight, k_cache, v_cache, hist_len, cand_count, tile_user, tile_rank
):
    n_cand = lax.axis_size("cand")
    n_hist = lax.axis_size("hist")
    micro, local_rows, model_width = cand_x.shape
    head_cols = k_cache.shape[1]
    heads_here = head_cols // HEAD_DIM
    tiles_here = k_cache.shape[0] // TILE

    cand_rows = cand_x.reshape(micro * local_rows, model_width)
    projected = jax.nn.silu(jnp.dot(cand_rows, qu_weight, preferred_element_type=jnp.float32))
    queries = projected[:, :model_width].astype(jnp.bfloat16).reshape(micro, local_rows, model_width)
    gate_vals = projected[:, model_width:].astype(jnp.bfloat16)
    queries_all = gather_queries(queries, n_cand, n_hist)
    all_cands = queries_all.shape[1]
    window = 2 * all_cands // USERS

    starts = jnp.cumsum(cand_count, axis=1) - cand_count
    offsets = jnp.minimum(starts, all_cands - window)
    base_rows = jnp.minimum(offsets // 8 * 8, all_cands - window - 8)
    shifts = offsets - base_rows
    lows = starts - offsets
    highs = lows + cand_count
    user_info = jnp.stack([base_rows, shifts, lows, highs], axis=2).astype(jnp.int32).reshape(-1)
    block_ids = jnp.arange(tiles_here, dtype=jnp.int32) // BLOCK_TILES
    last_block = jnp.max(jnp.where(tile_user < USERS, block_ids, 0)).reshape(1).astype(jnp.int32)

    first_rows = (jnp.minimum(tile_user, USERS - 1) * (micro * window)).astype(jnp.int32)
    rows_per_block = BLOCK_TILES * TILE
    n_blocks = tiles_here // BLOCK_TILES
    whole = pl.BlockSpec((micro, all_cands, head_cols), lambda b, *_: (0, 0, 0))
    tiles = pl.BlockSpec(
        (rows_per_block, head_cols), lambda b, *_: (jnp.minimum(b, _[4][0]), 0)
    )
    partial_value = pl.pallas_call(
        functools.partial(attend_kernel, window=window, heads_here=heads_here, micro=micro),
        grid_spec=pltpu.PrefetchScalarGridSpec(
            num_scalar_prefetch=6,
            grid=(n_blocks,),
            in_specs=[whole, tiles, tiles],
            out_specs=whole,
            scratch_shapes=[
                pltpu.VMEM((USERS * micro * window, head_cols), jnp.float32),
                pltpu.VMEM((USERS * micro * window, head_cols), jnp.float32),
            ],
        ),
        out_shape=jax.ShapeDtypeStruct((micro, all_cands, head_cols), jnp.float32),
        compiler_params=pltpu.CompilerParams(dimension_semantics=("arbitrary",)),
    )(tile_user, tile_rank, hist_len, user_info, last_block, first_rows, queries_all.astype(jnp.float32), k_cache, v_cache)

    reduced = reduce_over_hist(partial_value.reshape(micro, n_cand, n_hist, local_rows, head_cols))
    attended = spread_over_cand(reduced)
    attended = attended.reshape(micro * local_rows, model_width)
    average = jnp.mean(attended, axis=-1, keepdims=True)
    centered = attended - average
    spread_sq = jnp.mean(centered * centered, axis=-1, keepdims=True)
    normed = centered * lax.rsqrt(spread_sq + EPSILON)
    mixed_rows = (normed * gate_vals.astype(jnp.float32)).astype(jnp.bfloat16)
    ranked = jnp.dot(
        mixed_rows, out_weight, preferred_element_type=jnp.float32
    ) + cand_rows.astype(jnp.float32)
    return ranked.astype(jnp.bfloat16).reshape(micro, local_rows, model_width)


def solution(mesh):
    return jax.shard_map(
        body,
        mesh=mesh,
        in_specs=(
            P(None, ("cand", "hist"), None),
            P(),
            P(),
            P("hist", "cand"),
            P("hist", "cand"),
            P(),
            P(),
            P("hist"),
            P("hist"),
        ),
        out_specs=P(None, ("cand", "hist"), None),
        check_vma=False,
    )
```

```python
import functools

import jax
import jax.numpy as jnp
from jax import lax
from jax.experimental import pallas as pl
from jax.experimental.pallas import tpu as pltpu
from jax.sharding import PartitionSpec as P

HEAD_DIM = 128
TILE = 128
USERS = 16
MICRO = 2
BLOCK_TILES = 16


EPSILON = 1e-06


def silu_f32(x):
    return 0.5 * x * (1.0 + jnp.tanh(0.5 * x))


def attend_kernel(
    owner_ref, rank_ref, len_ref, user_ref, last_ref, row_ref,
    q_ref, k_ref, v_ref, out_ref, user_q, user_acc, *, window, heads_here, micro,
):
    block = pl.program_id(0)
    row_ids = lax.broadcasted_iota(jnp.int32, (window, 1), 0)
    pad = jnp.zeros((8, out_ref.shape[2]), jnp.float32)

    @pl.when(block == 0)
    def _():
        user_acc[...] = jnp.zeros_like(user_acc)
        for m in range(micro):
            def fill(user, carry):
                entry = (m * USERS + user) * 4
                span = pl.ds(pl.multiple_of(user_ref[entry], 8), window + 8)
                shift = user_ref[entry + 1]
                rows = pltpu.roll(q_ref[m, span, :], (window + 8 - shift) % (window + 8), 0)
                keep = (row_ids >= user_ref[entry + 2]) & (row_ids < user_ref[entry + 3])
                user_q[pl.ds(pl.multiple_of(user * (micro * window) + m * window, window), window), :] = jnp.where(
                    keep, rows[:window], 0.0
                )
                return carry

            lax.fori_loop(0, USERS, fill, 0)

    key_ids = lax.broadcasted_iota(jnp.int32, (TILE, 1), 0)

    def one_tile(j):
        if True:
            slot = block * BLOCK_TILES + j
            user = owner_ref[slot]
            klen = jnp.where(
                user < USERS, len_ref[jnp.minimum(user, USERS - 1)] - rank_ref[slot] * TILE, 0
            )
            rows = slice(j * TILE, (j + 1) * TILE)
            keys = jnp.where(key_ids < klen, k_ref[rows, :], 0)
            values = v_ref[rows, :]
            user_rows = pl.ds(pl.multiple_of(row_ref[slot], micro * window), micro * window)
            queries = user_q[user_rows, :].astype(jnp.bfloat16)
            if heads_here == 2:
                lanes = lax.broadcasted_iota(jnp.int32, (1, 2 * HEAD_DIM), 1)
                first = lanes < HEAD_DIM

                def diagonal(tile):
                    return jnp.concatenate(
                        [jnp.where(first, tile, 0), jnp.where(first, 0, tile)], axis=0
                    )

                scores = lax.dot_general(
                    queries,
                    diagonal(keys),
                    (((1,), (1,)), ((), ())),
                    preferred_element_type=jnp.float32,
                )
                weights = silu_f32(scores).astype(jnp.bfloat16)
                user_acc[user_rows, :] += jnp.dot(
                    weights, diagonal(values), preferred_element_type=jnp.float32
                )
            else:
                parts = []
                for h in range(heads_here):
                    cols = slice(h * HEAD_DIM, (h + 1) * HEAD_DIM)
                    scores = lax.dot_general(
                        queries[:, cols],
                        keys[:, cols],
                        (((1,), (1,)), ((), ())),
                        preferred_element_type=jnp.float32,
                    )
                    weights = silu_f32(scores).astype(jnp.bfloat16)
                    parts.append(
                        jnp.dot(weights, values[:, cols], preferred_element_type=jnp.float32)
                    )
                user_acc[user_rows, :] += jnp.concatenate(parts, axis=1) if heads_here > 1 else parts[0]


    @pl.when(block <= last_ref[0])
    def _():
        for j in range(BLOCK_TILES):
            one_tile(j)

    @pl.when(block == pl.num_programs(0) - 1)
    def _():
        out_ref[...] = jnp.zeros_like(out_ref)
        for m in range(micro):
            def place(user, carry):
                entry = (m * USERS + user) * 4
                span = pl.ds(pl.multiple_of(user_ref[entry], 8), window + 8)
                first = pl.multiple_of(user * (micro * window) + m * window, window)
                sums = jnp.concatenate([user_acc[pl.ds(first, window), :], pad])
                out_ref[m, span, :] += pltpu.roll(sums, user_ref[entry + 1], 0)
                return carry

            lax.fori_loop(0, USERS, place, 0)


def reduce_over_hist(partial):
    micro, n_cand, n_hist, rows, cols = partial.shape
    chips = n_hist // 2
    me = lax.axis_index("hist")
    chip, core = me // 2, me % 2
    halves = partial.reshape(micro, n_cand, chips, 2, rows, cols)
    mine = lax.dynamic_index_in_dim(halves, core, axis=3, keepdims=False)
    theirs = lax.dynamic_index_in_dim(halves, 1 - core, axis=3, keepdims=False)
    swapped = lax.ppermute(
        theirs.astype(jnp.bfloat16), "hist", perm=[(i, i ^ 1) for i in range(n_hist)]
    )
    chip_sums = mine + swapped.astype(jnp.float32)

    def block_of(index):
        index = jnp.clip(index, 0, chips - 1)
        return lax.dynamic_index_in_dim(chip_sums, index, axis=2, keepdims=False)

    total = block_of(chip)
    for shift in range(1, chips):
        send = block_of((chip + shift) % chips).astype(jnp.bfloat16)
        perm = [(2 * c + k, 2 * ((c + shift) % chips) + k) for c in range(chips) for k in range(2)]
        total = total + lax.ppermute(send, "hist", perm=perm).astype(jnp.float32)
    return total


def gather_queries(queries, n_cand, n_hist):
    micro, rows, width = queries.shape
    group = width // n_cand
    me_cand = lax.axis_index("cand")
    chunks = queries.reshape(micro, rows, n_cand, group)
    received = []
    for shift in range(n_cand):
        target = (me_cand + shift) % n_cand
        piece = lax.dynamic_index_in_dim(chunks, target, axis=2, keepdims=False)
        if shift:
            piece = lax.ppermute(
                piece, "cand", perm=[(i, (i + shift) % n_cand) for i in range(n_cand)]
            )
        received.append(piece)
    by_offset = jnp.stack(received)
    sources = jnp.stack(
        [
            lax.dynamic_index_in_dim(by_offset, (me_cand - c) % n_cand, axis=0, keepdims=False)
            for c in range(n_cand)
        ]
    )
    chips = n_hist // 2
    me = lax.axis_index("hist")
    chip, core = me // 2, me % 2
    by_offset = [sources]
    for shift in range(1, chips):
        perm = [(2 * c + k, 2 * ((c + shift) % chips) + k) for c in range(chips) for k in range(2)]
        by_offset.append(lax.ppermute(sources, "hist", perm=perm))
    by_offset = jnp.stack(by_offset)
    mine = jnp.stack(
        [
            lax.dynamic_index_in_dim(by_offset, (chip - c) % chips, axis=0, keepdims=False)
            for c in range(chips)
        ]
    )
    theirs = lax.ppermute(mine, "hist", perm=[(i, i ^ 1) for i in range(n_hist)])
    both = jnp.where(core == 0, jnp.stack([mine, theirs], axis=1), jnp.stack([theirs, mine], axis=1))
    both = both.reshape(n_hist, n_cand, micro, rows, group)
    return jnp.transpose(both, (2, 1, 0, 3, 4)).reshape(micro, n_cand * n_hist * rows, group)


def spread_over_cand(reduced):
    micro, n_cand, rows, group = reduced.shape
    me = lax.axis_index("cand")
    received = []
    for shift in range(n_cand):
        piece = lax.dynamic_index_in_dim(reduced, (me + shift) % n_cand, axis=1, keepdims=False)
        if shift:
            piece = lax.ppermute(
                piece, "cand", perm=[(i, (i + shift) % n_cand) for i in range(n_cand)]
            )
        received.append(piece)
    by_offset = jnp.stack(received)
    return jnp.concatenate(
        [
            lax.dynamic_index_in_dim(by_offset, (me - c) % n_cand, axis=0, keepdims=False)
            for c in range(n_cand)
        ],
        axis=-1,
    )


def body(
    cand_x, qu_weight, out_weight, k_cache, v_cache, hist_len, cand_count, tile_user, tile_rank
):
    n_cand = lax.axis_size("cand")
    n_hist = lax.axis_size("hist")
    micro, local_rows, model_width = cand_x.shape
    head_cols = k_cache.shape[1]
    heads_here = head_cols // HEAD_DIM
    tiles_here = k_cache.shape[0] // TILE

    cand_rows = cand_x.reshape(micro * local_rows, model_width)
    queries = jax.nn.silu(
        jnp.dot(cand_rows, qu_weight[:, :model_width], preferred_element_type=jnp.float32)
    )
    queries = queries.astype(jnp.bfloat16).reshape(micro, local_rows, model_width)
    gate_vals = jax.nn.silu(
        jnp.dot(cand_rows, qu_weight[:, model_width:], preferred_element_type=jnp.float32)
    ).astype(jnp.bfloat16)
    queries_all = gather_queries(queries, n_cand, n_hist)
    all_cands = queries_all.shape[1]
    window = 2 * all_cands // USERS

    starts = jnp.cumsum(cand_count, axis=1) - cand_count
    offsets = jnp.minimum(starts, all_cands - window)
    base_rows = jnp.minimum(offsets // 8 * 8, all_cands - window - 8)
    shifts = offsets - base_rows
    lows = starts - offsets
    highs = lows + cand_count
    user_info = jnp.stack([base_rows, shifts, lows, highs], axis=2).astype(jnp.int32).reshape(-1)
    block_ids = jnp.arange(tiles_here, dtype=jnp.int32) // BLOCK_TILES
    last_block = jnp.max(jnp.where(tile_user < USERS, block_ids, 0)).reshape(1).astype(jnp.int32)

    first_rows = (jnp.minimum(tile_user, USERS - 1) * (micro * window)).astype(jnp.int32)
    rows_per_block = BLOCK_TILES * TILE
    n_blocks = tiles_here // BLOCK_TILES
    whole = pl.BlockSpec((micro, all_cands, head_cols), lambda b, *_: (0, 0, 0))
    tiles = pl.BlockSpec(
        (rows_per_block, head_cols), lambda b, *_: (jnp.minimum(b, _[4][0]), 0)
    )
    partial_value = pl.pallas_call(
        functools.partial(attend_kernel, window=window, heads_here=heads_here, micro=micro),
        grid_spec=pltpu.PrefetchScalarGridSpec(
            num_scalar_prefetch=6,
            grid=(n_blocks,),
            in_specs=[whole, tiles, tiles],
            out_specs=whole,
            scratch_shapes=[
                pltpu.VMEM((USERS * micro * window, head_cols), jnp.float32),
                pltpu.VMEM((USERS * micro * window, head_cols), jnp.float32),
            ],
        ),
        out_shape=jax.ShapeDtypeStruct((micro, all_cands, head_cols), jnp.float32),
        compiler_params=pltpu.CompilerParams(dimension_semantics=("arbitrary",)),
    )(tile_user, tile_rank, hist_len, user_info, last_block, first_rows, queries_all.astype(jnp.float32), k_cache, v_cache)

    reduced = reduce_over_hist(partial_value.reshape(micro, n_cand, n_hist, local_rows, head_cols))
    attended = spread_over_cand(reduced)
    attended = attended.reshape(micro * local_rows, model_width)
    average = jnp.mean(attended, axis=-1, keepdims=True)
    centered = attended - average
    spread_sq = jnp.mean(centered * centered, axis=-1, keepdims=True)
    normed = centered * lax.rsqrt(spread_sq + EPSILON)
    mixed_rows = (normed * gate_vals.astype(jnp.float32)).astype(jnp.bfloat16)
    ranked = jnp.dot(
        mixed_rows, out_weight, preferred_element_type=jnp.float32
    ) + cand_rows.astype(jnp.float32)
    return ranked.astype(jnp.bfloat16).reshape(micro, local_rows, model_width)


def solution(mesh):
    return jax.shard_map(
        body,
        mesh=mesh,
        in_specs=(
            P(None, ("cand", "hist"), None),
            P(),
            P(),
            P("hist", "cand"),
            P("hist", "cand"),
            P(),
            P(),
            P("hist"),
            P("hist"),
        ),
        out_specs=P(None, ("cand", "hist"), None),
        check_vma=False,
    )
```

```python
import functools

import jax
import jax.numpy as jnp
from jax import lax
from jax.experimental import pallas as pl
from jax.experimental.pallas import tpu as pltpu
from jax.sharding import PartitionSpec as P

HEAD_DIM = 128
TILE = 128
USERS = 16
MICRO = 2
BLOCK_TILES = 16


EPSILON = 1e-06


def silu_f32(x):
    return 0.5 * x * (1.0 + jnp.tanh(0.5 * x))


def attend_kernel(
    owner_ref, rank_ref, len_ref, user_ref, last_ref, row_ref,
    q_ref, k_ref, v_ref, out_ref, user_q, user_acc, *, window, heads_here, micro,
):
    block = pl.program_id(0)
    row_ids = lax.broadcasted_iota(jnp.int32, (window, 1), 0)
    pad = jnp.zeros((8, out_ref.shape[2]), jnp.float32)

    @pl.when(block == 0)
    def _():
        user_acc[...] = jnp.zeros_like(user_acc)
        for m in range(micro):
            def fill(user, carry):
                entry = (m * USERS + user) * 4
                span = pl.ds(pl.multiple_of(user_ref[entry], 8), window + 8)
                shift = user_ref[entry + 1]
                rows = pltpu.roll(q_ref[m, span, :], (window + 8 - shift) % (window + 8), 0)
                keep = (row_ids >= user_ref[entry + 2]) & (row_ids < user_ref[entry + 3])
                user_q[pl.ds(pl.multiple_of(user * (micro * window) + m * window, window), window), :] = jnp.where(
                    keep, rows[:window], 0.0
                ).astype(jnp.bfloat16)
                return carry

            lax.fori_loop(0, USERS, fill, 0)

    key_ids = lax.broadcasted_iota(jnp.int32, (TILE, 1), 0)

    def one_tile(j):
        if True:
            slot = block * BLOCK_TILES + j
            user = owner_ref[slot]
            klen = jnp.where(
                user < USERS, len_ref[jnp.minimum(user, USERS - 1)] - rank_ref[slot] * TILE, 0
            )
            rows = slice(j * TILE, (j + 1) * TILE)
            keys = jnp.where(key_ids < klen, k_ref[rows, :], 0)
            values = v_ref[rows, :]
            user_rows = pl.ds(pl.multiple_of(row_ref[slot], micro * window), micro * window)
            queries = user_q[user_rows, :]
            if heads_here == 2:
                lanes = lax.broadcasted_iota(jnp.int32, (1, 2 * HEAD_DIM), 1)
                first = lanes < HEAD_DIM

                def diagonal(tile):
                    return jnp.concatenate(
                        [jnp.where(first, tile, 0), jnp.where(first, 0, tile)], axis=0
                    )

                scores = lax.dot_general(
                    queries,
                    diagonal(keys),
                    (((1,), (1,)), ((), ())),
                    preferred_element_type=jnp.float32,
                )
                weights = silu_f32(scores).astype(jnp.bfloat16)
                user_acc[user_rows, :] += jnp.dot(
                    weights, diagonal(values), preferred_element_type=jnp.float32
                )
            else:
                parts = []
                for h in range(heads_here):
                    cols = slice(h * HEAD_DIM, (h + 1) * HEAD_DIM)
                    scores = lax.dot_general(
                        queries[:, cols],
                        keys[:, cols],
                        (((1,), (1,)), ((), ())),
                        preferred_element_type=jnp.float32,
                    )
                    weights = silu_f32(scores).astype(jnp.bfloat16)
                    parts.append(
                        jnp.dot(weights, values[:, cols], preferred_element_type=jnp.float32)
                    )
                user_acc[user_rows, :] += jnp.concatenate(parts, axis=1) if heads_here > 1 else parts[0]


    @pl.when(block <= last_ref[0])
    def _():
        for j in range(BLOCK_TILES):
            one_tile(j)

    @pl.when(block == pl.num_programs(0) - 1)
    def _():
        out_ref[...] = jnp.zeros_like(out_ref)
        for m in range(micro):
            def place(user, carry):
                entry = (m * USERS + user) * 4
                span = pl.ds(pl.multiple_of(user_ref[entry], 8), window + 8)
                first = pl.multiple_of(user * (micro * window) + m * window, window)
                sums = jnp.concatenate([user_acc[pl.ds(first, window), :], pad])
                out_ref[m, span, :] += pltpu.roll(sums, user_ref[entry + 1], 0)
                return carry

            lax.fori_loop(0, USERS, place, 0)


def reduce_over_hist(partial):
    micro, n_cand, n_hist, rows, cols = partial.shape
    chips = n_hist // 2
    me = lax.axis_index("hist")
    chip, core = me // 2, me % 2
    halves = partial.reshape(micro, n_cand, chips, 2, rows, cols)
    mine = lax.dynamic_index_in_dim(halves, core, axis=3, keepdims=False)
    theirs = lax.dynamic_index_in_dim(halves, 1 - core, axis=3, keepdims=False)
    swapped = lax.ppermute(
        theirs.astype(jnp.bfloat16), "hist", perm=[(i, i ^ 1) for i in range(n_hist)]
    )
    chip_sums = mine + swapped.astype(jnp.float32)

    def block_of(index):
        index = jnp.clip(index, 0, chips - 1)
        return lax.dynamic_index_in_dim(chip_sums, index, axis=2, keepdims=False)

    total = block_of(chip)
    for shift in range(1, chips):
        send = block_of((chip + shift) % chips).astype(jnp.bfloat16)
        perm = [(2 * c + k, 2 * ((c + shift) % chips) + k) for c in range(chips) for k in range(2)]
        total = total + lax.ppermute(send, "hist", perm=perm).astype(jnp.float32)
    return total


def gather_queries(queries, n_cand, n_hist):
    micro, rows, width = queries.shape
    group = width // n_cand
    me_cand = lax.axis_index("cand")
    chunks = queries.reshape(micro, rows, n_cand, group)
    received = []
    for shift in range(n_cand):
        target = (me_cand + shift) % n_cand
        piece = lax.dynamic_index_in_dim(chunks, target, axis=2, keepdims=False)
        if shift:
            piece = lax.ppermute(
                piece, "cand", perm=[(i, (i + shift) % n_cand) for i in range(n_cand)]
            )
        received.append(piece)
    by_offset = jnp.stack(received)
    sources = jnp.stack(
        [
            lax.dynamic_index_in_dim(by_offset, (me_cand - c) % n_cand, axis=0, keepdims=False)
            for c in range(n_cand)
        ]
    )
    chips = n_hist // 2
    me = lax.axis_index("hist")
    chip, core = me // 2, me % 2
    by_offset = [sources]
    for shift in range(1, chips):
        perm = [(2 * c + k, 2 * ((c + shift) % chips) + k) for c in range(chips) for k in range(2)]
        by_offset.append(lax.ppermute(sources, "hist", perm=perm))
    by_offset = jnp.stack(by_offset)
    mine = jnp.stack(
        [
            lax.dynamic_index_in_dim(by_offset, (chip - c) % chips, axis=0, keepdims=False)
            for c in range(chips)
        ]
    )
    theirs = lax.ppermute(mine, "hist", perm=[(i, i ^ 1) for i in range(n_hist)])
    both = jnp.where(core == 0, jnp.stack([mine, theirs], axis=1), jnp.stack([theirs, mine], axis=1))
    both = both.reshape(n_hist, n_cand, micro, rows, group)
    return jnp.transpose(both, (2, 1, 0, 3, 4)).reshape(micro, n_cand * n_hist * rows, group)


def spread_over_cand(reduced):
    micro, n_cand, rows, group = reduced.shape
    me = lax.axis_index("cand")
    received = []
    for shift in range(n_cand):
        piece = lax.dynamic_index_in_dim(reduced, (me + shift) % n_cand, axis=1, keepdims=False)
        if shift:
            piece = lax.ppermute(
                piece, "cand", perm=[(i, (i + shift) % n_cand) for i in range(n_cand)]
            )
        received.append(piece)
    by_offset = jnp.stack(received)
    return jnp.concatenate(
        [
            lax.dynamic_index_in_dim(by_offset, (me - c) % n_cand, axis=0, keepdims=False)
            for c in range(n_cand)
        ],
        axis=-1,
    )


def body(
    cand_x, qu_weight, out_weight, k_cache, v_cache, hist_len, cand_count, tile_user, tile_rank
):
    n_cand = lax.axis_size("cand")
    n_hist = lax.axis_size("hist")
    micro, local_rows, model_width = cand_x.shape
    head_cols = k_cache.shape[1]
    heads_here = head_cols // HEAD_DIM
    tiles_here = k_cache.shape[0] // TILE

    cand_rows = cand_x.reshape(micro * local_rows, model_width)
    queries = jax.nn.silu(
        jnp.dot(cand_rows, qu_weight[:, :model_width], preferred_element_type=jnp.float32)
    )
    queries = queries.astype(jnp.bfloat16).reshape(micro, local_rows, model_width)
    gate_vals = jax.nn.silu(
        jnp.dot(cand_rows, qu_weight[:, model_width:], preferred_element_type=jnp.float32)
    ).astype(jnp.bfloat16)
    queries_all = gather_queries(queries, n_cand, n_hist)
    all_cands = queries_all.shape[1]
    window = 2 * all_cands // USERS

    starts = jnp.cumsum(cand_count, axis=1) - cand_count
    offsets = jnp.minimum(starts, all_cands - window)
    base_rows = jnp.minimum(offsets // 8 * 8, all_cands - window - 8)
    shifts = offsets - base_rows
    lows = starts - offsets
    highs = lows + cand_count
    user_info = jnp.stack([base_rows, shifts, lows, highs], axis=2).astype(jnp.int32).reshape(-1)
    block_ids = jnp.arange(tiles_here, dtype=jnp.int32) // BLOCK_TILES
    last_block = jnp.max(jnp.where(tile_user < USERS, block_ids, 0)).reshape(1).astype(jnp.int32)

    first_rows = (jnp.minimum(tile_user, USERS - 1) * (micro * window)).astype(jnp.int32)
    rows_per_block = BLOCK_TILES * TILE
    n_blocks = tiles_here // BLOCK_TILES
    whole = pl.BlockSpec((micro, all_cands, head_cols), lambda b, *_: (0, 0, 0))
    tiles = pl.BlockSpec(
        (rows_per_block, head_cols), lambda b, *_: (jnp.minimum(b, _[4][0]), 0)
    )
    partial_value = pl.pallas_call(
        functools.partial(attend_kernel, window=window, heads_here=heads_here, micro=micro),
        grid_spec=pltpu.PrefetchScalarGridSpec(
            num_scalar_prefetch=6,
            grid=(n_blocks,),
            in_specs=[whole, tiles, tiles],
            out_specs=whole,
            scratch_shapes=[
                pltpu.VMEM((USERS * micro * window, head_cols), jnp.bfloat16),
                pltpu.VMEM((USERS * micro * window, head_cols), jnp.float32),
            ],
        ),
        out_shape=jax.ShapeDtypeStruct((micro, all_cands, head_cols), jnp.float32),
        compiler_params=pltpu.CompilerParams(dimension_semantics=("arbitrary",)),
    )(tile_user, tile_rank, hist_len, user_info, last_block, first_rows, queries_all.astype(jnp.float32), k_cache, v_cache)

    reduced = reduce_over_hist(partial_value.reshape(micro, n_cand, n_hist, local_rows, head_cols))
    attended = spread_over_cand(reduced)
    attended = attended.reshape(micro * local_rows, model_width)
    average = jnp.mean(attended, axis=-1, keepdims=True)
    centered = attended - average
    spread_sq = jnp.mean(centered * centered, axis=-1, keepdims=True)
    normed = centered * lax.rsqrt(spread_sq + EPSILON)
    mixed_rows = (normed * gate_vals.astype(jnp.float32)).astype(jnp.bfloat16)
    ranked = jnp.dot(
        mixed_rows, out_weight, preferred_element_type=jnp.float32
    ) + cand_rows.astype(jnp.float32)
    return ranked.astype(jnp.bfloat16).reshape(micro, local_rows, model_width)


def solution(mesh):
    return jax.shard_map(
        body,
        mesh=mesh,
        in_specs=(
            P(None, ("cand", "hist"), None),
            P(),
            P(),
            P("hist", "cand"),
            P("hist", "cand"),
            P(),
            P(),
            P("hist"),
            P("hist"),
        ),
        out_specs=P(None, ("cand", "hist"), None),
        check_vma=False,
    )
```

```python
import functools

import jax
import jax.numpy as jnp
from jax import lax
from jax.experimental import pallas as pl
from jax.experimental.pallas import tpu as pltpu
from jax.sharding import PartitionSpec as P

HEAD_DIM = 128
TILE = 128
USERS = 16
MICRO = 2
BLOCK_TILES = 16


EPSILON = 1e-06


def silu_f32(x):
    return 0.5 * x * (1.0 + jnp.tanh(0.5 * x))


def attend_kernel(
    owner_ref, rank_ref, len_ref, user_ref, last_ref, row_ref,
    q_ref, k_ref, v_ref, out_ref, user_q, user_acc, *, window, heads_here, micro,
):
    block = pl.program_id(0)
    row_ids = lax.broadcasted_iota(jnp.int32, (window, 1), 0)
    pad = jnp.zeros((16, out_ref.shape[2]), jnp.float32)

    @pl.when(block == 0)
    def _():
        user_acc[...] = jnp.zeros_like(user_acc)
        for m in range(micro):
            def fill(user, carry):
                entry = (m * USERS + user) * 4
                span = pl.ds(pl.multiple_of(user_ref[entry], 16), window + 16)
                shift = user_ref[entry + 1]
                rows = q_ref[m, span, :].astype(jnp.float32)
                rows = pltpu.roll(rows, (window + 16 - shift) % (window + 16), 0)
                keep = (row_ids >= user_ref[entry + 2]) & (row_ids < user_ref[entry + 3])
                user_q[pl.ds(pl.multiple_of(user * (micro * window) + m * window, window), window), :] = jnp.where(
                    keep, rows[:window], 0.0
                ).astype(jnp.bfloat16)
                return carry

            lax.fori_loop(0, USERS, fill, 0)

    key_ids = lax.broadcasted_iota(jnp.int32, (TILE, 1), 0)

    def one_tile(j):
        if True:
            slot = block * BLOCK_TILES + j
            user = owner_ref[slot]
            klen = jnp.where(
                user < USERS, len_ref[jnp.minimum(user, USERS - 1)] - rank_ref[slot] * TILE, 0
            )
            rows = slice(j * TILE, (j + 1) * TILE)
            keys = jnp.where(key_ids < klen, k_ref[rows, :], 0)
            values = v_ref[rows, :]
            user_rows = pl.ds(pl.multiple_of(row_ref[slot], micro * window), micro * window)
            queries = user_q[user_rows, :]
            if heads_here == 2:
                lanes = lax.broadcasted_iota(jnp.int32, (1, 2 * HEAD_DIM), 1)
                first = lanes < HEAD_DIM

                def diagonal(tile):
                    return jnp.concatenate(
                        [jnp.where(first, tile, 0), jnp.where(first, 0, tile)], axis=0
                    )

                scores = lax.dot_general(
                    queries,
                    diagonal(keys),
                    (((1,), (1,)), ((), ())),
                    preferred_element_type=jnp.float32,
                )
                weights = silu_f32(scores).astype(jnp.bfloat16)
                user_acc[user_rows, :] += jnp.dot(
                    weights, diagonal(values), preferred_element_type=jnp.float32
                )
            else:
                parts = []
                for h in range(heads_here):
                    cols = slice(h * HEAD_DIM, (h + 1) * HEAD_DIM)
                    scores = lax.dot_general(
                        queries[:, cols],
                        keys[:, cols],
                        (((1,), (1,)), ((), ())),
                        preferred_element_type=jnp.float32,
                    )
                    weights = silu_f32(scores).astype(jnp.bfloat16)
                    parts.append(
                        jnp.dot(weights, values[:, cols], preferred_element_type=jnp.float32)
                    )
                user_acc[user_rows, :] += jnp.concatenate(parts, axis=1) if heads_here > 1 else parts[0]


    @pl.when(block <= last_ref[0])
    def _():
        for j in range(BLOCK_TILES):
            one_tile(j)

    @pl.when(block == pl.num_programs(0) - 1)
    def _():
        out_ref[...] = jnp.zeros_like(out_ref)
        for m in range(micro):
            def place(user, carry):
                entry = (m * USERS + user) * 4
                span = pl.ds(pl.multiple_of(user_ref[entry], 16), window + 16)
                first = pl.multiple_of(user * (micro * window) + m * window, window)
                sums = jnp.concatenate([user_acc[pl.ds(first, window), :], pad])
                out_ref[m, span, :] += pltpu.roll(sums, user_ref[entry + 1], 0)
                return carry

            lax.fori_loop(0, USERS, place, 0)


def reduce_over_hist(partial):
    micro, n_cand, n_hist, rows, cols = partial.shape
    chips = n_hist // 2
    me = lax.axis_index("hist")
    chip, core = me // 2, me % 2
    halves = partial.reshape(micro, n_cand, chips, 2, rows, cols)
    mine = lax.dynamic_index_in_dim(halves, core, axis=3, keepdims=False)
    theirs = lax.dynamic_index_in_dim(halves, 1 - core, axis=3, keepdims=False)
    swapped = lax.ppermute(
        theirs.astype(jnp.bfloat16), "hist", perm=[(i, i ^ 1) for i in range(n_hist)]
    )
    chip_sums = mine + swapped.astype(jnp.float32)

    def block_of(index):
        index = jnp.clip(index, 0, chips - 1)
        return lax.dynamic_index_in_dim(chip_sums, index, axis=2, keepdims=False)

    total = block_of(chip)
    for shift in range(1, chips):
        send = block_of((chip + shift) % chips).astype(jnp.bfloat16)
        perm = [(2 * c + k, 2 * ((c + shift) % chips) + k) for c in range(chips) for k in range(2)]
        total = total + lax.ppermute(send, "hist", perm=perm).astype(jnp.float32)
    return total


def gather_queries(queries, n_cand, n_hist):
    micro, rows, width = queries.shape
    group = width // n_cand
    me_cand = lax.axis_index("cand")
    chunks = queries.reshape(micro, rows, n_cand, group)
    received = []
    for shift in range(n_cand):
        target = (me_cand + shift) % n_cand
        piece = lax.dynamic_index_in_dim(chunks, target, axis=2, keepdims=False)
        if shift:
            piece = lax.ppermute(
                piece, "cand", perm=[(i, (i + shift) % n_cand) for i in range(n_cand)]
            )
        received.append(piece)
    by_offset = jnp.stack(received)
    sources = jnp.stack(
        [
            lax.dynamic_index_in_dim(by_offset, (me_cand - c) % n_cand, axis=0, keepdims=False)
            for c in range(n_cand)
        ]
    )
    chips = n_hist // 2
    me = lax.axis_index("hist")
    chip, core = me // 2, me % 2
    by_offset = [sources]
    for shift in range(1, chips):
        perm = [(2 * c + k, 2 * ((c + shift) % chips) + k) for c in range(chips) for k in range(2)]
        by_offset.append(lax.ppermute(sources, "hist", perm=perm))
    by_offset = jnp.stack(by_offset)
    mine = jnp.stack(
        [
            lax.dynamic_index_in_dim(by_offset, (chip - c) % chips, axis=0, keepdims=False)
            for c in range(chips)
        ]
    )
    theirs = lax.ppermute(mine, "hist", perm=[(i, i ^ 1) for i in range(n_hist)])
    both = jnp.where(core == 0, jnp.stack([mine, theirs], axis=1), jnp.stack([theirs, mine], axis=1))
    both = both.reshape(n_hist, n_cand, micro, rows, group)
    return jnp.transpose(both, (2, 1, 0, 3, 4)).reshape(micro, n_cand * n_hist * rows, group)


def spread_over_cand(reduced):
    micro, n_cand, rows, group = reduced.shape
    me = lax.axis_index("cand")
    received = []
    for shift in range(n_cand):
        piece = lax.dynamic_index_in_dim(reduced, (me + shift) % n_cand, axis=1, keepdims=False)
        if shift:
            piece = lax.ppermute(
                piece, "cand", perm=[(i, (i + shift) % n_cand) for i in range(n_cand)]
            )
        received.append(piece)
    by_offset = jnp.stack(received)
    return jnp.concatenate(
        [
            lax.dynamic_index_in_dim(by_offset, (me - c) % n_cand, axis=0, keepdims=False)
            for c in range(n_cand)
        ],
        axis=-1,
    )


def body(
    cand_x, qu_weight, out_weight, k_cache, v_cache, hist_len, cand_count, tile_user, tile_rank
):
    n_cand = lax.axis_size("cand")
    n_hist = lax.axis_size("hist")
    micro, local_rows, model_width = cand_x.shape
    head_cols = k_cache.shape[1]
    heads_here = head_cols // HEAD_DIM
    tiles_here = k_cache.shape[0] // TILE

    cand_rows = cand_x.reshape(micro * local_rows, model_width)
    queries = jax.nn.silu(
        jnp.dot(cand_rows, qu_weight[:, :model_width], preferred_element_type=jnp.float32)
    )
    queries = queries.astype(jnp.bfloat16).reshape(micro, local_rows, model_width)
    gate_vals = jax.nn.silu(
        jnp.dot(cand_rows, qu_weight[:, model_width:], preferred_element_type=jnp.float32)
    ).astype(jnp.bfloat16)
    queries_all = gather_queries(queries, n_cand, n_hist)
    all_cands = queries_all.shape[1]
    window = 2 * all_cands // USERS

    starts = jnp.cumsum(cand_count, axis=1) - cand_count
    offsets = jnp.minimum(starts, all_cands - window)
    base_rows = jnp.minimum(offsets // 16 * 16, all_cands - window - 16)
    shifts = offsets - base_rows
    lows = starts - offsets
    highs = lows + cand_count
    user_info = jnp.stack([base_rows, shifts, lows, highs], axis=2).astype(jnp.int32).reshape(-1)
    block_ids = jnp.arange(tiles_here, dtype=jnp.int32) // BLOCK_TILES
    last_block = jnp.max(jnp.where(tile_user < USERS, block_ids, 0)).reshape(1).astype(jnp.int32)

    first_rows = (jnp.minimum(tile_user, USERS - 1) * (micro * window)).astype(jnp.int32)
    rows_per_block = BLOCK_TILES * TILE
    n_blocks = tiles_here // BLOCK_TILES
    whole = pl.BlockSpec((micro, all_cands, head_cols), lambda b, *_: (0, 0, 0))
    tiles = pl.BlockSpec(
        (rows_per_block, head_cols), lambda b, *_: (jnp.minimum(b, _[4][0]), 0)
    )
    partial_value = pl.pallas_call(
        functools.partial(attend_kernel, window=window, heads_here=heads_here, micro=micro),
        grid_spec=pltpu.PrefetchScalarGridSpec(
            num_scalar_prefetch=6,
            grid=(n_blocks,),
            in_specs=[whole, tiles, tiles],
            out_specs=whole,
            scratch_shapes=[
                pltpu.VMEM((USERS * micro * window, head_cols), jnp.bfloat16),
                pltpu.VMEM((USERS * micro * window, head_cols), jnp.float32),
            ],
        ),
        out_shape=jax.ShapeDtypeStruct((micro, all_cands, head_cols), jnp.float32),
        compiler_params=pltpu.CompilerParams(dimension_semantics=("arbitrary",)),
    )(tile_user, tile_rank, hist_len, user_info, last_block, first_rows, queries_all, k_cache, v_cache)

    reduced = reduce_over_hist(partial_value.reshape(micro, n_cand, n_hist, local_rows, head_cols))
    attended = spread_over_cand(reduced)
    attended = attended.reshape(micro * local_rows, model_width)
    average = jnp.mean(attended, axis=-1, keepdims=True)
    centered = attended - average
    spread_sq = jnp.mean(centered * centered, axis=-1, keepdims=True)
    normed = centered * lax.rsqrt(spread_sq + EPSILON)
    mixed_rows = (normed * gate_vals.astype(jnp.float32)).astype(jnp.bfloat16)
    ranked = jnp.dot(
        mixed_rows, out_weight, preferred_element_type=jnp.float32
    ) + cand_rows.astype(jnp.float32)
    return ranked.astype(jnp.bfloat16).reshape(micro, local_rows, model_width)


def solution(mesh):
    return jax.shard_map(
        body,
        mesh=mesh,
        in_specs=(
            P(None, ("cand", "hist"), None),
            P(),
            P(),
            P("hist", "cand"),
            P("hist", "cand"),
            P(),
            P(),
            P("hist"),
            P("hist"),
        ),
        out_specs=P(None, ("cand", "hist"), None),
        check_vma=False,
    )
```

```python
import functools

import jax
import jax.numpy as jnp
from jax import lax
from jax.experimental import pallas as pl
from jax.experimental.pallas import tpu as pltpu
from jax.sharding import PartitionSpec as P

HEAD_DIM = 128
TILE = 128
USERS = 16
MICRO = 2
BLOCK_TILES = 16


EPSILON = 1e-06


def silu_f32(x):
    return 0.5 * x * (1.0 + jnp.tanh(0.5 * x))


def attend_kernel(
    owner_ref, rank_ref, len_ref, count_ref,
    q_ref, k_ref, v_ref, out_ref, user_q, user_acc, user_ref, *, window, heads_here, micro,
):
    block = pl.program_id(0)
    all_cands = q_ref.shape[1]
    row_ids = lax.broadcasted_iota(jnp.int32, (window, 1), 0)
    pad = jnp.zeros((16, out_ref.shape[2]), jnp.float32)

    @pl.when(block == 0)
    def _():
        user_acc[...] = jnp.zeros_like(user_acc)
        for m in range(micro):
            def scan(user, start):
                count = count_ref[m * USERS + user]
                offset = jnp.minimum(start, all_cands - window)
                base_row = jnp.minimum(offset // 16 * 16, all_cands - window - 16)
                entry = (m * USERS + user) * 4
                user_ref[entry] = base_row
                user_ref[entry + 1] = offset - base_row
                user_ref[entry + 2] = start - offset
                user_ref[entry + 3] = start - offset + count
                return start + count

            lax.fori_loop(0, USERS, scan, jnp.int32(0))

        for m in range(micro):
            def fill(user, carry):
                entry = (m * USERS + user) * 4
                span = pl.ds(pl.multiple_of(user_ref[entry], 16), window + 16)
                shift = user_ref[entry + 1]
                rows = q_ref[m, span, :].astype(jnp.float32)
                rows = pltpu.roll(rows, (window + 16 - shift) % (window + 16), 0)
                keep = (row_ids >= user_ref[entry + 2]) & (row_ids < user_ref[entry + 3])
                user_q[pl.ds(pl.multiple_of(user * (micro * window) + m * window, window), window), :] = jnp.where(
                    keep, rows[:window], 0.0
                ).astype(jnp.bfloat16)
                return carry

            lax.fori_loop(0, USERS, fill, 0)

    key_ids = lax.broadcasted_iota(jnp.int32, (TILE, 1), 0)

    def one_tile(j):
        if True:
            slot = block * BLOCK_TILES + j
            user = owner_ref[slot]
            klen = jnp.where(
                user < USERS, len_ref[jnp.minimum(user, USERS - 1)] - rank_ref[slot] * TILE, 0
            )
            rows = slice(j * TILE, (j + 1) * TILE)
            keys = jnp.where(key_ids < klen, k_ref[rows, :], 0)
            values = v_ref[rows, :]
            first_row = jnp.minimum(user, USERS - 1) * (micro * window)
            user_rows = pl.ds(pl.multiple_of(first_row, micro * window), micro * window)
            queries = user_q[user_rows, :]
            if heads_here == 2:
                lanes = lax.broadcasted_iota(jnp.int32, (1, 2 * HEAD_DIM), 1)
                first = lanes < HEAD_DIM

                def diagonal(tile):
                    return jnp.concatenate(
                        [jnp.where(first, tile, 0), jnp.where(first, 0, tile)], axis=0
                    )

                scores = lax.dot_general(
                    queries,
                    diagonal(keys),
                    (((1,), (1,)), ((), ())),
                    preferred_element_type=jnp.float32,
                )
                weights = silu_f32(scores).astype(jnp.bfloat16)
                user_acc[user_rows, :] += jnp.dot(
                    weights, diagonal(values), preferred_element_type=jnp.float32
                )
            else:
                parts = []
                for h in range(heads_here):
                    cols = slice(h * HEAD_DIM, (h + 1) * HEAD_DIM)
                    scores = lax.dot_general(
                        queries[:, cols],
                        keys[:, cols],
                        (((1,), (1,)), ((), ())),
                        preferred_element_type=jnp.float32,
                    )
                    weights = silu_f32(scores).astype(jnp.bfloat16)
                    parts.append(
                        jnp.dot(weights, values[:, cols], preferred_element_type=jnp.float32)
                    )
                user_acc[user_rows, :] += jnp.concatenate(parts, axis=1) if heads_here > 1 else parts[0]


    occupied = owner_ref[block * BLOCK_TILES]
    for j in range(1, BLOCK_TILES):
        occupied = jnp.minimum(occupied, owner_ref[block * BLOCK_TILES + j])

    @pl.when(occupied < USERS)
    def _():
        for j in range(BLOCK_TILES):
            one_tile(j)

    @pl.when(block == pl.num_programs(0) - 1)
    def _():
        out_ref[...] = jnp.zeros_like(out_ref)
        for m in range(micro):
            def place(user, carry):
                entry = (m * USERS + user) * 4
                span = pl.ds(pl.multiple_of(user_ref[entry], 16), window + 16)
                first = pl.multiple_of(user * (micro * window) + m * window, window)
                sums = jnp.concatenate([user_acc[pl.ds(first, window), :], pad])
                out_ref[m, span, :] += pltpu.roll(sums, user_ref[entry + 1], 0)
                return carry

            lax.fori_loop(0, USERS, place, 0)


def reduce_over_hist(partial):
    micro, n_cand, n_hist, rows, cols = partial.shape
    chips = n_hist // 2
    me = lax.axis_index("hist")
    chip, core = me // 2, me % 2
    halves = partial.reshape(micro, n_cand, chips, 2, rows, cols)
    mine = lax.dynamic_index_in_dim(halves, core, axis=3, keepdims=False)
    theirs = lax.dynamic_index_in_dim(halves, 1 - core, axis=3, keepdims=False)
    swapped = lax.ppermute(
        theirs.astype(jnp.bfloat16), "hist", perm=[(i, i ^ 1) for i in range(n_hist)]
    )
    chip_sums = mine + swapped.astype(jnp.float32)

    def block_of(index):
        index = jnp.clip(index, 0, chips - 1)
        return lax.dynamic_index_in_dim(chip_sums, index, axis=2, keepdims=False)

    total = block_of(chip)
    for shift in range(1, chips):
        send = block_of((chip + shift) % chips).astype(jnp.bfloat16)
        perm = [(2 * c + k, 2 * ((c + shift) % chips) + k) for c in range(chips) for k in range(2)]
        total = total + lax.ppermute(send, "hist", perm=perm).astype(jnp.float32)
    return total


def gather_queries(queries, n_cand, n_hist):
    micro, rows, width = queries.shape
    group = width // n_cand
    me_cand = lax.axis_index("cand")
    chunks = queries.reshape(micro, rows, n_cand, group)
    received = []
    for shift in range(n_cand):
        target = (me_cand + shift) % n_cand
        piece = lax.dynamic_index_in_dim(chunks, target, axis=2, keepdims=False)
        if shift:
            piece = lax.ppermute(
                piece, "cand", perm=[(i, (i + shift) % n_cand) for i in range(n_cand)]
            )
        received.append(piece)
    by_offset = jnp.stack(received)
    sources = jnp.stack(
        [
            lax.dynamic_index_in_dim(by_offset, (me_cand - c) % n_cand, axis=0, keepdims=False)
            for c in range(n_cand)
        ]
    )
    chips = n_hist // 2
    me = lax.axis_index("hist")
    chip, core = me // 2, me % 2
    by_offset = [sources]
    for shift in range(1, chips):
        perm = [(2 * c + k, 2 * ((c + shift) % chips) + k) for c in range(chips) for k in range(2)]
        by_offset.append(lax.ppermute(sources, "hist", perm=perm))
    by_offset = jnp.stack(by_offset)
    mine = jnp.stack(
        [
            lax.dynamic_index_in_dim(by_offset, (chip - c) % chips, axis=0, keepdims=False)
            for c in range(chips)
        ]
    )
    theirs = lax.ppermute(mine, "hist", perm=[(i, i ^ 1) for i in range(n_hist)])
    both = jnp.where(core == 0, jnp.stack([mine, theirs], axis=1), jnp.stack([theirs, mine], axis=1))
    both = both.reshape(n_hist, n_cand, micro, rows, group)
    return jnp.transpose(both, (2, 1, 0, 3, 4)).reshape(micro, n_cand * n_hist * rows, group)


def spread_over_cand(reduced):
    micro, n_cand, rows, group = reduced.shape
    me = lax.axis_index("cand")
    received = []
    for shift in range(n_cand):
        piece = lax.dynamic_index_in_dim(reduced, (me + shift) % n_cand, axis=1, keepdims=False)
        if shift:
            piece = lax.ppermute(
                piece, "cand", perm=[(i, (i + shift) % n_cand) for i in range(n_cand)]
            )
        received.append(piece)
    by_offset = jnp.stack(received)
    return jnp.concatenate(
        [
            lax.dynamic_index_in_dim(by_offset, (me - c) % n_cand, axis=0, keepdims=False)
            for c in range(n_cand)
        ],
        axis=-1,
    )


def body(
    cand_x, qu_weight, out_weight, k_cache, v_cache, hist_len, cand_count, tile_user, tile_rank
):
    n_cand = lax.axis_size("cand")
    n_hist = lax.axis_size("hist")
    micro, local_rows, model_width = cand_x.shape
    head_cols = k_cache.shape[1]
    heads_here = head_cols // HEAD_DIM
    tiles_here = k_cache.shape[0] // TILE

    cand_rows = cand_x.reshape(micro * local_rows, model_width)
    queries = jax.nn.silu(
        jnp.dot(cand_rows, qu_weight[:, :model_width], preferred_element_type=jnp.float32)
    )
    queries = queries.astype(jnp.bfloat16).reshape(micro, local_rows, model_width)
    gate_vals = jax.nn.silu(
        jnp.dot(cand_rows, qu_weight[:, model_width:], preferred_element_type=jnp.float32)
    ).astype(jnp.bfloat16)
    queries_all = gather_queries(queries, n_cand, n_hist)
    all_cands = queries_all.shape[1]
    window = 2 * all_cands // USERS

    rows_per_block = BLOCK_TILES * TILE
    n_blocks = tiles_here // BLOCK_TILES
    whole = pl.BlockSpec((micro, all_cands, head_cols), lambda b, *_: (0, 0, 0))
    tiles = pl.BlockSpec(
        (rows_per_block, head_cols), lambda b, *_: (b, 0)
    )
    partial_value = pl.pallas_call(
        functools.partial(attend_kernel, window=window, heads_here=heads_here, micro=micro),
        grid_spec=pltpu.PrefetchScalarGridSpec(
            num_scalar_prefetch=4,
            grid=(n_blocks,),
            in_specs=[whole, tiles, tiles],
            out_specs=whole,
            scratch_shapes=[
                pltpu.VMEM((USERS * micro * window, head_cols), jnp.bfloat16),
                pltpu.VMEM((USERS * micro * window, head_cols), jnp.float32),
                pltpu.SMEM((micro * USERS * 4,), jnp.int32),
            ],
        ),
        out_shape=jax.ShapeDtypeStruct((micro, all_cands, head_cols), jnp.float32),
        compiler_params=pltpu.CompilerParams(dimension_semantics=("arbitrary",)),
    )(tile_user, tile_rank, hist_len, cand_count.reshape(-1), queries_all, k_cache, v_cache)

    reduced = reduce_over_hist(partial_value.reshape(micro, n_cand, n_hist, local_rows, head_cols))
    attended = spread_over_cand(reduced)
    attended = attended.reshape(micro * local_rows, model_width)
    average = jnp.mean(attended, axis=-1, keepdims=True)
    centered = attended - average
    spread_sq = jnp.mean(centered * centered, axis=-1, keepdims=True)
    normed = centered * lax.rsqrt(spread_sq + EPSILON)
    mixed_rows = (normed * gate_vals.astype(jnp.float32)).astype(jnp.bfloat16)
    ranked = jnp.dot(
        mixed_rows, out_weight, preferred_element_type=jnp.float32
    ) + cand_rows.astype(jnp.float32)
    return ranked.astype(jnp.bfloat16).reshape(micro, local_rows, model_width)


def solution(mesh):
    return jax.shard_map(
        body,
        mesh=mesh,
        in_specs=(
            P(None, ("cand", "hist"), None),
            P(),
            P(),
            P("hist", "cand"),
            P("hist", "cand"),
            P(),
            P(),
            P("hist"),
            P("hist"),
        ),
        out_specs=P(None, ("cand", "hist"), None),
        check_vma=False,
    )
```

```python
import functools

import jax
import jax.numpy as jnp
from jax import lax
from jax.experimental import pallas as pl
from jax.experimental.pallas import tpu as pltpu
from jax.sharding import PartitionSpec as P

HEAD_DIM = 128
TILE = 128
USERS = 16
MICRO = 2
BLOCK_TILES = 16


EPSILON = 1e-06


def silu_f32(x):
    half = 0.5 * x
    return half + half * jnp.tanh(half)


def attend_kernel(
    owner_ref, rank_ref, len_ref, count_ref,
    q_ref, k_ref, v_ref, out_ref, user_q, user_acc, user_ref, *, window, heads_here, micro,
):
    block = pl.program_id(0)
    all_cands = q_ref.shape[1]
    row_ids = lax.broadcasted_iota(jnp.int32, (window, 1), 0)
    pad = jnp.zeros((16, out_ref.shape[2]), jnp.float32)

    @pl.when(block == 0)
    def _():
        user_acc[...] = jnp.zeros_like(user_acc)
        for m in range(micro):
            def scan(user, start):
                count = count_ref[m * USERS + user]
                offset = jnp.minimum(start, all_cands - window)
                base_row = jnp.minimum(offset // 16 * 16, all_cands - window - 16)
                entry = (m * USERS + user) * 4
                user_ref[entry] = base_row
                user_ref[entry + 1] = offset - base_row
                user_ref[entry + 2] = start - offset
                user_ref[entry + 3] = start - offset + count
                return start + count

            lax.fori_loop(0, USERS, scan, jnp.int32(0))

        for m in range(micro):
            def fill(user, carry):
                entry = (m * USERS + user) * 4
                span = pl.ds(pl.multiple_of(user_ref[entry], 16), window + 16)
                shift = user_ref[entry + 1]
                rows = q_ref[m, span, :].astype(jnp.float32)
                rows = pltpu.roll(rows, (window + 16 - shift) % (window + 16), 0)
                keep = (row_ids >= user_ref[entry + 2]) & (row_ids < user_ref[entry + 3])
                user_q[pl.ds(pl.multiple_of(user * (micro * window) + m * window, window), window), :] = jnp.where(
                    keep, rows[:window], 0.0
                ).astype(jnp.bfloat16)
                return carry

            lax.fori_loop(0, USERS, fill, 0)

    key_ids = lax.broadcasted_iota(jnp.int32, (TILE, 1), 0)

    def one_tile(j):
        if True:
            slot = block * BLOCK_TILES + j
            user = owner_ref[slot]
            klen = jnp.where(
                user < USERS, len_ref[jnp.minimum(user, USERS - 1)] - rank_ref[slot] * TILE, 0
            )
            rows = slice(j * TILE, (j + 1) * TILE)
            keys = jnp.where(key_ids < klen, k_ref[rows, :], 0)
            values = v_ref[rows, :]
            first_row = jnp.minimum(user, USERS - 1) * (micro * window)
            user_rows = pl.ds(pl.multiple_of(first_row, micro * window), micro * window)
            queries = user_q[user_rows, :]
            if heads_here == 2:
                lanes = lax.broadcasted_iota(jnp.int32, (1, 2 * HEAD_DIM), 1)
                first = lanes < HEAD_DIM

                def diagonal(tile):
                    return jnp.concatenate(
                        [jnp.where(first, tile, 0), jnp.where(first, 0, tile)], axis=0
                    )

                scores = lax.dot_general(
                    queries,
                    diagonal(keys),
                    (((1,), (1,)), ((), ())),
                    preferred_element_type=jnp.float32,
                )
                weights = silu_f32(scores).astype(jnp.bfloat16)
                user_acc[user_rows, :] += jnp.dot(
                    weights, diagonal(values), preferred_element_type=jnp.float32
                )
            else:
                parts = []
                for h in range(heads_here):
                    cols = slice(h * HEAD_DIM, (h + 1) * HEAD_DIM)
                    scores = lax.dot_general(
                        queries[:, cols],
                        keys[:, cols],
                        (((1,), (1,)), ((), ())),
                        preferred_element_type=jnp.float32,
                    )
                    weights = silu_f32(scores).astype(jnp.bfloat16)
                    parts.append(
                        jnp.dot(weights, values[:, cols], preferred_element_type=jnp.float32)
                    )
                user_acc[user_rows, :] += jnp.concatenate(parts, axis=1) if heads_here > 1 else parts[0]


    occupied = owner_ref[block * BLOCK_TILES]
    for j in range(1, BLOCK_TILES):
        occupied = jnp.minimum(occupied, owner_ref[block * BLOCK_TILES + j])

    @pl.when(occupied < USERS)
    def _():
        for j in range(BLOCK_TILES):
            one_tile(j)

    @pl.when(block == pl.num_programs(0) - 1)
    def _():
        out_ref[...] = jnp.zeros_like(out_ref)
        for m in range(micro):
            def place(user, carry):
                entry = (m * USERS + user) * 4
                span = pl.ds(pl.multiple_of(user_ref[entry], 16), window + 16)
                first = pl.multiple_of(user * (micro * window) + m * window, window)
                sums = jnp.concatenate([user_acc[pl.ds(first, window), :], pad])
                out_ref[m, span, :] += pltpu.roll(sums, user_ref[entry + 1], 0)
                return carry

            lax.fori_loop(0, USERS, place, 0)


def reduce_over_hist(partial):
    micro, n_cand, n_hist, rows, cols = partial.shape
    chips = n_hist // 2
    me = lax.axis_index("hist")
    chip, core = me // 2, me % 2
    halves = partial.reshape(micro, n_cand, chips, 2, rows, cols)
    mine = lax.dynamic_index_in_dim(halves, core, axis=3, keepdims=False)
    theirs = lax.dynamic_index_in_dim(halves, 1 - core, axis=3, keepdims=False)
    swapped = lax.ppermute(
        theirs.astype(jnp.bfloat16), "hist", perm=[(i, i ^ 1) for i in range(n_hist)]
    )
    chip_sums = mine + swapped.astype(jnp.float32)

    def block_of(index):
        index = jnp.clip(index, 0, chips - 1)
        return lax.dynamic_index_in_dim(chip_sums, index, axis=2, keepdims=False)

    total = block_of(chip)
    for shift in range(1, chips):
        send = block_of((chip + shift) % chips).astype(jnp.bfloat16)
        perm = [(2 * c + k, 2 * ((c + shift) % chips) + k) for c in range(chips) for k in range(2)]
        total = total + lax.ppermute(send, "hist", perm=perm).astype(jnp.float32)
    return total


def gather_queries(queries, n_cand, n_hist):
    micro, rows, width = queries.shape
    group = width // n_cand
    me_cand = lax.axis_index("cand")
    chunks = queries.reshape(micro, rows, n_cand, group)
    received = []
    for shift in range(n_cand):
        target = (me_cand + shift) % n_cand
        piece = lax.dynamic_index_in_dim(chunks, target, axis=2, keepdims=False)
        if shift:
            piece = lax.ppermute(
                piece, "cand", perm=[(i, (i + shift) % n_cand) for i in range(n_cand)]
            )
        received.append(piece)
    by_offset = jnp.stack(received)
    sources = jnp.stack(
        [
            lax.dynamic_index_in_dim(by_offset, (me_cand - c) % n_cand, axis=0, keepdims=False)
            for c in range(n_cand)
        ]
    )
    chips = n_hist // 2
    me = lax.axis_index("hist")
    chip, core = me // 2, me % 2
    by_offset = [sources]
    for shift in range(1, chips):
        perm = [(2 * c + k, 2 * ((c + shift) % chips) + k) for c in range(chips) for k in range(2)]
        by_offset.append(lax.ppermute(sources, "hist", perm=perm))
    by_offset = jnp.stack(by_offset)
    mine = jnp.stack(
        [
            lax.dynamic_index_in_dim(by_offset, (chip - c) % chips, axis=0, keepdims=False)
            for c in range(chips)
        ]
    )
    theirs = lax.ppermute(mine, "hist", perm=[(i, i ^ 1) for i in range(n_hist)])
    both = jnp.where(core == 0, jnp.stack([mine, theirs], axis=1), jnp.stack([theirs, mine], axis=1))
    both = both.reshape(n_hist, n_cand, micro, rows, group)
    return jnp.transpose(both, (2, 1, 0, 3, 4)).reshape(micro, n_cand * n_hist * rows, group)


def spread_over_cand(reduced):
    micro, n_cand, rows, group = reduced.shape
    me = lax.axis_index("cand")
    received = []
    for shift in range(n_cand):
        piece = lax.dynamic_index_in_dim(reduced, (me + shift) % n_cand, axis=1, keepdims=False)
        if shift:
            piece = lax.ppermute(
                piece, "cand", perm=[(i, (i + shift) % n_cand) for i in range(n_cand)]
            )
        received.append(piece)
    by_offset = jnp.stack(received)
    return jnp.concatenate(
        [
            lax.dynamic_index_in_dim(by_offset, (me - c) % n_cand, axis=0, keepdims=False)
            for c in range(n_cand)
        ],
        axis=-1,
    )


def body(
    cand_x, qu_weight, out_weight, k_cache, v_cache, hist_len, cand_count, tile_user, tile_rank
):
    n_cand = lax.axis_size("cand")
    n_hist = lax.axis_size("hist")
    micro, local_rows, model_width = cand_x.shape
    head_cols = k_cache.shape[1]
    heads_here = head_cols // HEAD_DIM
    tiles_here = k_cache.shape[0] // TILE

    cand_rows = cand_x.reshape(micro * local_rows, model_width)
    queries = jax.nn.silu(
        jnp.dot(cand_rows, qu_weight[:, :model_width], preferred_element_type=jnp.float32)
    )
    queries = queries.astype(jnp.bfloat16).reshape(micro, local_rows, model_width)
    gate_vals = jax.nn.silu(
        jnp.dot(cand_rows, qu_weight[:, model_width:], preferred_element_type=jnp.float32)
    ).astype(jnp.bfloat16)
    queries_all = gather_queries(queries, n_cand, n_hist)
    all_cands = queries_all.shape[1]
    window = 2 * all_cands // USERS

    rows_per_block = BLOCK_TILES * TILE
    n_blocks = tiles_here // BLOCK_TILES
    whole = pl.BlockSpec((micro, all_cands, head_cols), lambda b, *_: (0, 0, 0))
    tiles = pl.BlockSpec(
        (rows_per_block, head_cols),
        lambda b, owner, *_: (jnp.where(owner[b * BLOCK_TILES] < USERS, b, 0), 0),
    )
    partial_value = pl.pallas_call(
        functools.partial(attend_kernel, window=window, heads_here=heads_here, micro=micro),
        grid_spec=pltpu.PrefetchScalarGridSpec(
            num_scalar_prefetch=4,
            grid=(n_blocks,),
            in_specs=[whole, tiles, tiles],
            out_specs=whole,
            scratch_shapes=[
                pltpu.VMEM((USERS * micro * window, head_cols), jnp.bfloat16),
                pltpu.VMEM((USERS * micro * window, head_cols), jnp.float32),
                pltpu.SMEM((micro * USERS * 4,), jnp.int32),
            ],
        ),
        out_shape=jax.ShapeDtypeStruct((micro, all_cands, head_cols), jnp.float32),
        compiler_params=pltpu.CompilerParams(dimension_semantics=("arbitrary",)),
    )(tile_user, tile_rank, hist_len, cand_count.reshape(-1), queries_all, k_cache, v_cache)

    reduced = reduce_over_hist(partial_value.reshape(micro, n_cand, n_hist, local_rows, head_cols))
    attended = spread_over_cand(reduced)
    attended = attended.reshape(micro * local_rows, model_width)
    average = jnp.mean(attended, axis=-1, keepdims=True)
    centered = attended - average
    spread_sq = jnp.mean(centered * centered, axis=-1, keepdims=True)
    normed = centered * lax.rsqrt(spread_sq + EPSILON)
    mixed_rows = (normed * gate_vals.astype(jnp.float32)).astype(jnp.bfloat16)
    ranked = jnp.dot(
        mixed_rows, out_weight, preferred_element_type=jnp.float32
    ) + cand_rows.astype(jnp.float32)
    return ranked.astype(jnp.bfloat16).reshape(micro, local_rows, model_width)


def solution(mesh):
    return jax.shard_map(
        body,
        mesh=mesh,
        in_specs=(
            P(None, ("cand", "hist"), None),
            P(),
            P(),
            P("hist", "cand"),
            P("hist", "cand"),
            P(),
            P(),
            P("hist"),
            P("hist"),
        ),
        out_specs=P(None, ("cand", "hist"), None),
        check_vma=False,
    )
```

```python
import functools

import jax
import jax.numpy as jnp
from jax import lax
from jax.experimental import pallas as pl
from jax.experimental.pallas import tpu as pltpu
from jax.sharding import PartitionSpec as P

HEAD_DIM = 128
TILE = 128
USERS = 16
MICRO = 2
BLOCK_TILES = 16


EPSILON = 1e-06


def silu_f32(x):
    half = 0.5 * x
    return half + half * jnp.tanh(half)


def attend_kernel(
    owner_ref, rank_ref, len_ref, count_ref,
    q_ref, k_ref, v_ref, out_ref, user_q, user_acc, user_ref, *, window, heads_here, micro,
):
    block = pl.program_id(0)
    all_cands = q_ref.shape[1]
    row_ids = lax.broadcasted_iota(jnp.int32, (window, 1), 0)
    pad = jnp.zeros((16, out_ref.shape[2]), jnp.float32)

    @pl.when(block == 0)
    def _():
        user_acc[...] = jnp.zeros_like(user_acc)
        for m in range(micro):
            def scan(user, start):
                count = count_ref[m * USERS + user]
                offset = jnp.minimum(start, all_cands - window)
                base_row = jnp.minimum(offset // 16 * 16, all_cands - window - 16)
                entry = (m * USERS + user) * 4
                user_ref[entry] = base_row
                user_ref[entry + 1] = offset - base_row
                user_ref[entry + 2] = start - offset
                user_ref[entry + 3] = start - offset + count
                return start + count

            lax.fori_loop(0, USERS, scan, jnp.int32(0))

        for m in range(micro):
            def fill(user, carry):
                entry = (m * USERS + user) * 4
                span = pl.ds(pl.multiple_of(user_ref[entry], 16), window + 16)
                shift = user_ref[entry + 1]
                rows = q_ref[m, span, :].astype(jnp.float32)
                rows = pltpu.roll(rows, (window + 16 - shift) % (window + 16), 0)
                keep = (row_ids >= user_ref[entry + 2]) & (row_ids < user_ref[entry + 3])
                user_q[pl.ds(pl.multiple_of(user * (micro * window) + m * window, window), window), :] = jnp.where(
                    keep, rows[:window], 0.0
                ).astype(jnp.bfloat16)
                return carry

            lax.fori_loop(0, USERS, fill, 0)

    key_ids = lax.broadcasted_iota(jnp.int32, (TILE, 1), 0)

    def one_tile(j):
        if True:
            slot = block * BLOCK_TILES + j
            user = owner_ref[slot]
            klen = jnp.where(
                user < USERS, len_ref[jnp.minimum(user, USERS - 1)] - rank_ref[slot] * TILE, 0
            )
            rows = slice(j * TILE, (j + 1) * TILE)
            keys = jnp.where(key_ids < klen, k_ref[rows, :], 0)
            values = v_ref[rows, :]
            first_row = jnp.minimum(user, USERS - 1) * (micro * window)
            user_rows = pl.ds(pl.multiple_of(first_row, micro * window), micro * window)
            queries = user_q[user_rows, :]
            if heads_here == 2:
                lanes = lax.broadcasted_iota(jnp.int32, (1, 2 * HEAD_DIM), 1)
                first = lanes < HEAD_DIM

                def diagonal(tile):
                    return jnp.concatenate(
                        [jnp.where(first, tile, 0), jnp.where(first, 0, tile)], axis=0
                    )

                scores = lax.dot_general(
                    queries,
                    diagonal(keys),
                    (((1,), (1,)), ((), ())),
                    preferred_element_type=jnp.float32,
                )
                weights = silu_f32(scores).astype(jnp.bfloat16)
                user_acc[user_rows, :] += jnp.dot(
                    weights, diagonal(values), preferred_element_type=jnp.float32
                )
            else:
                parts = []
                for h in range(heads_here):
                    cols = slice(h * HEAD_DIM, (h + 1) * HEAD_DIM)
                    scores = lax.dot_general(
                        queries[:, cols],
                        keys[:, cols],
                        (((1,), (1,)), ((), ())),
                        preferred_element_type=jnp.float32,
                    )
                    weights = silu_f32(scores).astype(jnp.bfloat16)
                    parts.append(
                        jnp.dot(weights, values[:, cols], preferred_element_type=jnp.float32)
                    )
                user_acc[user_rows, :] += jnp.concatenate(parts, axis=1) if heads_here > 1 else parts[0]


    occupied = owner_ref[block * BLOCK_TILES]
    for j in range(1, BLOCK_TILES):
        occupied = jnp.minimum(occupied, owner_ref[block * BLOCK_TILES + j])

    @pl.when(occupied < USERS)
    def _():
        for j in range(BLOCK_TILES):
            one_tile(j)

    @pl.when(block == pl.num_programs(0) - 1)
    def _():
        out_ref[...] = jnp.zeros_like(out_ref)
        for m in range(micro):
            def place(user, carry):
                entry = (m * USERS + user) * 4
                span = pl.ds(pl.multiple_of(user_ref[entry], 16), window + 16)
                first = pl.multiple_of(user * (micro * window) + m * window, window)
                sums = jnp.concatenate([user_acc[pl.ds(first, window), :], pad])
                out_ref[m, span, :] += pltpu.roll(sums, user_ref[entry + 1], 0)
                return carry

            lax.fori_loop(0, USERS, place, 0)


def reduce_over_hist(partial):
    micro, n_cand, n_hist, rows, cols = partial.shape
    chips = n_hist // 2
    me = lax.axis_index("hist")
    chip, core = me // 2, me % 2
    halves = partial.reshape(micro, n_cand, chips, 2, rows, cols)
    mine = lax.dynamic_index_in_dim(halves, core, axis=3, keepdims=False)
    theirs = lax.dynamic_index_in_dim(halves, 1 - core, axis=3, keepdims=False)
    swapped = lax.ppermute(
        theirs.astype(jnp.bfloat16), "hist", perm=[(i, i ^ 1) for i in range(n_hist)]
    )
    chip_sums = mine + swapped.astype(jnp.float32)

    def block_of(index):
        index = jnp.clip(index, 0, chips - 1)
        return lax.dynamic_index_in_dim(chip_sums, index, axis=2, keepdims=False)

    total = block_of(chip)
    for shift in range(1, chips):
        send = block_of((chip + shift) % chips).astype(jnp.bfloat16)
        perm = [(2 * c + k, 2 * ((c + shift) % chips) + k) for c in range(chips) for k in range(2)]
        total = total + lax.ppermute(send, "hist", perm=perm).astype(jnp.float32)
    return total


def gather_queries(queries, n_cand, n_hist):
    micro, rows, width = queries.shape
    group = width // n_cand
    me_cand = lax.axis_index("cand")
    chunks = queries.reshape(micro, rows, n_cand, group)
    received = []
    for shift in range(n_cand):
        target = (me_cand + shift) % n_cand
        piece = lax.dynamic_index_in_dim(chunks, target, axis=2, keepdims=False)
        if shift:
            piece = lax.ppermute(
                piece, "cand", perm=[(i, (i + shift) % n_cand) for i in range(n_cand)]
            )
        received.append(piece)
    by_offset = jnp.stack(received)
    sources = jnp.stack(
        [
            lax.dynamic_index_in_dim(by_offset, (me_cand - c) % n_cand, axis=0, keepdims=False)
            for c in range(n_cand)
        ],
        axis=1,
    )
    chips = n_hist // 2
    me = lax.axis_index("hist")
    chip, core = me // 2, me % 2
    by_offset = [sources]
    for shift in range(1, chips):
        perm = [(2 * c + k, 2 * ((c + shift) % chips) + k) for c in range(chips) for k in range(2)]
        by_offset.append(lax.ppermute(sources, "hist", perm=perm))
    by_offset = jnp.stack(by_offset)
    mine = jnp.stack(
        [
            lax.dynamic_index_in_dim(by_offset, (chip - c) % chips, axis=0, keepdims=False)
            for c in range(chips)
        ],
        axis=2,
    )
    theirs = lax.ppermute(mine, "hist", perm=[(i, i ^ 1) for i in range(n_hist)])
    both = jnp.where(core == 0, jnp.stack([mine, theirs], axis=3), jnp.stack([theirs, mine], axis=3))
    return both.reshape(micro, n_cand * n_hist * rows, group)


def spread_over_cand(reduced):
    micro, n_cand, rows, group = reduced.shape
    me = lax.axis_index("cand")
    received = []
    for shift in range(n_cand):
        piece = lax.dynamic_index_in_dim(reduced, (me + shift) % n_cand, axis=1, keepdims=False)
        if shift:
            piece = lax.ppermute(
                piece, "cand", perm=[(i, (i + shift) % n_cand) for i in range(n_cand)]
            )
        received.append(piece)
    by_offset = jnp.stack(received)
    return jnp.concatenate(
        [
            lax.dynamic_index_in_dim(by_offset, (me - c) % n_cand, axis=0, keepdims=False)
            for c in range(n_cand)
        ],
        axis=-1,
    )


def body(
    cand_x, qu_weight, out_weight, k_cache, v_cache, hist_len, cand_count, tile_user, tile_rank
):
    n_cand = lax.axis_size("cand")
    n_hist = lax.axis_size("hist")
    micro, local_rows, model_width = cand_x.shape
    head_cols = k_cache.shape[1]
    heads_here = head_cols // HEAD_DIM
    tiles_here = k_cache.shape[0] // TILE

    cand_rows = cand_x.reshape(micro * local_rows, model_width)
    queries = jax.nn.silu(
        jnp.dot(cand_rows, qu_weight[:, :model_width], preferred_element_type=jnp.float32)
    )
    queries = queries.astype(jnp.bfloat16).reshape(micro, local_rows, model_width)
    gate_vals = jax.nn.silu(
        jnp.dot(cand_rows, qu_weight[:, model_width:], preferred_element_type=jnp.float32)
    ).astype(jnp.bfloat16)
    queries_all = gather_queries(queries, n_cand, n_hist)
    all_cands = queries_all.shape[1]
    window = 2 * all_cands // USERS

    rows_per_block = BLOCK_TILES * TILE
    n_blocks = tiles_here // BLOCK_TILES
    whole = pl.BlockSpec((micro, all_cands, head_cols), lambda b, *_: (0, 0, 0))
    tiles = pl.BlockSpec(
        (rows_per_block, head_cols),
        lambda b, owner, *_: (jnp.where(owner[b * BLOCK_TILES] < USERS, b, 0), 0),
    )
    partial_value = pl.pallas_call(
        functools.partial(attend_kernel, window=window, heads_here=heads_here, micro=micro),
        grid_spec=pltpu.PrefetchScalarGridSpec(
            num_scalar_prefetch=4,
            grid=(n_blocks,),
            in_specs=[whole, tiles, tiles],
            out_specs=whole,
            scratch_shapes=[
                pltpu.VMEM((USERS * micro * window, head_cols), jnp.bfloat16),
                pltpu.VMEM((USERS * micro * window, head_cols), jnp.float32),
                pltpu.SMEM((micro * USERS * 4,), jnp.int32),
            ],
        ),
        out_shape=jax.ShapeDtypeStruct((micro, all_cands, head_cols), jnp.float32),
        compiler_params=pltpu.CompilerParams(dimension_semantics=("arbitrary",)),
    )(tile_user, tile_rank, hist_len, cand_count.reshape(-1), queries_all, k_cache, v_cache)

    reduced = reduce_over_hist(partial_value.reshape(micro, n_cand, n_hist, local_rows, head_cols))
    attended = spread_over_cand(reduced)
    attended = attended.reshape(micro * local_rows, model_width)
    average = jnp.mean(attended, axis=-1, keepdims=True)
    centered = attended - average
    spread_sq = jnp.mean(centered * centered, axis=-1, keepdims=True)
    normed = centered * lax.rsqrt(spread_sq + EPSILON)
    mixed_rows = (normed * gate_vals.astype(jnp.float32)).astype(jnp.bfloat16)
    ranked = jnp.dot(
        mixed_rows, out_weight, preferred_element_type=jnp.float32
    ) + cand_rows.astype(jnp.float32)
    return ranked.astype(jnp.bfloat16).reshape(micro, local_rows, model_width)


def solution(mesh):
    return jax.shard_map(
        body,
        mesh=mesh,
        in_specs=(
            P(None, ("cand", "hist"), None),
            P(),
            P(),
            P("hist", "cand"),
            P("hist", "cand"),
            P(),
            P(),
            P("hist"),
            P("hist"),
        ),
        out_specs=P(None, ("cand", "hist"), None),
        check_vma=False,
    )
```

```python
import functools

import jax
import jax.numpy as jnp
from jax import lax
from jax.experimental import pallas as pl
from jax.experimental.pallas import tpu as pltpu
from jax.sharding import PartitionSpec as P

HEAD_DIM = 128
TILE = 128
USERS = 16
MICRO = 2
BLOCK_TILES = 32


EPSILON = 1e-06


def silu_f32(x):
    return 0.5 * x * (1.0 + jnp.tanh(0.5 * x))


def attend_kernel(
    owner_ref, rank_ref, len_ref, count_ref,
    q_ref, k_ref, v_ref, out_ref, user_q, user_acc, user_ref, *, window, heads_here, micro,
):
    block = pl.program_id(0)
    all_cands = q_ref.shape[1]
    row_ids = lax.broadcasted_iota(jnp.int32, (window, 1), 0)
    pad = jnp.zeros((16, out_ref.shape[2]), jnp.float32)

    @pl.when(block == 0)
    def _():
        user_acc[...] = jnp.zeros_like(user_acc)
        for m in range(micro):
            def scan(user, start):
                count = count_ref[m * USERS + user]
                offset = jnp.minimum(start, all_cands - window)
                base_row = jnp.minimum(offset // 16 * 16, all_cands - window - 16)
                entry = (m * USERS + user) * 4
                user_ref[entry] = base_row
                user_ref[entry + 1] = offset - base_row
                user_ref[entry + 2] = start - offset
                user_ref[entry + 3] = start - offset + count
                return start + count

            lax.fori_loop(0, USERS, scan, jnp.int32(0))

        for m in range(micro):
            def fill(user, carry):
                entry = (m * USERS + user) * 4
                span = pl.ds(pl.multiple_of(user_ref[entry], 16), window + 16)
                shift = user_ref[entry + 1]
                rows = q_ref[m, span, :].astype(jnp.float32)
                rows = pltpu.roll(rows, (window + 16 - shift) % (window + 16), 0)
                keep = (row_ids >= user_ref[entry + 2]) & (row_ids < user_ref[entry + 3])
                user_q[pl.ds(pl.multiple_of(user * (micro * window) + m * window, window), window), :] = jnp.where(
                    keep, rows[:window], 0.0
                ).astype(jnp.bfloat16)
                return carry

            lax.fori_loop(0, USERS, fill, 0)

    key_ids = lax.broadcasted_iota(jnp.int32, (TILE, 1), 0)

    def one_tile(j):
        if True:
            slot = block * BLOCK_TILES + j
            user = owner_ref[slot]
            klen = jnp.where(
                user < USERS, len_ref[jnp.minimum(user, USERS - 1)] - rank_ref[slot] * TILE, 0
            )
            rows = slice(j * TILE, (j + 1) * TILE)
            keys = jnp.where(key_ids < klen, k_ref[rows, :], 0)
            values = v_ref[rows, :]
            first_row = jnp.minimum(user, USERS - 1) * (micro * window)
            user_rows = pl.ds(pl.multiple_of(first_row, micro * window), micro * window)
            queries = user_q[user_rows, :]
            if heads_here == 2:
                lanes = lax.broadcasted_iota(jnp.int32, (1, 2 * HEAD_DIM), 1)
                first = lanes < HEAD_DIM

                def diagonal(tile):
                    return jnp.concatenate(
                        [jnp.where(first, tile, 0), jnp.where(first, 0, tile)], axis=0
                    )

                scores = lax.dot_general(
                    queries,
                    diagonal(keys),
                    (((1,), (1,)), ((), ())),
                    preferred_element_type=jnp.float32,
                )
                weights = silu_f32(scores).astype(jnp.bfloat16)
                user_acc[user_rows, :] += jnp.dot(
                    weights, diagonal(values), preferred_element_type=jnp.float32
                )
            else:
                parts = []
                for h in range(heads_here):
                    cols = slice(h * HEAD_DIM, (h + 1) * HEAD_DIM)
                    scores = lax.dot_general(
                        queries[:, cols],
                        keys[:, cols],
                        (((1,), (1,)), ((), ())),
                        preferred_element_type=jnp.float32,
                    )
                    weights = silu_f32(scores).astype(jnp.bfloat16)
                    parts.append(
                        jnp.dot(weights, values[:, cols], preferred_element_type=jnp.float32)
                    )
                user_acc[user_rows, :] += jnp.concatenate(parts, axis=1) if heads_here > 1 else parts[0]


    occupied = owner_ref[block * BLOCK_TILES]
    for j in range(1, BLOCK_TILES):
        occupied = jnp.minimum(occupied, owner_ref[block * BLOCK_TILES + j])

    @pl.when(occupied < USERS)
    def _():
        for j in range(BLOCK_TILES):
            one_tile(j)

    @pl.when(block == pl.num_programs(0) - 1)
    def _():
        out_ref[...] = jnp.zeros_like(out_ref)
        for m in range(micro):
            def place(user, carry):
                entry = (m * USERS + user) * 4
                span = pl.ds(pl.multiple_of(user_ref[entry], 16), window + 16)
                first = pl.multiple_of(user * (micro * window) + m * window, window)
                sums = jnp.concatenate([user_acc[pl.ds(first, window), :], pad])
                out_ref[m, span, :] += pltpu.roll(sums, user_ref[entry + 1], 0)
                return carry

            lax.fori_loop(0, USERS, place, 0)


def reduce_over_hist(partial):
    micro, n_cand, n_hist, rows, cols = partial.shape
    chips = n_hist // 2
    me = lax.axis_index("hist")
    chip, core = me // 2, me % 2
    halves = partial.reshape(micro, n_cand, chips, 2, rows, cols)
    mine = lax.dynamic_index_in_dim(halves, core, axis=3, keepdims=False)
    theirs = lax.dynamic_index_in_dim(halves, 1 - core, axis=3, keepdims=False)
    swapped = lax.ppermute(
        theirs.astype(jnp.bfloat16), "hist", perm=[(i, i ^ 1) for i in range(n_hist)]
    )
    chip_sums = mine + swapped.astype(jnp.float32)

    def block_of(index):
        index = jnp.clip(index, 0, chips - 1)
        return lax.dynamic_index_in_dim(chip_sums, index, axis=2, keepdims=False)

    total = block_of(chip)
    for shift in range(1, chips):
        send = block_of((chip + shift) % chips).astype(jnp.bfloat16)
        perm = [(2 * c + k, 2 * ((c + shift) % chips) + k) for c in range(chips) for k in range(2)]
        total = total + lax.ppermute(send, "hist", perm=perm).astype(jnp.float32)
    return total


def gather_queries(queries, n_cand, n_hist):
    micro, rows, width = queries.shape
    group = width // n_cand
    me_cand = lax.axis_index("cand")
    chunks = queries.reshape(micro, rows, n_cand, group)
    received = []
    for shift in range(n_cand):
        target = (me_cand + shift) % n_cand
        piece = lax.dynamic_index_in_dim(chunks, target, axis=2, keepdims=False)
        if shift:
            piece = lax.ppermute(
                piece, "cand", perm=[(i, (i + shift) % n_cand) for i in range(n_cand)]
            )
        received.append(piece)
    by_offset = jnp.stack(received)
    sources = jnp.stack(
        [
            lax.dynamic_index_in_dim(by_offset, (me_cand - c) % n_cand, axis=0, keepdims=False)
            for c in range(n_cand)
        ]
    )
    chips = n_hist // 2
    me = lax.axis_index("hist")
    chip, core = me // 2, me % 2
    by_offset = [sources]
    for shift in range(1, chips):
        perm = [(2 * c + k, 2 * ((c + shift) % chips) + k) for c in range(chips) for k in range(2)]
        by_offset.append(lax.ppermute(sources, "hist", perm=perm))
    by_offset = jnp.stack(by_offset)
    mine = jnp.stack(
        [
            lax.dynamic_index_in_dim(by_offset, (chip - c) % chips, axis=0, keepdims=False)
            for c in range(chips)
        ]
    )
    theirs = lax.ppermute(mine, "hist", perm=[(i, i ^ 1) for i in range(n_hist)])
    both = jnp.where(core == 0, jnp.stack([mine, theirs], axis=1), jnp.stack([theirs, mine], axis=1))
    both = both.reshape(n_hist, n_cand, micro, rows, group)
    return jnp.transpose(both, (2, 1, 0, 3, 4)).reshape(micro, n_cand * n_hist * rows, group)


def spread_over_cand(reduced):
    micro, n_cand, rows, group = reduced.shape
    me = lax.axis_index("cand")
    received = []
    for shift in range(n_cand):
        piece = lax.dynamic_index_in_dim(reduced, (me + shift) % n_cand, axis=1, keepdims=False)
        if shift:
            piece = lax.ppermute(
                piece, "cand", perm=[(i, (i + shift) % n_cand) for i in range(n_cand)]
            )
        received.append(piece)
    by_offset = jnp.stack(received)
    return jnp.concatenate(
        [
            lax.dynamic_index_in_dim(by_offset, (me - c) % n_cand, axis=0, keepdims=False)
            for c in range(n_cand)
        ],
        axis=-1,
    )


def body(
    cand_x, qu_weight, out_weight, k_cache, v_cache, hist_len, cand_count, tile_user, tile_rank
):
    n_cand = lax.axis_size("cand")
    n_hist = lax.axis_size("hist")
    micro, local_rows, model_width = cand_x.shape
    head_cols = k_cache.shape[1]
    heads_here = head_cols // HEAD_DIM
    tiles_here = k_cache.shape[0] // TILE

    cand_rows = cand_x.reshape(micro * local_rows, model_width)
    queries = jax.nn.silu(
        jnp.dot(cand_rows, qu_weight[:, :model_width], preferred_element_type=jnp.float32)
    )
    queries = queries.astype(jnp.bfloat16).reshape(micro, local_rows, model_width)
    gate_vals = jax.nn.silu(
        jnp.dot(cand_rows, qu_weight[:, model_width:], preferred_element_type=jnp.float32)
    ).astype(jnp.bfloat16)
    queries_all = gather_queries(queries, n_cand, n_hist)
    all_cands = queries_all.shape[1]
    window = 2 * all_cands // USERS

    rows_per_block = BLOCK_TILES * TILE
    n_blocks = tiles_here // BLOCK_TILES
    whole = pl.BlockSpec((micro, all_cands, head_cols), lambda b, *_: (0, 0, 0))
    tiles = pl.BlockSpec(
        (rows_per_block, head_cols), lambda b, *_: (b, 0)
    )
    partial_value = pl.pallas_call(
        functools.partial(attend_kernel, window=window, heads_here=heads_here, micro=micro),
        grid_spec=pltpu.PrefetchScalarGridSpec(
            num_scalar_prefetch=4,
            grid=(n_blocks,),
            in_specs=[whole, tiles, tiles],
            out_specs=whole,
            scratch_shapes=[
                pltpu.VMEM((USERS * micro * window, head_cols), jnp.bfloat16),
                pltpu.VMEM((USERS * micro * window, head_cols), jnp.float32),
                pltpu.SMEM((micro * USERS * 4,), jnp.int32),
            ],
        ),
        out_shape=jax.ShapeDtypeStruct((micro, all_cands, head_cols), jnp.float32),
        compiler_params=pltpu.CompilerParams(dimension_semantics=("arbitrary",)),
    )(tile_user, tile_rank, hist_len, cand_count.reshape(-1), queries_all, k_cache, v_cache)

    reduced = reduce_over_hist(partial_value.reshape(micro, n_cand, n_hist, local_rows, head_cols))
    attended = spread_over_cand(reduced)
    attended = attended.reshape(micro * local_rows, model_width)
    average = jnp.mean(attended, axis=-1, keepdims=True)
    centered = attended - average
    spread_sq = jnp.mean(centered * centered, axis=-1, keepdims=True)
    normed = centered * lax.rsqrt(spread_sq + EPSILON)
    mixed_rows = (normed * gate_vals.astype(jnp.float32)).astype(jnp.bfloat16)
    ranked = jnp.dot(
        mixed_rows, out_weight, preferred_element_type=jnp.float32
    ) + cand_rows.astype(jnp.float32)
    return ranked.astype(jnp.bfloat16).reshape(micro, local_rows, model_width)


def solution(mesh):
    return jax.shard_map(
        body,
        mesh=mesh,
        in_specs=(
            P(None, ("cand", "hist"), None),
            P(),
            P(),
            P("hist", "cand"),
            P("hist", "cand"),
            P(),
            P(),
            P("hist"),
            P("hist"),
        ),
        out_specs=P(None, ("cand", "hist"), None),
        check_vma=False,
    )
```

```python
import functools

import jax
import jax.numpy as jnp
from jax import lax
from jax.experimental import pallas as pl
from jax.experimental.pallas import tpu as pltpu
from jax.sharding import PartitionSpec as P

HEAD_DIM = 128
TILE = 128
USERS = 16
MICRO = 2
BLOCK_TILES = 32


EPSILON = 1e-06


def silu_f32(x):
    return 0.5 * x * (1.0 + jnp.tanh(0.5 * x))


def attend_kernel(
    owner_ref, rank_ref, len_ref, count_ref,
    q_ref, k_ref, v_ref, out_ref, user_q, user_acc, user_ref, *, window, heads_here, micro,
):
    block = pl.program_id(0)
    all_cands = q_ref.shape[1]
    row_ids = lax.broadcasted_iota(jnp.int32, (window, 1), 0)
    pad = jnp.zeros((16, out_ref.shape[2]), jnp.float32)

    @pl.when(block == 0)
    def _():
        user_acc[...] = jnp.zeros_like(user_acc)
        for m in range(micro):
            def scan(user, start):
                count = count_ref[m * USERS + user]
                offset = jnp.minimum(start, all_cands - window)
                base_row = jnp.minimum(offset // 16 * 16, all_cands - window - 16)
                entry = (m * USERS + user) * 4
                user_ref[entry] = base_row
                user_ref[entry + 1] = offset - base_row
                user_ref[entry + 2] = start - offset
                user_ref[entry + 3] = start - offset + count
                return start + count

            lax.fori_loop(0, USERS, scan, jnp.int32(0))

        for m in range(micro):
            def fill(user, carry):
                entry = (m * USERS + user) * 4
                span = pl.ds(pl.multiple_of(user_ref[entry], 16), window + 16)
                shift = user_ref[entry + 1]
                rows = q_ref[m, span, :].astype(jnp.float32)
                rows = pltpu.roll(rows, (window + 16 - shift) % (window + 16), 0)
                keep = (row_ids >= user_ref[entry + 2]) & (row_ids < user_ref[entry + 3])
                user_q[pl.ds(pl.multiple_of(user * (micro * window) + m * window, window), window), :] = jnp.where(
                    keep, rows[:window], 0.0
                ).astype(jnp.bfloat16)
                return carry

            lax.fori_loop(0, USERS, fill, 0)

    key_ids = lax.broadcasted_iota(jnp.int32, (TILE, 1), 0)

    def one_tile(j):
        if True:
            slot = block * BLOCK_TILES + j
            user = owner_ref[slot]
            klen = jnp.where(
                user < USERS, len_ref[jnp.minimum(user, USERS - 1)] - rank_ref[slot] * TILE, 0
            )
            rows = slice(j * TILE, (j + 1) * TILE)
            keys = jnp.where(key_ids < klen, k_ref[rows, :], 0)
            values = v_ref[rows, :]
            first_row = jnp.minimum(user, USERS - 1) * (micro * window)
            user_rows = pl.ds(pl.multiple_of(first_row, micro * window), micro * window)
            queries = user_q[user_rows, :]
            if heads_here == 2:
                lanes = lax.broadcasted_iota(jnp.int32, (1, 2 * HEAD_DIM), 1)
                first = lanes < HEAD_DIM

                def diagonal(tile):
                    return jnp.concatenate(
                        [jnp.where(first, tile, 0), jnp.where(first, 0, tile)], axis=0
                    )

                scores = lax.dot_general(
                    queries,
                    diagonal(keys),
                    (((1,), (1,)), ((), ())),
                    preferred_element_type=jnp.float32,
                )
                weights = silu_f32(scores).astype(jnp.bfloat16)
                user_acc[user_rows, :] += jnp.dot(
                    weights, diagonal(values), preferred_element_type=jnp.float32
                )
            else:
                parts = []
                for h in range(heads_here):
                    cols = slice(h * HEAD_DIM, (h + 1) * HEAD_DIM)
                    scores = lax.dot_general(
                        queries[:, cols],
                        keys[:, cols],
                        (((1,), (1,)), ((), ())),
                        preferred_element_type=jnp.float32,
                    )
                    weights = silu_f32(scores).astype(jnp.bfloat16)
                    parts.append(
                        jnp.dot(weights, values[:, cols], preferred_element_type=jnp.float32)
                    )
                user_acc[user_rows, :] += jnp.concatenate(parts, axis=1) if heads_here > 1 else parts[0]


    occupied = owner_ref[block * BLOCK_TILES]
    for j in range(1, BLOCK_TILES):
        occupied = jnp.minimum(occupied, owner_ref[block * BLOCK_TILES + j])

    @pl.when(occupied < USERS)
    def _():
        for j in range(BLOCK_TILES):
            one_tile(j)

    @pl.when(block == pl.num_programs(0) - 1)
    def _():
        out_ref[...] = jnp.zeros_like(out_ref)
        for m in range(micro):
            def place(user, carry):
                entry = (m * USERS + user) * 4
                span = pl.ds(pl.multiple_of(user_ref[entry], 16), window + 16)
                first = pl.multiple_of(user * (micro * window) + m * window, window)
                sums = jnp.concatenate([user_acc[pl.ds(first, window), :], pad])
                out_ref[m, span, :] += pltpu.roll(sums, user_ref[entry + 1], 0)
                return carry

            lax.fori_loop(0, USERS, place, 0)


def reduce_over_hist(partial):
    micro, n_cand, n_hist, rows, cols = partial.shape
    chips = n_hist // 2
    me = lax.axis_index("hist")
    chip, core = me // 2, me % 2
    halves = partial.reshape(micro, n_cand, chips, 2, rows, cols)
    mine = lax.dynamic_index_in_dim(halves, core, axis=3, keepdims=False)
    theirs = lax.dynamic_index_in_dim(halves, 1 - core, axis=3, keepdims=False)
    swapped = lax.ppermute(
        theirs.astype(jnp.bfloat16), "hist", perm=[(i, i ^ 1) for i in range(n_hist)]
    )
    chip_sums = mine + swapped.astype(jnp.float32)

    def block_of(index):
        index = jnp.clip(index, 0, chips - 1)
        return lax.dynamic_index_in_dim(chip_sums, index, axis=2, keepdims=False)

    total = block_of(chip)
    for shift in range(1, chips):
        send = block_of((chip + shift) % chips).astype(jnp.bfloat16)
        perm = [(2 * c + k, 2 * ((c + shift) % chips) + k) for c in range(chips) for k in range(2)]
        total = total + lax.ppermute(send, "hist", perm=perm).astype(jnp.float32)
    return total


def gather_queries(queries, n_cand, n_hist):
    micro, rows, width = queries.shape
    group = width // n_cand
    me_cand = lax.axis_index("cand")
    chunks = queries.reshape(micro, rows, n_cand, group)
    received = []
    for shift in range(n_cand):
        target = (me_cand + shift) % n_cand
        piece = lax.dynamic_index_in_dim(chunks, target, axis=2, keepdims=False)
        if shift:
            piece = lax.ppermute(
                piece, "cand", perm=[(i, (i + shift) % n_cand) for i in range(n_cand)]
            )
        received.append(piece)
    by_offset = jnp.stack(received)
    sources = jnp.stack(
        [
            lax.dynamic_index_in_dim(by_offset, (me_cand - c) % n_cand, axis=0, keepdims=False)
            for c in range(n_cand)
        ]
    )
    chips = n_hist // 2
    me = lax.axis_index("hist")
    chip, core = me // 2, me % 2
    by_offset = [sources]
    for shift in range(1, chips):
        perm = [(2 * c + k, 2 * ((c + shift) % chips) + k) for c in range(chips) for k in range(2)]
        by_offset.append(lax.ppermute(sources, "hist", perm=perm))
    by_offset = jnp.stack(by_offset)
    mine = jnp.stack(
        [
            lax.dynamic_index_in_dim(by_offset, (chip - c) % chips, axis=0, keepdims=False)
            for c in range(chips)
        ]
    )
    theirs = lax.ppermute(mine, "hist", perm=[(i, i ^ 1) for i in range(n_hist)])
    both = jnp.where(core == 0, jnp.stack([mine, theirs], axis=1), jnp.stack([theirs, mine], axis=1))
    both = both.reshape(n_hist, n_cand, micro, rows, group)
    return jnp.transpose(both, (2, 1, 0, 3, 4)).reshape(micro, n_cand * n_hist * rows, group)


def spread_over_cand(reduced):
    micro, n_cand, rows, group = reduced.shape
    me = lax.axis_index("cand")
    received = []
    for shift in range(n_cand):
        piece = lax.dynamic_index_in_dim(reduced, (me + shift) % n_cand, axis=1, keepdims=False)
        if shift:
            piece = lax.ppermute(
                piece, "cand", perm=[(i, (i + shift) % n_cand) for i in range(n_cand)]
            )
        received.append(piece)
    by_offset = jnp.stack(received)
    return jnp.concatenate(
        [
            lax.dynamic_index_in_dim(by_offset, (me - c) % n_cand, axis=0, keepdims=False)
            for c in range(n_cand)
        ],
        axis=-1,
    )


def body(
    cand_x, qu_weight, out_weight, k_cache, v_cache, hist_len, cand_count, tile_user, tile_rank
):
    n_cand = lax.axis_size("cand")
    n_hist = lax.axis_size("hist")
    micro, local_rows, model_width = cand_x.shape
    head_cols = k_cache.shape[1]
    heads_here = head_cols // HEAD_DIM
    tiles_here = k_cache.shape[0] // TILE

    cand_rows = cand_x.reshape(micro * local_rows, model_width)
    projected = jax.nn.silu(jnp.dot(cand_rows, qu_weight, preferred_element_type=jnp.float32))
    queries = projected[:, :model_width].astype(jnp.bfloat16).reshape(micro, local_rows, model_width)
    gate_vals = projected[:, model_width:].astype(jnp.bfloat16)
    queries_all = gather_queries(queries, n_cand, n_hist)
    all_cands = queries_all.shape[1]
    window = 2 * all_cands // USERS

    rows_per_block = BLOCK_TILES * TILE
    n_blocks = tiles_here // BLOCK_TILES
    whole = pl.BlockSpec((micro, all_cands, head_cols), lambda b, *_: (0, 0, 0))
    tiles = pl.BlockSpec(
        (rows_per_block, head_cols), lambda b, *_: (b, 0)
    )
    partial_value = pl.pallas_call(
        functools.partial(attend_kernel, window=window, heads_here=heads_here, micro=micro),
        grid_spec=pltpu.PrefetchScalarGridSpec(
            num_scalar_prefetch=4,
            grid=(n_blocks,),
            in_specs=[whole, tiles, tiles],
            out_specs=whole,
            scratch_shapes=[
                pltpu.VMEM((USERS * micro * window, head_cols), jnp.bfloat16),
                pltpu.VMEM((USERS * micro * window, head_cols), jnp.float32),
                pltpu.SMEM((micro * USERS * 4,), jnp.int32),
            ],
        ),
        out_shape=jax.ShapeDtypeStruct((micro, all_cands, head_cols), jnp.float32),
        compiler_params=pltpu.CompilerParams(dimension_semantics=("arbitrary",)),
    )(tile_user, tile_rank, hist_len, cand_count.reshape(-1), queries_all, k_cache, v_cache)

    reduced = reduce_over_hist(partial_value.reshape(micro, n_cand, n_hist, local_rows, head_cols))
    attended = spread_over_cand(reduced)
    attended = attended.reshape(micro * local_rows, model_width)
    average = jnp.mean(attended, axis=-1, keepdims=True)
    centered = attended - average
    spread_sq = jnp.mean(centered * centered, axis=-1, keepdims=True)
    normed = centered * lax.rsqrt(spread_sq + EPSILON)
    mixed_rows = (normed * gate_vals.astype(jnp.float32)).astype(jnp.bfloat16)
    ranked = jnp.dot(
        mixed_rows, out_weight, preferred_element_type=jnp.float32
    ) + cand_rows.astype(jnp.float32)
    return ranked.astype(jnp.bfloat16).reshape(micro, local_rows, model_width)


def solution(mesh):
    return jax.shard_map(
        body,
        mesh=mesh,
        in_specs=(
            P(None, ("cand", "hist"), None),
            P(),
            P(),
            P("hist", "cand"),
            P("hist", "cand"),
            P(),
            P(),
            P("hist"),
            P("hist"),
        ),
        out_specs=P(None, ("cand", "hist"), None),
        check_vma=False,
    )
```
